256 devices in a mesh: blk: 64 (over x, y, z_hi, core), mode: 4 (over z_lo).
Axes of the slice: x: 4, y: 4, z: 8 (z_hi: 2, z_lo: 4; z = z_hi * 4 + z_lo), core: 2. Of those that a mesh axis runs over, the one named last changes fastest.
Arguments:
- direct: float32 [16, 2, 5, 128, 8, 512], P('mode', None, None, 'blk'), may hold values from -6 to 6
- adjoint: float32 [16, 2, 5, 128, 8, 512], P('mode', None, None, 'blk'), may hold values from -6 to 6
- density: float32 [128, 8, 512], P('blk'), may hold values from 0.7 to 1.4
- velocity: float32 [2, 128, 8, 512], P(None, 'blk'), may hold values from -0.8 to 0.8
- pressure: float32 [128, 8, 512], P('blk'), may hold values from 0.5 to 1
- block_home: int32 [128], replicated, may hold values from 0 to 127, as said below
- face_nbr: int32 [128, 4], P('blk'), may hold values from -1 to 127, as said below
- face_flip: int32 [128, 4], P('blk'), may hold values from 0 to 1, as said below
Outputs:
- direct_out: float32 [16, 2, 5, 128, 8, 512], P('mode', None, None, 'blk')
- adjoint_out: float32 [16, 2, 5, 128, 8, 512], P('mode', None, None, 'blk')
- sensitivity: float32 [128, 8, 512], P('blk')
The draws below stay inside these ranges and needn't reach their ends.
Inputs may be any that keep to these rules, and one draw needn't show every extreme that they name: Block g lies on blk device g // 2; block_home is a permutation of positions that keeps each block on its device. `face_nbr`: the low-i neighbour of a block on device d lies on device d - 1 and the high-i one on device d + 1 (cyclically along blk), the high-i face of one meeting the low-i face of the other; j neighbours lie on the same device or are walls (-1); connections are mutual. `face_flip`: both sides of a connection carry the same flag; j faces carry 0.
All inputs are finite; a program needn't handle non-finite values.
Results may differ from the reference program's by a relative error of at most 0.0001.
Values sent between devices are 32-bit elements; how exact they have to be, the bound alone decides.
No kernel may reach another device: no remote copies, remote signals or barrier semaphores. Data moves between devices by JAX's collectives and lax.ppermute only.
A program may use at most 64 MiB of HBM per device.

```python
import math
import jax
import jax.numpy as jnp
from jax import lax

MODES = 16
BPD = 2
BI = 8
BJ = 512
STEPS = 2
NBLK = 128


def layout_tables(key):
    columns = NBLK // BPD
    keys = jax.random.split(jax.random.fold_in(key, 11), 3)
    slot_perm = jax.vmap(lambda single: jax.random.permutation(single, BPD))(jax.random.split(keys[0], columns)).astype(jnp.int32)
    matching = jax.vmap(lambda single: jax.random.permutation(single, BPD))(jax.random.split(keys[1], columns)).astype(jnp.int32)
    flag_draw = jax.random.randint(keys[2], (columns, BPD), 0, 2).astype(jnp.int32)
    column_id = jnp.arange(columns, dtype=jnp.int32)[:, None]
    row_id = jnp.arange(BPD, dtype=jnp.int32)[None, :]
    home = (column_id * BPD + slot_perm).reshape(-1)
    inverse = jnp.argsort(matching, axis=1).astype(jnp.int32)
    previous = (jnp.arange(columns, dtype=jnp.int32) - 1) % columns
    prev_inverse = inverse[previous]
    west = (column_id - 1) % columns * BPD + prev_inverse
    east = (column_id + 1) % columns * BPD + matching
    south = jnp.where(row_id > 0, column_id * BPD + row_id - 1, -1)
    north = jnp.where(row_id < BPD - 1, column_id * BPD + row_id + 1, -1)
    flip_west = jnp.take_along_axis(flag_draw[previous], prev_inverse, axis=1)
    flip_east = flag_draw
    zeros = jnp.zeros_like(flag_draw)
    neighbours = jnp.stack([west, east, south, north], axis=-1).reshape(NBLK, 4).astype(jnp.int32)
    flags = jnp.stack([flip_west, flip_east, zeros, zeros], axis=-1).reshape(NBLK, 4).astype(jnp.int32)
    by_position = jnp.zeros((NBLK, 4), jnp.int32).at[home].set(neighbours)
    flags_position = jnp.zeros((NBLK, 4), jnp.int32).at[home].set(flags)
    return (home.astype(jnp.int32), by_position, flags_position)


def draw_block_home(key, part):
    return layout_tables(key)[0]


def draw_face_nbr(key, part):
    return layout_tables(key)[1]


def draw_face_flip(key, part):
    return layout_tables(key)[2]


def block_scale(stream_key, dims, cuts, smallest, high):
    def one(dim, parts):
        steps = jax.random.uniform(jax.random.fold_in(jax.random.fold_in(stream_key, 6), dim), (parts,), jnp.float32, smallest / len(cuts), high / len(cuts))
        return jnp.repeat(jnp.exp(steps), dims[dim] // parts).reshape((-1,) + (1,) * (len(dims) - dim - 1))

    gain = one(*cuts[0])
    for cut in cuts[1:]:
        gain = gain * one(*cut)
    return gain


def normal_values(own_key, extent, width, limit, cuts=(), kind=jnp.bfloat16):
    values = jax.random.normal(own_key, extent, jnp.float32) * width
    if len(cuts) > 0:
        values = block_scale(own_key, extent, cuts, -0.22, 0.18) * values
    return jnp.clip(values, min=-limit, max=limit).astype(kind)


def setup_inputs(seed: int = 0) -> dict:
    streams_of = jax.random.split(jax.random.key(seed), 9)
    return {
        "direct": normal_values(streams_of[0], (MODES, 2, 5, NBLK, BI, BJ), 1.0, 6.0, ((0, 4), (3, 64)), jnp.float32),
        "adjoint": normal_values(streams_of[1], (MODES, 2, 5, NBLK, BI, BJ), 1.0, 6.0, ((0, 4), (3, 64)), jnp.float32),
        "density": jnp.clip(jnp.exp(math.log(1.4) - 0.6931472 * jax.random.uniform(streams_of[2], (NBLK, BI, BJ), jnp.float32) ** block_scale(streams_of[2], (NBLK, BI, BJ), ((0, 64),), -0.2, 0.2)), 0.7, 1.4),
        "velocity": jnp.clip(jax.random.uniform(streams_of[3], (2, NBLK, BI, BJ), jnp.float32, -0.8, 0.8) * block_scale(streams_of[3], (2, NBLK, BI, BJ), ((1, 64),), -0.4, 0.0), -0.8, 0.8),
        "pressure": jnp.clip(jnp.exp(math.log(1.0) - 0.6931472 * jax.random.uniform(streams_of[4], (NBLK, BI, BJ), jnp.float32) ** block_scale(streams_of[4], (NBLK, BI, BJ), ((0, 64),), -0.2, 0.2)), 0.5, 1.0),
        "block_home": draw_block_home(jax.random.fold_in(streams_of[8], 71), 0),
        "face_nbr": draw_face_nbr(jax.random.fold_in(streams_of[8], 71), 0),
        "face_flip": draw_face_flip(jax.random.fold_in(streams_of[8], 71), 0),
    }


HEAT_RATIO = 1.4
VISCOSITY = 0.25
TIME_STEP = 0.05
SPAN_WAVE = 0.5
BASE_FREQ = 0.2


def component(values, number):
    return values[..., number, :, :, :]


def stream_jac(base_flow, values):
    density, stream_speed, cross_speed, pressure = base_flow
    f0, f1, f2, f3, f4 = [component(values, n) for n in range(5)]
    return jnp.stack([stream_speed * f0 + density * f1, stream_speed * f1 + f4 / density, stream_speed * f2, stream_speed * f3, HEAT_RATIO * pressure * f1 + stream_speed * f4], axis=-4)


def cross_jac(base_flow, values):
    density, stream_speed, cross_speed, pressure = base_flow
    f0, f1, f2, f3, f4 = [component(values, n) for n in range(5)]
    return jnp.stack([cross_speed * f0 + density * f2, cross_speed * f1, cross_speed * f2 + f4 / density, cross_speed * f3, HEAT_RATIO * pressure * f2 + cross_speed * f4], axis=-4)


def span_jac(base_flow, values):
    density, stream_speed, cross_speed, pressure = base_flow
    f0, f1, f2, f3, f4 = [component(values, n) for n in range(5)]
    zeros = jnp.zeros_like(f0)
    return jnp.stack([density * f3, zeros, zeros, f4 / density, HEAT_RATIO * pressure * f3], axis=-4)


def stream_adj(base_flow, values):
    density, stream_speed, cross_speed, pressure = base_flow
    f0, f1, f2, f3, f4 = [component(values, n) for n in range(5)]
    return jnp.stack([stream_speed * f0, density * f0 + stream_speed * f1 + HEAT_RATIO * pressure * f4, stream_speed * f2, stream_speed * f3, f1 / density + stream_speed * f4], axis=-4)


def cross_adj(base_flow, values):
    density, stream_speed, cross_speed, pressure = base_flow
    f0, f1, f2, f3, f4 = [component(values, n) for n in range(5)]
    return jnp.stack([cross_speed * f0, cross_speed * f1, density * f0 + cross_speed * f2 + HEAT_RATIO * pressure * f4, cross_speed * f3, f2 / density + cross_speed * f4], axis=-4)


def span_adj(base_flow, values):
    density, stream_speed, cross_speed, pressure = base_flow
    f0, f1, f2, f3, f4 = [component(values, n) for n in range(5)]
    zeros = jnp.zeros_like(f0)
    return jnp.stack([zeros, zeros, zeros, density * f0 + HEAT_RATIO * pressure * f4, f3 / density], axis=-4)


def extend(values, ghost_west, ghost_east, ghost_south, ghost_north):
    middle = jnp.concatenate([ghost_south[..., None], values, ghost_north[..., None]], axis=-1)
    corner = jnp.zeros_like(ghost_west[..., :1])
    top_row = jnp.concatenate([corner, ghost_west, corner], axis=-1)[..., None, :]
    bottom_row = jnp.concatenate([corner, ghost_east, corner], axis=-1)[..., None, :]
    return jnp.concatenate([top_row, middle, bottom_row], axis=-2)


def stencils(padded):
    deriv_stream = (padded[..., 2:, 1:-1] - padded[..., :-2, 1:-1]) / 2.0
    deriv_cross = (padded[..., 1:-1, 2:] - padded[..., 1:-1, :-2]) / 2.0
    centre = padded[..., 1:-1, 1:-1]
    laplace = padded[..., 2:, 1:-1] + padded[..., :-2, 1:-1] + padded[..., 1:-1, 2:] + padded[..., 1:-1, :-2] - 4.0 * centre
    return deriv_stream, deriv_cross, laplace


def direct_rate(base_flow, padded, values, frequency):
    real_part = values[..., 0, :, :, :, :]
    imag_part = values[..., 1, :, :, :, :]
    ds_re, dc_re, lap_re = stencils(padded[..., 0, :, :, :, :])
    ds_im, dc_im, lap_im = stencils(padded[..., 1, :, :, :, :])
    damping = SPAN_WAVE * SPAN_WAVE
    rate_re = -(stream_jac(base_flow, ds_re) + cross_jac(base_flow, dc_re)) + VISCOSITY * (lap_re - damping * real_part) + SPAN_WAVE * span_jac(base_flow, imag_part) + frequency * imag_part
    rate_im = -(stream_jac(base_flow, ds_im) + cross_jac(base_flow, dc_im)) + VISCOSITY * (lap_im - damping * imag_part) - SPAN_WAVE * span_jac(base_flow, real_part) - frequency * real_part
    return jnp.stack([rate_re, rate_im], axis=-5)


def adjoint_rate(base_flow, padded, values, frequency):
    real_part = values[..., 0, :, :, :, :]
    imag_part = values[..., 1, :, :, :, :]
    ds_re, dc_re, lap_re = stencils(padded[..., 0, :, :, :, :])
    ds_im, dc_im, lap_im = stencils(padded[..., 1, :, :, :, :])
    damping = SPAN_WAVE * SPAN_WAVE
    rate_re = stream_adj(base_flow, ds_re) + cross_adj(base_flow, dc_re) + VISCOSITY * (lap_re - damping * real_part) - SPAN_WAVE * span_adj(base_flow, imag_part) - frequency * imag_part
    rate_im = stream_adj(base_flow, ds_im) + cross_adj(base_flow, dc_im) + VISCOSITY * (lap_im - damping * imag_part) + SPAN_WAVE * span_adj(base_flow, real_part) + frequency * real_part
    return jnp.stack([rate_re, rate_im], axis=-5)


def orient(face_rows, flags):
    return jnp.where(flags[:, None] == 1, face_rows[..., ::-1], face_rows)


def neighbour_pad(values, positions, face_flip, live_face):
    ghost_west = orient(jnp.take(values[..., -1, :], positions[:, 0], axis=2), face_flip[:, 0])
    ghost_east = orient(jnp.take(values[..., 0, :], positions[:, 1], axis=2), face_flip[:, 1])
    ghost_south = jnp.where(live_face[:, 2][:, None], jnp.take(values[..., :, -1], positions[:, 2], axis=2), 0.0)
    ghost_north = jnp.where(live_face[:, 3][:, None], jnp.take(values[..., :, 0], positions[:, 3], axis=2), 0.0)
    return extend(values, ghost_west, ghost_east, ghost_south, ghost_north)


def reference(direct, adjoint, density, velocity, pressure, block_home, face_nbr, face_flip):
    base_flow = (density, velocity[0], velocity[1], pressure)
    live_face = face_nbr >= 0
    positions = jnp.take(block_home, jnp.maximum(face_nbr, 0).astype(jnp.int32)).astype(jnp.int32)

    def one_mode(item):
        primal, dual, mode_index = item
        frequency = BASE_FREQ * (mode_index.astype(jnp.float32) - MODES / 2 + 0.5)
        summed = jnp.zeros(primal.shape[2:], jnp.float32)
        for advance in range(STEPS):
            padded_q = neighbour_pad(primal, positions, face_flip, live_face)
            padded_a = neighbour_pad(dual, positions, face_flip, live_face)
            primal_next = primal + TIME_STEP * direct_rate(base_flow, padded_q, primal, frequency)
            dual = dual + TIME_STEP * adjoint_rate(base_flow, padded_a, dual, frequency)
            primal = primal_next
            summed = summed + jnp.mean(primal * primal, axis=(0, 1)) * jnp.mean(dual * dual, axis=(0, 1))
        return primal, dual, summed

    direct_out, adjoint_out, contribs = lax.map(one_mode, (direct, adjoint, jnp.arange(MODES, dtype=jnp.int32)))
    sensitivity = jnp.sum(contribs, axis=0) / (STEPS * MODES)
    return direct_out, adjoint_out, sensitivity
```

```python
import functools

import jax
import jax.numpy as jnp
from jax import lax
from jax.experimental import pallas as pl
from jax.experimental.pallas import tpu as pltpu
from jax.sharding import PartitionSpec as P

STEPS = 2

HEAT_RATIO = 1.4
VISCOSITY = 0.25
TIME_STEP = 0.05
SPAN_WAVE = 0.5
BASE_FREQ = 0.2

NV = 5
ENTRIES = 8


def shifted(block, axis, distance):
    n = lax.axis_size(axis)
    route = [((i - distance) % n, i) for i in range(n)]
    return lax.ppermute(block, axis, route)


def direct_rates(bf, X, Y, dsX, dcX, lapX, dsY, dcY, lapY, w):
    r, ir, u, v, kp = bf
    b = SPAN_WAVE
    damp = SPAN_WAVE * SPAN_WAVE

    def conv(ds, dc):
        return [
            u * ds[0] + r * ds[1] + (v * dc[0] + r * dc[2]),
            u * ds[1] + ds[4] * ir + v * dc[1],
            u * ds[2] + (v * dc[2] + dc[4] * ir),
            u * ds[3] + v * dc[3],
            kp * ds[1] + u * ds[4] + (kp * dc[2] + v * dc[4]),
        ]

    def span(f):
        return [r * f[3], None, None, f[4] * ir, kp * f[3]]

    cX = conv(dsX, dcX)
    cY = conv(dsY, dcY)
    sX = span(X)
    sY = span(Y)
    re, im = [], []
    for n in range(NV):
        a = -cX[n] + VISCOSITY * (lapX[n] - damp * X[n])
        if sY[n] is not None:
            a = a + b * sY[n]
        a = a + w * Y[n]
        c = -cY[n] + VISCOSITY * (lapY[n] - damp * Y[n])
        if sX[n] is not None:
            c = c - b * sX[n]
        c = c - w * X[n]
        re.append(a)
        im.append(c)
    return re, im


def adjoint_rates(bf, X, Y, dsX, dcX, lapX, dsY, dcY, lapY, w):
    r, ir, u, v, kp = bf
    b = SPAN_WAVE
    damp = SPAN_WAVE * SPAN_WAVE

    def conv(ds, dc):
        return [
            u * ds[0] + v * dc[0],
            r * ds[0] + u * ds[1] + kp * ds[4] + v * dc[1],
            u * ds[2] + (r * dc[0] + v * dc[2] + kp * dc[4]),
            u * ds[3] + v * dc[3],
            ds[1] * ir + u * ds[4] + (dc[2] * ir + v * dc[4]),
        ]

    def span(f):
        return [None, None, None, r * f[0] + kp * f[4], f[3] * ir]

    cX = conv(dsX, dcX)
    cY = conv(dsY, dcY)
    sX = span(X)
    sY = span(Y)
    re, im = [], []
    for n in range(NV):
        a = cX[n] + VISCOSITY * (lapX[n] - damp * X[n])
        if sY[n] is not None:
            a = a - b * sY[n]
        a = a - w * Y[n]
        c = cY[n] + VISCOSITY * (lapY[n] - damp * Y[n])
        if sX[n] is not None:
            c = c + b * sX[n]
        c = c + w * X[n]
        re.append(a)
        im.append(c)
    return re, im


def step_kernel(tbl, x_ref, a_ref, rlo_ref, rhi_ref, rho_ref, vel_ref, prs_ref, *rest, modes_total, first):
    if first:
        xo_ref, ao_ref, sens_ref, elo_ref, ehi_ref, rev_ref = rest
    else:
        sin_ref, xo_ref, ao_ref, sens_ref, rev_ref = rest
    m = pl.program_id(0)
    slots = x_ref.shape[3]
    height = x_ref.shape[4]
    width = x_ref.shape[5]
    shape = (height, width)

    @pl.when(m == 0)
    def _init():
        ri = lax.broadcasted_iota(jnp.int32, (width, width), 0)
        ci = lax.broadcasted_iota(jnp.int32, (width, width), 1)
        rev_ref[...] = jnp.where(ri + ci == width - 1, 1.0, 0.0).astype(jnp.float32)
        if first:
            sens_ref[...] = jnp.zeros(sens_ref.shape, jnp.float32)
        else:
            sens_ref[...] = sin_ref[...]

    kf = (tbl[slots * ENTRIES] + m).astype(jnp.float32)
    w = BASE_FREQ * (jnp.zeros(shape, jnp.float32) + (kf - modes_total / 2 + 0.5))
    row = lax.broadcasted_iota(jnp.int32, shape, 0)
    col = lax.broadcasted_iota(jnp.int32, shape, 1)
    zero_i = jnp.zeros(shape, jnp.int32)
    rev = rev_ref[...]

    def flip_rows(rows, flag):
        turned = jnp.dot(rows, rev, precision=lax.Precision.HIGHEST, preferred_element_type=jnp.float32)
        mask = (jnp.zeros(rows.shape, jnp.int32) + flag) != 0
        return jnp.where(mask, turned, rows)

    for s in range(slots):
        base = s * ENTRIES
        lo_t, lo_f = tbl[base + 0], tbl[base + 1]
        hi_t, hi_f = tbl[base + 2], tbl[base + 3]
        jl_s, jl_live = tbl[base + 4], tbl[base + 5]
        jh_s, jh_live = tbl[base + 6], tbl[base + 7]
        jl_mask = (zero_i + jl_live) != 0
        jh_mask = (zero_i + jh_live) != 0
        r = rho_ref[s]
        ir = 1.0 / r
        u = vel_ref[0, s]
        v = vel_ref[1, s]
        kp = HEAT_RATIO * prs_ref[s]
        bf = (r, ir, u, v, kp)
        news = []
        for arr, (src, dst, rates) in enumerate(((x_ref, xo_ref, direct_rates), (a_ref, ao_ref, adjoint_rates))):
            lo_rows = flip_rows(rlo_ref[arr, 0, lo_t], lo_f)
            hi_rows = flip_rows(rhi_ref[arr, 0, hi_t], hi_f)
            vals, dss, dcs, laps = [], [], [], []
            for p in range(2):
                for n in range(NV):
                    k = p * NV + n
                    g = src[0, p, n, s]
                    lo_b = jnp.broadcast_to(lo_rows[k:k + 1, :], shape)
                    hi_b = jnp.broadcast_to(hi_rows[k:k + 1, :], shape)
                    im1 = jnp.where(row == 0, lo_b, pltpu.roll(g, 1, 0))
                    ip1 = jnp.where(row == height - 1, hi_b, pltpu.roll(g, height - 1, 0))
                    nl = pltpu.roll(src[0, p, n, jl_s], 1, 1)
                    nh = pltpu.roll(src[0, p, n, jh_s], width - 1, 1)
                    jm1 = jnp.where(col == 0, jnp.where(jl_mask, nl, 0.0), pltpu.roll(g, 1, 1))
                    jp1 = jnp.where(col == width - 1, jnp.where(jh_mask, nh, 0.0), pltpu.roll(g, width - 1, 1))
                    vals.append(g)
                    dss.append((ip1 - im1) * 0.5)
                    dcs.append((jp1 - jm1) * 0.5)
                    laps.append(ip1 + im1 + jp1 + jm1 - 4.0 * g)
            X, Y = vals[:NV], vals[NV:]
            re, im = rates(bf, X, Y, dss[:NV], dcs[:NV], laps[:NV], dss[NV:], dcs[NV:], laps[NV:], w)
            total = None
            for p, rate in enumerate((re, im)):
                for n in range(NV):
                    k = p * NV + n
                    nv = vals[k] + TIME_STEP * rate[n]
                    dst[0, p, n, s] = nv
                    if first:
                        elo_ref[arr, 0, s, pl.ds(k, 1), :] = nv[0:1, :]
                        ehi_ref[arr, 0, s, pl.ds(k, 1), :] = nv[height - 1:height, :]
                    sq = nv * nv
                    total = sq if total is None else total + sq
            news.append(total / 10.0)
        sens_ref[s] = sens_ref[s] + news[0] * news[1]


def run_step(tbl, x, a, rlo, rhi, density, velocity, pressure, sens_in, modes_total, first):
    modes, parts, nv, slots, height, width = x.shape
    state_block = (1, parts, nv, slots, height, width)
    edge_block = (2, 1, slots, parts * nv, width)
    state_spec = pl.BlockSpec(state_block, lambda m, t: (m, 0, 0, 0, 0, 0))
    edge_spec = pl.BlockSpec(edge_block, lambda m, t: (0, m, 0, 0, 0))
    flow_spec = pl.BlockSpec((slots, height, width), lambda m, t: (0, 0, 0))
    vel_spec = pl.BlockSpec((2, slots, height, width), lambda m, t: (0, 0, 0, 0))
    in_specs = [state_spec, state_spec, edge_spec, edge_spec, flow_spec, vel_spec, flow_spec]
    args = [x, a, rlo, rhi, density, velocity, pressure]
    if not first:
        in_specs.append(flow_spec)
        args.append(sens_in)
    out_shape = [
        jax.ShapeDtypeStruct(x.shape, jnp.float32),
        jax.ShapeDtypeStruct(a.shape, jnp.float32),
        jax.ShapeDtypeStruct((slots, height, width), jnp.float32),
    ]
    out_specs = [state_spec, state_spec, flow_spec]
    if first:
        edge_shape = jax.ShapeDtypeStruct((2, modes, slots, parts * nv, width), jnp.float32)
        out_shape += [edge_shape, edge_shape]
        out_specs += [edge_spec, edge_spec]
    grid_spec = pltpu.PrefetchScalarGridSpec(
        num_scalar_prefetch=1,
        grid=(modes,),
        in_specs=in_specs,
        out_specs=out_specs,
        scratch_shapes=[pltpu.VMEM((width, width), jnp.float32)],
    )
    kernel = functools.partial(step_kernel, modes_total=modes_total, first=first)
    return pl.pallas_call(
        kernel,
        grid_spec=grid_spec,
        out_shape=out_shape,
        compiler_params=pltpu.CompilerParams(dimension_semantics=("arbitrary",)),
    )(tbl, *args)


def edges(x, row):
    modes, parts, nv, slots, height, width = x.shape
    e = x[:, :, :, :, row, :]
    return jnp.transpose(e, (0, 3, 1, 2, 4)).reshape(modes, slots, parts * nv, width)


def per_device(direct, adjoint, density, velocity, pressure, block_home, face_nbr, face_flip):
    modes, parts, nv, slots, height, width = direct.shape
    modes_total = modes * lax.axis_size("mode")
    live = (face_nbr >= 0).astype(jnp.int32)
    positions = jnp.take(block_home, jnp.maximum(face_nbr, 0), axis=0)
    slot_of = positions % slots
    table = jnp.stack(
        [
            slot_of[:, 0], face_flip[:, 0], slot_of[:, 1], face_flip[:, 1],
            slot_of[:, 2], live[:, 2], slot_of[:, 3], live[:, 3],
        ],
        axis=1,
    ).reshape(-1)
    mode_base = (lax.axis_index("mode") * modes).astype(jnp.int32)
    table = jnp.concatenate([table.astype(jnp.int32), mode_base[None]])

    with jax.named_scope("edge_exchange_0"):
        up = jnp.stack([edges(direct, height - 1), edges(adjoint, height - 1)])
        down = jnp.stack([edges(direct, 0), edges(adjoint, 0)])
        rlo = shifted(up, "blk", 1)
        rhi = shifted(down, "blk", -1)
    with jax.named_scope("flow_step_0"):
        q1, a1, sens, elo, ehi = run_step(
            table, direct, adjoint, rlo, rhi, density, velocity, pressure, None, modes_total, True
        )
    with jax.named_scope("edge_exchange_1"):
        rlo = shifted(ehi, "blk", 1)
        rhi = shifted(elo, "blk", -1)
    with jax.named_scope("flow_step_1"):
        q2, a2, sens = run_step(
            table, q1, a1, rlo, rhi, density, velocity, pressure, sens, modes_total, False
        )
    with jax.named_scope("mode_reduce"):
        count = lax.axis_size("mode")
        me = lax.axis_index("mode")
        stacked = jnp.stack([sens] + [shifted(sens, "mode", k) for k in range(1, count)])
        total = None
        for j in range(count):
            part = lax.dynamic_index_in_dim(stacked, (me - j) % count, axis=0, keepdims=False)
            total = part if total is None else total + part
        sensitivity = total / (STEPS * modes_total)
    return (q2, a2, sensitivity)


def solution(mesh):
    placed = (
        P("mode", None, None, "blk", None, None),
        P("mode", None, None, "blk", None, None),
        P("blk", None, None),
        P(None, "blk", None, None),
        P("blk", None, None),
        P(),
        P("blk", None),
        P("blk", None),
    )
    return jax.shard_map(
        per_device,
        mesh=mesh,
        in_specs=placed,
        out_specs=(
            P("mode", None, None, "blk", None, None),
            P("mode", None, None, "blk", None, None),
            P("blk", None, None),
        ),
        check_vma=False,
    )
```

```python
import functools

import jax
import jax.numpy as jnp
from jax import lax
from jax.experimental import pallas as pl
from jax.experimental.pallas import tpu as pltpu
from jax.sharding import PartitionSpec as P

STEPS = 2

HEAT_RATIO = 1.4
VISCOSITY = 0.25
TIME_STEP = 0.05
SPAN_WAVE = 0.5
BASE_FREQ = 0.2

NV = 5
ENTRIES = 8


def shifted(block, axis, distance):
    n = lax.axis_size(axis)
    route = [((i - distance) % n, i) for i in range(n)]
    return lax.ppermute(block, axis, route)


def direct_rates(bf, X, Y, dsX, dcX, lapX, dsY, dcY, lapY, w):
    r, ir, u, v, kp = bf
    b = SPAN_WAVE
    damp = SPAN_WAVE * SPAN_WAVE

    def conv(ds, dc):
        return [
            u * ds[0] + r * ds[1] + (v * dc[0] + r * dc[2]),
            u * ds[1] + ds[4] * ir + v * dc[1],
            u * ds[2] + (v * dc[2] + dc[4] * ir),
            u * ds[3] + v * dc[3],
            kp * ds[1] + u * ds[4] + (kp * dc[2] + v * dc[4]),
        ]

    def span(f):
        return [r * f[3], None, None, f[4] * ir, kp * f[3]]

    cX = conv(dsX, dcX)
    cY = conv(dsY, dcY)
    sX = span(X)
    sY = span(Y)
    re, im = [], []
    for n in range(NV):
        a = -cX[n] + VISCOSITY * (lapX[n] - damp * X[n])
        if sY[n] is not None:
            a = a + b * sY[n]
        a = a + w * Y[n]
        c = -cY[n] + VISCOSITY * (lapY[n] - damp * Y[n])
        if sX[n] is not None:
            c = c - b * sX[n]
        c = c - w * X[n]
        re.append(a)
        im.append(c)
    return re, im


def adjoint_rates(bf, X, Y, dsX, dcX, lapX, dsY, dcY, lapY, w):
    r, ir, u, v, kp = bf
    b = SPAN_WAVE
    damp = SPAN_WAVE * SPAN_WAVE

    def conv(ds, dc):
        return [
            u * ds[0] + v * dc[0],
            r * ds[0] + u * ds[1] + kp * ds[4] + v * dc[1],
            u * ds[2] + (r * dc[0] + v * dc[2] + kp * dc[4]),
            u * ds[3] + v * dc[3],
            ds[1] * ir + u * ds[4] + (dc[2] * ir + v * dc[4]),
        ]

    def span(f):
        return [None, None, None, r * f[0] + kp * f[4], f[3] * ir]

    cX = conv(dsX, dcX)
    cY = conv(dsY, dcY)
    sX = span(X)
    sY = span(Y)
    re, im = [], []
    for n in range(NV):
        a = cX[n] + VISCOSITY * (lapX[n] - damp * X[n])
        if sY[n] is not None:
            a = a - b * sY[n]
        a = a - w * Y[n]
        c = cY[n] + VISCOSITY * (lapY[n] - damp * Y[n])
        if sX[n] is not None:
            c = c + b * sX[n]
        c = c + w * X[n]
        re.append(a)
        im.append(c)
    return re, im


LANES = 128


def lane_reverse_into(dst, rows):
    height = rows.shape[0]
    chunks = rows.shape[1] // LANES
    lane = lax.broadcasted_iota(jnp.int32, (height, LANES), 1)
    for b in range(chunks):
        y = rows[:, b * LANES:(b + 1) * LANES]
        k = 1
        while k < LANES:
            y = jnp.where((lane & k) != 0, pltpu.roll(y, k, 1), pltpu.roll(y, LANES - k, 1))
            k *= 2
        c = chunks - 1 - b
        dst[:, c * LANES:(c + 1) * LANES] = y


def step_kernel(tbl, x_ref, a_ref, rlo_ref, rhi_ref, rho_ref, vel_ref, prs_ref, *rest, modes_total, first):
    if first:
        xo_ref, ao_ref, sens_ref, elo_ref, ehi_ref, gh_ref = rest
    else:
        sin_ref, xo_ref, ao_ref, sens_ref, gh_ref = rest
    m = pl.program_id(0)
    slots = x_ref.shape[3]
    height = x_ref.shape[4]
    width = x_ref.shape[5]
    chunks = width // LANES
    shape = (height, LANES)

    @pl.when(m == 0)
    def _init():
        if first:
            sens_ref[...] = jnp.zeros(sens_ref.shape, jnp.float32)
        else:
            sens_ref[...] = sin_ref[...]

    for s in range(slots):
        for side, (recv, tcol, fcol) in enumerate(((rlo_ref, 0, 1), (rhi_ref, 2, 3))):
            t = tbl[s * ENTRIES + tcol]
            f = tbl[s * ENTRIES + fcol]
            for arr in range(2):
                gh_ref[arr, side, s] = recv[arr, 0, t]

                @pl.when(f != 0)
                def _turn():
                    lane_reverse_into(gh_ref.at[arr, side, s], recv[arr, 0, t])

    kf = (tbl[slots * ENTRIES] + m).astype(jnp.float32)
    w = BASE_FREQ * (jnp.zeros(shape, jnp.float32) + (kf - modes_total / 2 + 0.5))
    row = lax.broadcasted_iota(jnp.int32, shape, 0)
    lane = lax.broadcasted_iota(jnp.int32, shape, 1)
    zero_i = jnp.zeros(shape, jnp.int32)
    first_row = row == 0
    last_row = row == height - 1
    first_lane = lane == 0
    last_lane = lane == LANES - 1

    for s in range(slots):
        base = s * ENTRIES
        jl_s, jl_live = tbl[base + 4], tbl[base + 5]
        jh_s, jh_live = tbl[base + 6], tbl[base + 7]
        jl_mask = (zero_i + jl_live) != 0
        jh_mask = (zero_i + jh_live) != 0
        for b in range(chunks):
            cs = slice(b * LANES, (b + 1) * LANES)
            r = rho_ref[s, :, cs]
            ir = 1.0 / r
            u = vel_ref[0, s, :, cs]
            v = vel_ref[1, s, :, cs]
            kp = HEAT_RATIO * prs_ref[s, :, cs]
            bf = (r, ir, u, v, kp)
            means = []
            for arr, (src, dst, rates) in enumerate(((x_ref, xo_ref, direct_rates), (a_ref, ao_ref, adjoint_rates))):
                vals, dss, dcs, laps = [], [], [], []
                for p in range(2):
                    for n in range(NV):
                        k = p * NV + n
                        g = src[0, p, n, s, :, cs]
                        lo_b = jnp.broadcast_to(gh_ref[arr, 0, s, k:k + 1, cs], shape)
                        hi_b = jnp.broadcast_to(gh_ref[arr, 1, s, k:k + 1, cs], shape)
                        im1 = jnp.where(first_row, lo_b, pltpu.roll(g, 1, 0))
                        ip1 = jnp.where(last_row, hi_b, pltpu.roll(g, height - 1, 0))
                        if b > 0:
                            left = src[0, p, n, s, :, (b - 1) * LANES:b * LANES]
                        else:
                            left = jnp.where(jl_mask, src[0, p, n, jl_s, :, width - LANES:width], 0.0)
                        if b < chunks - 1:
                            right = src[0, p, n, s, :, (b + 1) * LANES:(b + 2) * LANES]
                        else:
                            right = jnp.where(jh_mask, src[0, p, n, jh_s, :, 0:LANES], 0.0)
                        jm1 = jnp.where(first_lane, pltpu.roll(left, 1, 1), pltpu.roll(g, 1, 1))
                        jp1 = jnp.where(last_lane, pltpu.roll(right, LANES - 1, 1), pltpu.roll(g, LANES - 1, 1))
                        vals.append(g)
                        dss.append((ip1 - im1) * 0.5)
                        dcs.append((jp1 - jm1) * 0.5)
                        laps.append(ip1 + im1 + jp1 + jm1 - 4.0 * g)
                X, Y = vals[:NV], vals[NV:]
                re, im = rates(bf, X, Y, dss[:NV], dcs[:NV], laps[:NV], dss[NV:], dcs[NV:], laps[NV:], w)
                total = None
                for p, rate in enumerate((re, im)):
                    for n in range(NV):
                        k = p * NV + n
                        nv = vals[k] + TIME_STEP * rate[n]
                        dst[0, p, n, s, :, cs] = nv
                        if first:
                            elo_ref[arr, 0, s, pl.ds(k, 1), cs] = nv[0:1, :]
                            ehi_ref[arr, 0, s, pl.ds(k, 1), cs] = nv[height - 1:height, :]
                        sq = nv * nv
                        total = sq if total is None else total + sq
                means.append(total / 10.0)
            sens_ref[s, :, cs] = sens_ref[s, :, cs] + means[0] * means[1]


def run_step(tbl, x, a, rlo, rhi, density, velocity, pressure, sens_in, modes_total, first):
    modes, parts, nv, slots, height, width = x.shape
    state_block = (1, parts, nv, slots, height, width)
    edge_block = (2, 1, slots, parts * nv, width)
    state_spec = pl.BlockSpec(state_block, lambda m, t: (m, 0, 0, 0, 0, 0))
    edge_spec = pl.BlockSpec(edge_block, lambda m, t: (0, m, 0, 0, 0))
    flow_spec = pl.BlockSpec((slots, height, width), lambda m, t: (0, 0, 0))
    vel_spec = pl.BlockSpec((2, slots, height, width), lambda m, t: (0, 0, 0, 0))
    in_specs = [state_spec, state_spec, edge_spec, edge_spec, flow_spec, vel_spec, flow_spec]
    args = [x, a, rlo, rhi, density, velocity, pressure]
    if not first:
        in_specs.append(flow_spec)
        args.append(sens_in)
    out_shape = [
        jax.ShapeDtypeStruct(x.shape, jnp.float32),
        jax.ShapeDtypeStruct(a.shape, jnp.float32),
        jax.ShapeDtypeStruct((slots, height, width), jnp.float32),
    ]
    out_specs = [state_spec, state_spec, flow_spec]
    if first:
        edge_shape = jax.ShapeDtypeStruct((2, modes, slots, parts * nv, width), jnp.float32)
        out_shape += [edge_shape, edge_shape]
        out_specs += [edge_spec, edge_spec]
    grid_spec = pltpu.PrefetchScalarGridSpec(
        num_scalar_prefetch=1,
        grid=(modes,),
        in_specs=in_specs,
        out_specs=out_specs,
        scratch_shapes=[pltpu.VMEM((2, 2, slots, parts * nv, width), jnp.float32)],
    )
    kernel = functools.partial(step_kernel, modes_total=modes_total, first=first)
    return pl.pallas_call(
        kernel,
        grid_spec=grid_spec,
        out_shape=out_shape,
        compiler_params=pltpu.CompilerParams(dimension_semantics=("arbitrary",)),
    )(tbl, *args)


def edges(x, row):
    modes, parts, nv, slots, height, width = x.shape
    e = x[:, :, :, :, row, :]
    return jnp.transpose(e, (0, 3, 1, 2, 4)).reshape(modes, slots, parts * nv, width)


def per_device(direct, adjoint, density, velocity, pressure, block_home, face_nbr, face_flip):
    modes, parts, nv, slots, height, width = direct.shape
    modes_total = modes * lax.axis_size("mode")
    live = (face_nbr >= 0).astype(jnp.int32)
    positions = jnp.take(block_home, jnp.maximum(face_nbr, 0), axis=0)
    slot_of = positions % slots
    table = jnp.stack(
        [
            slot_of[:, 0], face_flip[:, 0], slot_of[:, 1], face_flip[:, 1],
            slot_of[:, 2], live[:, 2], slot_of[:, 3], live[:, 3],
        ],
        axis=1,
    ).reshape(-1)
    mode_base = (lax.axis_index("mode") * modes).astype(jnp.int32)
    table = jnp.concatenate([table.astype(jnp.int32), mode_base[None]])

    with jax.named_scope("edge_exchange_0"):
        up = jnp.stack([edges(direct, height - 1), edges(adjoint, height - 1)])
        down = jnp.stack([edges(direct, 0), edges(adjoint, 0)])
        rlo = shifted(up, "blk", 1)
        rhi = shifted(down, "blk", -1)
    with jax.named_scope("flow_step_0"):
        q1, a1, sens, elo, ehi = run_step(
            table, direct, adjoint, rlo, rhi, density, velocity, pressure, None, modes_total, True
        )
    with jax.named_scope("edge_exchange_1"):
        rlo = shifted(ehi, "blk", 1)
        rhi = shifted(elo, "blk", -1)
    with jax.named_scope("flow_step_1"):
        q2, a2, sens = run_step(
            table, q1, a1, rlo, rhi, density, velocity, pressure, sens, modes_total, False
        )
    with jax.named_scope("mode_reduce"):
        count = lax.axis_size("mode")
        me = lax.axis_index("mode")
        stacked = jnp.stack([sens] + [shifted(sens, "mode", k) for k in range(1, count)])
        total = None
        for j in range(count):
            part = lax.dynamic_index_in_dim(stacked, (me - j) % count, axis=0, keepdims=False)
            total = part if total is None else total + part
        sensitivity = total / (STEPS * modes_total)
    return (q2, a2, sensitivity)


def solution(mesh):
    placed = (
        P("mode", None, None, "blk", None, None),
        P("mode", None, None, "blk", None, None),
        P("blk", None, None),
        P(None, "blk", None, None),
        P("blk", None, None),
        P(),
        P("blk", None),
        P("blk", None),
    )
    return jax.shard_map(
        per_device,
        mesh=mesh,
        in_specs=placed,
        out_specs=(
            P("mode", None, None, "blk", None, None),
            P("mode", None, None, "blk", None, None),
            P("blk", None, None),
        ),
        check_vma=False,
    )
```

```python
import functools

import jax
import jax.numpy as jnp
from jax import lax
from jax.experimental import pallas as pl
from jax.experimental.pallas import tpu as pltpu
from jax.sharding import PartitionSpec as P

STEPS = 2

HEAT_RATIO = 1.4
VISCOSITY = 0.25
TIME_STEP = 0.05
SPAN_WAVE = 0.5
BASE_FREQ = 0.2

NV = 5
ENTRIES = 8


def shifted(block, axis, distance):
    n = lax.axis_size(axis)
    route = [((i - distance) % n, i) for i in range(n)]
    return lax.ppermute(block, axis, route)


def direct_rates(bf, X, Y, dsX, dcX, lapX, dsY, dcY, lapY, w):
    r, ir, u, v, kp = bf
    b = SPAN_WAVE
    damp = SPAN_WAVE * SPAN_WAVE

    def conv(ds, dc):
        return [
            u * ds[0] + r * ds[1] + (v * dc[0] + r * dc[2]),
            u * ds[1] + ds[4] * ir + v * dc[1],
            u * ds[2] + (v * dc[2] + dc[4] * ir),
            u * ds[3] + v * dc[3],
            kp * ds[1] + u * ds[4] + (kp * dc[2] + v * dc[4]),
        ]

    def span(f):
        return [r * f[3], None, None, f[4] * ir, kp * f[3]]

    cX = conv(dsX, dcX)
    cY = conv(dsY, dcY)
    sX = span(X)
    sY = span(Y)
    re, im = [], []
    for n in range(NV):
        a = -cX[n] + VISCOSITY * (lapX[n] - damp * X[n])
        if sY[n] is not None:
            a = a + b * sY[n]
        a = a + w * Y[n]
        c = -cY[n] + VISCOSITY * (lapY[n] - damp * Y[n])
        if sX[n] is not None:
            c = c - b * sX[n]
        c = c - w * X[n]
        re.append(a)
        im.append(c)
    return re, im


def adjoint_rates(bf, X, Y, dsX, dcX, lapX, dsY, dcY, lapY, w):
    r, ir, u, v, kp = bf
    b = SPAN_WAVE
    damp = SPAN_WAVE * SPAN_WAVE

    def conv(ds, dc):
        return [
            u * ds[0] + v * dc[0],
            r * ds[0] + u * ds[1] + kp * ds[4] + v * dc[1],
            u * ds[2] + (r * dc[0] + v * dc[2] + kp * dc[4]),
            u * ds[3] + v * dc[3],
            ds[1] * ir + u * ds[4] + (dc[2] * ir + v * dc[4]),
        ]

    def span(f):
        return [None, None, None, r * f[0] + kp * f[4], f[3] * ir]

    cX = conv(dsX, dcX)
    cY = conv(dsY, dcY)
    sX = span(X)
    sY = span(Y)
    re, im = [], []
    for n in range(NV):
        a = cX[n] + VISCOSITY * (lapX[n] - damp * X[n])
        if sY[n] is not None:
            a = a - b * sY[n]
        a = a - w * Y[n]
        c = cY[n] + VISCOSITY * (lapY[n] - damp * Y[n])
        if sX[n] is not None:
            c = c + b * sX[n]
        c = c + w * X[n]
        re.append(a)
        im.append(c)
    return re, im


LANES = 128


def step_kernel(tbl, x_ref, a_ref, recv_ref, turn_ref, rho_ref, vel_ref, prs_ref, *rest, modes_total, first):
    if first:
        xo_ref, ao_ref, sens_ref, elo_ref, ehi_ref, gh_ref = rest
    else:
        sin_ref, xo_ref, ao_ref, sens_ref, gh_ref = rest
    m = pl.program_id(0)
    slots = x_ref.shape[3]
    height = x_ref.shape[4]
    width = x_ref.shape[5]
    chunks = width // LANES
    shape = (height, LANES)
    full = (height, width)

    @pl.when(m == 0)
    def _init():
        if first:
            sens_ref[...] = jnp.zeros(sens_ref.shape, jnp.float32)
        else:
            sens_ref[...] = sin_ref[...]

    for s in range(slots):
        for side, (tcol, fcol) in enumerate(((0, 1), (2, 3))):
            t = tbl[s * ENTRIES + tcol]
            f = tbl[s * ENTRIES + fcol]
            for arr in range(2):
                plain = recv_ref[side, arr, 0, t]
                turned = turn_ref[side, arr, 0, t]
                flag = (jnp.zeros(plain.shape, jnp.int32) + f) != 0
                gh_ref[arr, side, s] = jnp.where(flag, turned, plain)

    kf = (tbl[slots * ENTRIES] + m).astype(jnp.float32)
    w = BASE_FREQ * (jnp.zeros(shape, jnp.float32) + (kf - modes_total / 2 + 0.5))
    row = lax.broadcasted_iota(jnp.int32, shape, 0)
    lane = lax.broadcasted_iota(jnp.int32, shape, 1)
    zero_i = jnp.zeros(shape, jnp.int32)
    first_row = row == 0
    last_row = row == height - 1
    first_lane = lane == 0
    last_lane = lane == LANES - 1
    for s in range(slots):
        base = s * ENTRIES
        jl_s, jl_live = tbl[base + 4], tbl[base + 5]
        jh_s, jh_live = tbl[base + 6], tbl[base + 7]
        jl_mask = (zero_i + jl_live) != 0
        jh_mask = (zero_i + jh_live) != 0
        for b in range(chunks):
            cs = slice(b * LANES, (b + 1) * LANES)
            r = rho_ref[s, :, cs]
            ir = 1.0 / r
            u = vel_ref[0, s, :, cs]
            v = vel_ref[1, s, :, cs]
            kp = HEAT_RATIO * prs_ref[s, :, cs]
            bf = (r, ir, u, v, kp)
            means = []
            for arr, (src, dst, rates) in enumerate(((x_ref, xo_ref, direct_rates), (a_ref, ao_ref, adjoint_rates))):
                vals, dss, dcs, laps = [], [], [], []
                for p in range(2):
                    for n in range(NV):
                        k = p * NV + n
                        g = src[0, p, n, s, :, cs]
                        lo_b = jnp.broadcast_to(gh_ref[arr, 0, s, k:k + 1, cs], shape)
                        hi_b = jnp.broadcast_to(gh_ref[arr, 1, s, k:k + 1, cs], shape)
                        im1 = jnp.where(first_row, lo_b, pltpu.roll(g, 1, 0))
                        ip1 = jnp.where(last_row, hi_b, pltpu.roll(g, height - 1, 0))
                        if b > 0:
                            left = src[0, p, n, s, :, (b - 1) * LANES:b * LANES]
                        else:
                            left = jnp.where(jl_mask, src[0, p, n, jl_s, :, width - LANES:width], 0.0)
                        if b < chunks - 1:
                            right = src[0, p, n, s, :, (b + 1) * LANES:(b + 2) * LANES]
                        else:
                            right = jnp.where(jh_mask, src[0, p, n, jh_s, :, 0:LANES], 0.0)
                        jm1 = jnp.where(first_lane, pltpu.roll(left, 1, 1), pltpu.roll(g, 1, 1))
                        jp1 = jnp.where(last_lane, pltpu.roll(right, LANES - 1, 1), pltpu.roll(g, LANES - 1, 1))
                        vals.append(g)
                        dss.append((ip1 - im1) * 0.5)
                        dcs.append((jp1 - jm1) * 0.5)
                        laps.append(ip1 + im1 + jp1 + jm1 - 4.0 * g)
                X, Y = vals[:NV], vals[NV:]
                re, im = rates(bf, X, Y, dss[:NV], dcs[:NV], laps[:NV], dss[NV:], dcs[NV:], laps[NV:], w)
                total = None
                for p, rate in enumerate((re, im)):
                    for n in range(NV):
                        k = p * NV + n
                        nv = vals[k] + TIME_STEP * rate[n]
                        dst[0, p, n, s, :, cs] = nv
                        if first:
                            elo_ref[arr, 0, s, pl.ds(k, 1), cs] = nv[0:1, :]
                            ehi_ref[arr, 0, s, pl.ds(k, 1), cs] = nv[height - 1:height, :]
                        sq = nv * nv
                        total = sq if total is None else total + sq
                means.append(total / 10.0)
            sens_ref[s, :, cs] = sens_ref[s, :, cs] + means[0] * means[1]


def run_step(tbl, x, a, recv, turned, density, velocity, pressure, sens_in, modes_total, first):
    modes, parts, nv, slots, height, width = x.shape
    state_block = (1, parts, nv, slots, height, width)
    edge_block = (2, 1, slots, parts * nv, width)
    state_spec = pl.BlockSpec(state_block, lambda m, t: (m, 0, 0, 0, 0, 0))
    edge_spec = pl.BlockSpec(edge_block, lambda m, t: (0, m, 0, 0, 0))
    both_spec = pl.BlockSpec((2,) + edge_block, lambda m, t: (0, 0, m, 0, 0, 0))
    flow_spec = pl.BlockSpec((slots, height, width), lambda m, t: (0, 0, 0))
    vel_spec = pl.BlockSpec((2, slots, height, width), lambda m, t: (0, 0, 0, 0))
    in_specs = [state_spec, state_spec, both_spec, both_spec, flow_spec, vel_spec, flow_spec]
    args = [x, a, recv, turned, density, velocity, pressure]
    if not first:
        in_specs.append(flow_spec)
        args.append(sens_in)
    out_shape = [
        jax.ShapeDtypeStruct(x.shape, jnp.float32),
        jax.ShapeDtypeStruct(a.shape, jnp.float32),
        jax.ShapeDtypeStruct((slots, height, width), jnp.float32),
    ]
    out_specs = [state_spec, state_spec, flow_spec]
    if first:
        edge_shape = jax.ShapeDtypeStruct((2, modes, slots, parts * nv, width), jnp.float32)
        out_shape += [edge_shape, edge_shape]
        out_specs += [edge_spec, edge_spec]
    grid_spec = pltpu.PrefetchScalarGridSpec(
        num_scalar_prefetch=1,
        grid=(modes,),
        in_specs=in_specs,
        out_specs=out_specs,
        scratch_shapes=[
            pltpu.VMEM((2, 2, slots, parts * nv, width), jnp.float32),
        ],
    )
    kernel = functools.partial(step_kernel, modes_total=modes_total, first=first)
    return pl.pallas_call(
        kernel,
        grid_spec=grid_spec,
        out_shape=out_shape,
        compiler_params=pltpu.CompilerParams(dimension_semantics=("arbitrary",)),
    )(tbl, *args)


def reverse_lanes(rows):
    width = rows.shape[-1]
    ri = lax.broadcasted_iota(jnp.int32, (width, width), 0)
    ci = lax.broadcasted_iota(jnp.int32, (width, width), 1)
    turn = jnp.where(ri + ci == width - 1, 1.0, 0.0).astype(jnp.float32)
    flat = rows.reshape(-1, width)
    out = jnp.dot(flat, turn, precision=lax.Precision.HIGHEST, preferred_element_type=jnp.float32)
    return out.reshape(rows.shape)


def edges(x, row):
    modes, parts, nv, slots, height, width = x.shape
    e = x[:, :, :, :, row, :]
    return jnp.transpose(e, (0, 3, 1, 2, 4)).reshape(modes, slots, parts * nv, width)


def per_device(direct, adjoint, density, velocity, pressure, block_home, face_nbr, face_flip):
    modes, parts, nv, slots, height, width = direct.shape
    modes_total = modes * lax.axis_size("mode")
    live = (face_nbr >= 0).astype(jnp.int32)
    positions = jnp.take(block_home, jnp.maximum(face_nbr, 0), axis=0)
    slot_of = positions % slots
    table = jnp.stack(
        [
            slot_of[:, 0], face_flip[:, 0], slot_of[:, 1], face_flip[:, 1],
            slot_of[:, 2], live[:, 2], slot_of[:, 3], live[:, 3],
        ],
        axis=1,
    ).reshape(-1)
    mode_base = (lax.axis_index("mode") * modes).astype(jnp.int32)
    table = jnp.concatenate([table.astype(jnp.int32), mode_base[None]])

    with jax.named_scope("edge_exchange_0"):
        up = jnp.stack([edges(direct, height - 1), edges(adjoint, height - 1)])
        down = jnp.stack([edges(direct, 0), edges(adjoint, 0)])
        recv = jnp.stack([shifted(up, "blk", 1), shifted(down, "blk", -1)])
        turned = reverse_lanes(recv)
    with jax.named_scope("flow_step_0"):
        q1, a1, sens, elo, ehi = run_step(
            table, direct, adjoint, recv, turned, density, velocity, pressure, None, modes_total, True
        )
    with jax.named_scope("edge_exchange_1"):
        recv = jnp.stack([shifted(ehi, "blk", 1), shifted(elo, "blk", -1)])
        turned = reverse_lanes(recv)
    with jax.named_scope("flow_step_1"):
        q2, a2, sens = run_step(
            table, q1, a1, recv, turned, density, velocity, pressure, sens, modes_total, False
        )
    with jax.named_scope("mode_reduce"):
        count = lax.axis_size("mode")
        me = lax.axis_index("mode")
        stacked = jnp.stack([sens] + [shifted(sens, "mode", k) for k in range(1, count)])
        total = None
        for j in range(count):
            part = lax.dynamic_index_in_dim(stacked, (me - j) % count, axis=0, keepdims=False)
            total = part if total is None else total + part
        sensitivity = total / (STEPS * modes_total)
    return (q2, a2, sensitivity)


def solution(mesh):
    placed = (
        P("mode", None, None, "blk", None, None),
        P("mode", None, None, "blk", None, None),
        P("blk", None, None),
        P(None, "blk", None, None),
        P("blk", None, None),
        P(),
        P("blk", None),
        P("blk", None),
    )
    return jax.shard_map(
        per_device,
        mesh=mesh,
        in_specs=placed,
        out_specs=(
            P("mode", None, None, "blk", None, None),
            P("mode", None, None, "blk", None, None),
            P("blk", None, None),
        ),
        check_vma=False,
    )
```

```python
import functools

import jax
import jax.numpy as jnp
from jax import lax
from jax.experimental import pallas as pl
from jax.experimental.pallas import tpu as pltpu
from jax.sharding import PartitionSpec as P

STEPS = 2

HEAT_RATIO = 1.4
VISCOSITY = 0.25
TIME_STEP = 0.05
SPAN_WAVE = 0.5
BASE_FREQ = 0.2

NV = 5
ENTRIES = 8


def shifted(block, axis, distance):
    n = lax.axis_size(axis)
    route = [((i - distance) % n, i) for i in range(n)]
    return lax.ppermute(block, axis, route)


def direct_rates(bf, X, Y, dsX, dcX, lapX, dsY, dcY, lapY, w):
    r, ir, u, v, kp = bf
    b = SPAN_WAVE
    damp = SPAN_WAVE * SPAN_WAVE

    def conv(ds, dc):
        return [
            u * ds[0] + r * ds[1] + (v * dc[0] + r * dc[2]),
            u * ds[1] + ds[4] * ir + v * dc[1],
            u * ds[2] + (v * dc[2] + dc[4] * ir),
            u * ds[3] + v * dc[3],
            kp * ds[1] + u * ds[4] + (kp * dc[2] + v * dc[4]),
        ]

    def span(f):
        return [r * f[3], None, None, f[4] * ir, kp * f[3]]

    cX = conv(dsX, dcX)
    cY = conv(dsY, dcY)
    sX = span(X)
    sY = span(Y)
    re, im = [], []
    for n in range(NV):
        a = -cX[n] + VISCOSITY * (lapX[n] - damp * X[n])
        if sY[n] is not None:
            a = a + b * sY[n]
        a = a + w * Y[n]
        c = -cY[n] + VISCOSITY * (lapY[n] - damp * Y[n])
        if sX[n] is not None:
            c = c - b * sX[n]
        c = c - w * X[n]
        re.append(a)
        im.append(c)
    return re, im


def adjoint_rates(bf, X, Y, dsX, dcX, lapX, dsY, dcY, lapY, w):
    r, ir, u, v, kp = bf
    b = SPAN_WAVE
    damp = SPAN_WAVE * SPAN_WAVE

    def conv(ds, dc):
        return [
            u * ds[0] + v * dc[0],
            r * ds[0] + u * ds[1] + kp * ds[4] + v * dc[1],
            u * ds[2] + (r * dc[0] + v * dc[2] + kp * dc[4]),
            u * ds[3] + v * dc[3],
            ds[1] * ir + u * ds[4] + (dc[2] * ir + v * dc[4]),
        ]

    def span(f):
        return [None, None, None, r * f[0] + kp * f[4], f[3] * ir]

    cX = conv(dsX, dcX)
    cY = conv(dsY, dcY)
    sX = span(X)
    sY = span(Y)
    re, im = [], []
    for n in range(NV):
        a = cX[n] + VISCOSITY * (lapX[n] - damp * X[n])
        if sY[n] is not None:
            a = a - b * sY[n]
        a = a - w * Y[n]
        c = cY[n] + VISCOSITY * (lapY[n] - damp * Y[n])
        if sX[n] is not None:
            c = c + b * sX[n]
        c = c + w * X[n]
        re.append(a)
        im.append(c)
    return re, im


LANES = 128


def step_kernel(tbl, x_ref, a_ref, rlo_ref, rhi_ref, tlo_ref, thi_ref, rho_ref, vel_ref, prs_ref, *rest, modes_total, first):
    if first:
        xo_ref, ao_ref, sens_ref, elo_ref, ehi_ref, gh_ref = rest
    else:
        sin_ref, xo_ref, ao_ref, sens_ref, gh_ref = rest
    m = pl.program_id(0)
    slots = x_ref.shape[3]
    height = x_ref.shape[4]
    width = x_ref.shape[5]
    chunks = width // LANES
    shape = (height, LANES)
    full = (height, width)

    @pl.when(m == 0)
    def _init():
        if first:
            sens_ref[...] = jnp.zeros(sens_ref.shape, jnp.float32)
        else:
            sens_ref[...] = sin_ref[...]

    for s in range(slots):
        for side, (recv_ref, turn_ref, tcol, fcol) in enumerate(((rlo_ref, tlo_ref, 0, 1), (rhi_ref, thi_ref, 2, 3))):
            t = tbl[s * ENTRIES + tcol]
            f = tbl[s * ENTRIES + fcol]
            for arr in range(2):
                plain = recv_ref[arr, 0, t]
                turned = turn_ref[arr, 0, t]
                flag = (jnp.zeros(plain.shape, jnp.int32) + f) != 0
                gh_ref[arr, side, s] = jnp.where(flag, turned, plain)

    kf = (tbl[slots * ENTRIES] + m).astype(jnp.float32)
    w = BASE_FREQ * (jnp.zeros(shape, jnp.float32) + (kf - modes_total / 2 + 0.5))
    row = lax.broadcasted_iota(jnp.int32, shape, 0)
    lane = lax.broadcasted_iota(jnp.int32, shape, 1)
    zero_i = jnp.zeros(shape, jnp.int32)
    first_row = row == 0
    last_row = row == height - 1
    first_lane = lane == 0
    last_lane = lane == LANES - 1
    for s in range(slots):
        base = s * ENTRIES
        jl_s, jl_live = tbl[base + 4], tbl[base + 5]
        jh_s, jh_live = tbl[base + 6], tbl[base + 7]
        jl_mask = (zero_i + jl_live) != 0
        jh_mask = (zero_i + jh_live) != 0
        for b in range(chunks):
            cs = slice(b * LANES, (b + 1) * LANES)
            r = rho_ref[s, :, cs]
            ir = 1.0 / r
            u = vel_ref[0, s, :, cs]
            v = vel_ref[1, s, :, cs]
            kp = HEAT_RATIO * prs_ref[s, :, cs]
            bf = (r, ir, u, v, kp)
            means = []
            for arr, (src, dst, rates) in enumerate(((x_ref, xo_ref, direct_rates), (a_ref, ao_ref, adjoint_rates))):
                vals, dss, dcs, laps = [], [], [], []
                for p in range(2):
                    for n in range(NV):
                        k = p * NV + n
                        g = src[0, p, n, s, :, cs]
                        lo_b = jnp.broadcast_to(gh_ref[arr, 0, s, k:k + 1, cs], shape)
                        hi_b = jnp.broadcast_to(gh_ref[arr, 1, s, k:k + 1, cs], shape)
                        im1 = jnp.where(first_row, lo_b, pltpu.roll(g, 1, 0))
                        ip1 = jnp.where(last_row, hi_b, pltpu.roll(g, height - 1, 0))
                        if b > 0:
                            left = src[0, p, n, s, :, (b - 1) * LANES:b * LANES]
                        else:
                            left = jnp.where(jl_mask, src[0, p, n, jl_s, :, width - LANES:width], 0.0)
                        if b < chunks - 1:
                            right = src[0, p, n, s, :, (b + 1) * LANES:(b + 2) * LANES]
                        else:
                            right = jnp.where(jh_mask, src[0, p, n, jh_s, :, 0:LANES], 0.0)
                        jm1 = jnp.where(first_lane, pltpu.roll(left, 1, 1), pltpu.roll(g, 1, 1))
                        jp1 = jnp.where(last_lane, pltpu.roll(right, LANES - 1, 1), pltpu.roll(g, LANES - 1, 1))
                        vals.append(g)
                        dss.append((ip1 - im1) * 0.5)
                        dcs.append((jp1 - jm1) * 0.5)
                        laps.append(ip1 + im1 + jp1 + jm1 - 4.0 * g)
                X, Y = vals[:NV], vals[NV:]
                re, im = rates(bf, X, Y, dss[:NV], dcs[:NV], laps[:NV], dss[NV:], dcs[NV:], laps[NV:], w)
                total = None
                for p, rate in enumerate((re, im)):
                    for n in range(NV):
                        k = p * NV + n
                        nv = vals[k] + TIME_STEP * rate[n]
                        dst[0, p, n, s, :, cs] = nv
                        if first:
                            elo_ref[arr, 0, s, pl.ds(k, 1), cs] = nv[0:1, :]
                            ehi_ref[arr, 0, s, pl.ds(k, 1), cs] = nv[height - 1:height, :]
                        sq = nv * nv
                        total = sq if total is None else total + sq
                means.append(total / 10.0)
            sens_ref[s, :, cs] = sens_ref[s, :, cs] + means[0] * means[1]


def run_step(tbl, x, a, rlo, rhi, density, velocity, pressure, sens_in, modes_total, first):
    modes, parts, nv, slots, height, width = x.shape
    state_block = (1, parts, nv, slots, height, width)
    edge_block = (2, 1, slots, parts * nv, width)
    state_spec = pl.BlockSpec(state_block, lambda m, t: (m, 0, 0, 0, 0, 0))
    edge_spec = pl.BlockSpec(edge_block, lambda m, t: (0, m, 0, 0, 0))
    flow_spec = pl.BlockSpec((slots, height, width), lambda m, t: (0, 0, 0))
    vel_spec = pl.BlockSpec((2, slots, height, width), lambda m, t: (0, 0, 0, 0))
    in_specs = [state_spec, state_spec, edge_spec, edge_spec, edge_spec, edge_spec, flow_spec, vel_spec, flow_spec]
    args = [x, a, rlo, rhi, reverse_lanes(rlo), reverse_lanes(rhi), density, velocity, pressure]
    if not first:
        in_specs.append(flow_spec)
        args.append(sens_in)
    out_shape = [
        jax.ShapeDtypeStruct(x.shape, jnp.float32),
        jax.ShapeDtypeStruct(a.shape, jnp.float32),
        jax.ShapeDtypeStruct((slots, height, width), jnp.float32),
    ]
    out_specs = [state_spec, state_spec, flow_spec]
    if first:
        edge_shape = jax.ShapeDtypeStruct((2, modes, slots, parts * nv, width), jnp.float32)
        out_shape += [edge_shape, edge_shape]
        out_specs += [edge_spec, edge_spec]
    grid_spec = pltpu.PrefetchScalarGridSpec(
        num_scalar_prefetch=1,
        grid=(modes,),
        in_specs=in_specs,
        out_specs=out_specs,
        scratch_shapes=[
            pltpu.VMEM((2, 2, slots, parts * nv, width), jnp.float32),
        ],
    )
    kernel = functools.partial(step_kernel, modes_total=modes_total, first=first)
    return pl.pallas_call(
        kernel,
        grid_spec=grid_spec,
        out_shape=out_shape,
        compiler_params=pltpu.CompilerParams(dimension_semantics=("arbitrary",)),
    )(tbl, *args)


def reverse_lanes(rows):
    width = rows.shape[-1]
    ri = lax.broadcasted_iota(jnp.int32, (width, width), 0)
    ci = lax.broadcasted_iota(jnp.int32, (width, width), 1)
    turn = jnp.where(ri + ci == width - 1, 1.0, 0.0).astype(jnp.float32)
    flat = rows.reshape(-1, width)
    out = jnp.dot(flat, turn, precision=lax.Precision.HIGHEST, preferred_element_type=jnp.float32)
    return out.reshape(rows.shape)


def edge_kernel(x_ref, a_ref, lo_ref, hi_ref):
    nv = x_ref.shape[2]
    height = x_ref.shape[4]
    for arr, src in enumerate((x_ref, a_ref)):
        for p in range(x_ref.shape[1]):
            for n in range(nv):
                k = p * nv + n
                for s in range(x_ref.shape[3]):
                    lo_ref[arr, 0, s, pl.ds(k, 1), :] = src[0, p, n, s, 0:1, :]
                    hi_ref[arr, 0, s, pl.ds(k, 1), :] = src[0, p, n, s, height - 1:height, :]


def edge_rows(x, a):
    modes, parts, nv, slots, height, width = x.shape
    state_spec = pl.BlockSpec((1, parts, nv, slots, height, width), lambda m: (m, 0, 0, 0, 0, 0))
    edge_spec = pl.BlockSpec((2, 1, slots, parts * nv, width), lambda m: (0, m, 0, 0, 0))
    edge_shape = jax.ShapeDtypeStruct((2, modes, slots, parts * nv, width), jnp.float32)
    return pl.pallas_call(
        edge_kernel,
        grid=(modes,),
        in_specs=[state_spec, state_spec],
        out_specs=[edge_spec, edge_spec],
        out_shape=[edge_shape, edge_shape],
    )(x, a)


def per_device(direct, adjoint, density, velocity, pressure, block_home, face_nbr, face_flip):
    modes, parts, nv, slots, height, width = direct.shape
    modes_total = modes * lax.axis_size("mode")
    live = (face_nbr >= 0).astype(jnp.int32)
    positions = jnp.take(block_home, jnp.maximum(face_nbr, 0), axis=0)
    slot_of = positions % slots
    table = jnp.stack(
        [
            slot_of[:, 0], face_flip[:, 0], slot_of[:, 1], face_flip[:, 1],
            slot_of[:, 2], live[:, 2], slot_of[:, 3], live[:, 3],
        ],
        axis=1,
    ).reshape(-1)
    mode_base = (lax.axis_index("mode") * modes).astype(jnp.int32)
    table = jnp.concatenate([table.astype(jnp.int32), mode_base[None]])

    with jax.named_scope("edge_exchange_0"):
        down, up = edge_rows(direct, adjoint)
        rlo = shifted(up, "blk", 1)
        rhi = shifted(down, "blk", -1)
    with jax.named_scope("flow_step_0"):
        q1, a1, sens, elo, ehi = run_step(
            table, direct, adjoint, rlo, rhi, density, velocity, pressure, None, modes_total, True
        )
    with jax.named_scope("edge_exchange_1"):
        rlo = shifted(ehi, "blk", 1)
        rhi = shifted(elo, "blk", -1)
    with jax.named_scope("flow_step_1"):
        q2, a2, sens = run_step(
            table, q1, a1, rlo, rhi, density, velocity, pressure, sens, modes_total, False
        )
    with jax.named_scope("mode_reduce"):
        count = lax.axis_size("mode")
        me = lax.axis_index("mode")
        stacked = jnp.stack([sens] + [shifted(sens, "mode", k) for k in range(1, count)])
        total = None
        for j in range(count):
            part = lax.dynamic_index_in_dim(stacked, (me - j) % count, axis=0, keepdims=False)
            total = part if total is None else total + part
        sensitivity = total / (STEPS * modes_total)
    return (q2, a2, sensitivity)


def solution(mesh):
    placed = (
        P("mode", None, None, "blk", None, None),
        P("mode", None, None, "blk", None, None),
        P("blk", None, None),
        P(None, "blk", None, None),
        P("blk", None, None),
        P(),
        P("blk", None),
        P("blk", None),
    )
    return jax.shard_map(
        per_device,
        mesh=mesh,
        in_specs=placed,
        out_specs=(
            P("mode", None, None, "blk", None, None),
            P("mode", None, None, "blk", None, None),
            P("blk", None, None),
        ),
        check_vma=False,
    )
```

```python
import functools

import jax
import jax.numpy as jnp
from jax import lax
from jax.experimental import pallas as pl
from jax.experimental.pallas import tpu as pltpu
from jax.sharding import PartitionSpec as P

STEPS = 2

HEAT_RATIO = 1.4
VISCOSITY = 0.25
TIME_STEP = 0.05
SPAN_WAVE = 0.5
BASE_FREQ = 0.2

NV = 5
ENTRIES = 8


def shifted(block, axis, distance):
    n = lax.axis_size(axis)
    route = [((i - distance) % n, i) for i in range(n)]
    return lax.ppermute(block, axis, route)


def direct_rates(bf, X, Y, dsX, dcX, lapX, dsY, dcY, lapY, w):
    r, ir, u, v, kp = bf
    b = SPAN_WAVE
    damp = SPAN_WAVE * SPAN_WAVE

    def conv(ds, dc):
        return [
            u * ds[0] + r * ds[1] + (v * dc[0] + r * dc[2]),
            u * ds[1] + ds[4] * ir + v * dc[1],
            u * ds[2] + (v * dc[2] + dc[4] * ir),
            u * ds[3] + v * dc[3],
            kp * ds[1] + u * ds[4] + (kp * dc[2] + v * dc[4]),
        ]

    def span(f):
        return [r * f[3], None, None, f[4] * ir, kp * f[3]]

    cX = conv(dsX, dcX)
    cY = conv(dsY, dcY)
    sX = span(X)
    sY = span(Y)
    re, im = [], []
    for n in range(NV):
        a = -cX[n] + VISCOSITY * (lapX[n] - damp * X[n])
        if sY[n] is not None:
            a = a + b * sY[n]
        a = a + w * Y[n]
        c = -cY[n] + VISCOSITY * (lapY[n] - damp * Y[n])
        if sX[n] is not None:
            c = c - b * sX[n]
        c = c - w * X[n]
        re.append(a)
        im.append(c)
    return re, im


def adjoint_rates(bf, X, Y, dsX, dcX, lapX, dsY, dcY, lapY, w):
    r, ir, u, v, kp = bf
    b = SPAN_WAVE
    damp = SPAN_WAVE * SPAN_WAVE

    def conv(ds, dc):
        return [
            u * ds[0] + v * dc[0],
            r * ds[0] + u * ds[1] + kp * ds[4] + v * dc[1],
            u * ds[2] + (r * dc[0] + v * dc[2] + kp * dc[4]),
            u * ds[3] + v * dc[3],
            ds[1] * ir + u * ds[4] + (dc[2] * ir + v * dc[4]),
        ]

    def span(f):
        return [None, None, None, r * f[0] + kp * f[4], f[3] * ir]

    cX = conv(dsX, dcX)
    cY = conv(dsY, dcY)
    sX = span(X)
    sY = span(Y)
    re, im = [], []
    for n in range(NV):
        a = cX[n] + VISCOSITY * (lapX[n] - damp * X[n])
        if sY[n] is not None:
            a = a - b * sY[n]
        a = a - w * Y[n]
        c = cY[n] + VISCOSITY * (lapY[n] - damp * Y[n])
        if sX[n] is not None:
            c = c + b * sX[n]
        c = c + w * X[n]
        re.append(a)
        im.append(c)
    return re, im


LANES = 128


def step_kernel(tbl, *refs, modes_total, first, ghosts, patched):
    refs = list(refs)
    x_ref, a_ref = refs[0], refs[1]
    refs = refs[2:]
    if ghosts:
        rlo_ref, rhi_ref, tlo_ref, thi_ref = refs[:4]
        refs = refs[4:]
    if patched:
        c0_ref, c7_ref = refs[:2]
        refs = refs[2:]
    rho_ref, vel_ref, prs_ref = refs[:3]
    refs = refs[3:]
    if not first:
        sin_ref = refs.pop(0)
    if first:
        xo_ref, ao_ref, sens_ref, elo_ref, ehi_ref, gh_ref = refs
    else:
        xo_ref, ao_ref, sens_ref, gh_ref = refs
    m = pl.program_id(0)
    slots = x_ref.shape[3]
    height = x_ref.shape[4]
    width = x_ref.shape[5]
    chunks = width // LANES
    shape = (height, LANES)

    @pl.when(m == 0)
    def _init():
        if first:
            sens_ref[...] = jnp.zeros(sens_ref.shape, jnp.float32)
        else:
            sens_ref[...] = sin_ref[...]

    for s in range(slots):
        for side, (tcol, fcol) in enumerate(((0, 1), (2, 3))):
            t = tbl[s * ENTRIES + tcol]
            f = tbl[s * ENTRIES + fcol]
            for arr in range(2):
                if ghosts:
                    recv_ref, turn_ref = ((rlo_ref, tlo_ref), (rhi_ref, thi_ref))[side]
                    plain = recv_ref[arr, 0, t]
                    turned = turn_ref[arr, 0, t]
                    flag = (jnp.zeros(plain.shape, jnp.int32) + f) != 0
                    gh_ref[arr, side, s] = jnp.where(flag, turned, plain)
                else:
                    gh_ref[arr, side, s] = jnp.zeros(gh_ref.shape[3:], jnp.float32)

    kf = (tbl[slots * ENTRIES] + m).astype(jnp.float32)
    w = BASE_FREQ * (jnp.zeros(shape, jnp.float32) + (kf - modes_total / 2 + 0.5))
    row = lax.broadcasted_iota(jnp.int32, shape, 0)
    lane = lax.broadcasted_iota(jnp.int32, shape, 1)
    zero_i = jnp.zeros(shape, jnp.int32)
    first_row = row == 0
    last_row = row == height - 1
    first_lane = lane == 0
    last_lane = lane == LANES - 1
    def load(src, arr, p, n, slot, k, cols):
        g = src[0, p, n, slot, :, cols]
        if patched:
            top = jnp.broadcast_to(c0_ref[arr, 0, slot, pl.ds(k, 1), cols], shape)
            bottom = jnp.broadcast_to(c7_ref[arr, 0, slot, pl.ds(k, 1), cols], shape)
            g = jnp.where(first_row, top, jnp.where(last_row, bottom, g))
        return g

    inner = (row > 0) & (row < height - 1)

    for s in range(slots):
        base = s * ENTRIES
        jl_s, jl_live = tbl[base + 4], tbl[base + 5]
        jh_s, jh_live = tbl[base + 6], tbl[base + 7]
        jl_mask = (zero_i + jl_live) != 0
        jh_mask = (zero_i + jh_live) != 0
        for b in range(chunks):
            cs = slice(b * LANES, (b + 1) * LANES)
            r = rho_ref[s, :, cs]
            ir = 1.0 / r
            u = vel_ref[0, s, :, cs]
            v = vel_ref[1, s, :, cs]
            kp = HEAT_RATIO * prs_ref[s, :, cs]
            bf = (r, ir, u, v, kp)
            means = []
            for arr, (src, dst, rates) in enumerate(((x_ref, xo_ref, direct_rates), (a_ref, ao_ref, adjoint_rates))):
                vals, dss, dcs, laps = [], [], [], []
                for p in range(2):
                    for n in range(NV):
                        k = p * NV + n
                        g = load(src, arr, p, n, s, k, cs)
                        lo_b = jnp.broadcast_to(gh_ref[arr, 0, s, k:k + 1, cs], shape)
                        hi_b = jnp.broadcast_to(gh_ref[arr, 1, s, k:k + 1, cs], shape)
                        im1 = jnp.where(first_row, lo_b, pltpu.roll(g, 1, 0))
                        ip1 = jnp.where(last_row, hi_b, pltpu.roll(g, height - 1, 0))
                        if b > 0:
                            left = load(src, arr, p, n, s, k, slice((b - 1) * LANES, b * LANES))
                        else:
                            left = jnp.where(jl_mask, load(src, arr, p, n, jl_s, k, slice(width - LANES, width)), 0.0)
                        if b < chunks - 1:
                            right = load(src, arr, p, n, s, k, slice((b + 1) * LANES, (b + 2) * LANES))
                        else:
                            right = jnp.where(jh_mask, load(src, arr, p, n, jh_s, k, slice(0, LANES)), 0.0)
                        jm1 = jnp.where(first_lane, pltpu.roll(left, 1, 1), pltpu.roll(g, 1, 1))
                        jp1 = jnp.where(last_lane, pltpu.roll(right, LANES - 1, 1), pltpu.roll(g, LANES - 1, 1))
                        vals.append(g)
                        dss.append((ip1 - im1) * 0.5)
                        dcs.append((jp1 - jm1) * 0.5)
                        laps.append(ip1 + im1 + jp1 + jm1 - 4.0 * g)
                X, Y = vals[:NV], vals[NV:]
                re, im = rates(bf, X, Y, dss[:NV], dcs[:NV], laps[:NV], dss[NV:], dcs[NV:], laps[NV:], w)
                total = None
                for p, rate in enumerate((re, im)):
                    for n in range(NV):
                        k = p * NV + n
                        nv = vals[k] + TIME_STEP * rate[n]
                        dst[0, p, n, s, :, cs] = nv
                        if first:
                            elo_ref[arr, 0, s, pl.ds(k, 1), cs] = nv[0:1, :]
                            ehi_ref[arr, 0, s, pl.ds(k, 1), cs] = nv[height - 1:height, :]
                        sq = nv * nv
                        total = sq if total is None else total + sq
                means.append(total / 10.0)
            term = means[0] * means[1]
            if not ghosts:
                term = jnp.where(inner, term, 0.0)
            sens_ref[s, :, cs] = sens_ref[s, :, cs] + term


def run_step(tbl, x, a, rlo, rhi, patch, density, velocity, pressure, sens_in, modes_total, first):
    modes, parts, nv, slots, height, width = x.shape
    state_block = (1, parts, nv, slots, height, width)
    edge_block = (2, 1, slots, parts * nv, width)
    state_spec = pl.BlockSpec(state_block, lambda m, t: (m, 0, 0, 0, 0, 0))
    edge_spec = pl.BlockSpec(edge_block, lambda m, t: (0, m, 0, 0, 0))
    flow_spec = pl.BlockSpec((slots, height, width), lambda m, t: (0, 0, 0))
    vel_spec = pl.BlockSpec((2, slots, height, width), lambda m, t: (0, 0, 0, 0))
    ghosts = rlo is not None
    patched = patch is not None
    in_specs = [state_spec, state_spec]
    args = [x, a]
    if ghosts:
        in_specs += [edge_spec] * 4
        args += [rlo, rhi, reverse_lanes(rlo), reverse_lanes(rhi)]
    if patched:
        in_specs += [edge_spec] * 2
        args += list(patch)
    in_specs += [flow_spec, vel_spec, flow_spec]
    args += [density, velocity, pressure]
    if not first:
        in_specs.append(flow_spec)
        args.append(sens_in)
    out_shape = [
        jax.ShapeDtypeStruct(x.shape, jnp.float32),
        jax.ShapeDtypeStruct(a.shape, jnp.float32),
        jax.ShapeDtypeStruct((slots, height, width), jnp.float32),
    ]
    out_specs = [state_spec, state_spec, flow_spec]
    if first:
        edge_shape = jax.ShapeDtypeStruct((2, modes, slots, parts * nv, width), jnp.float32)
        out_shape += [edge_shape, edge_shape]
        out_specs += [edge_spec, edge_spec]
    grid_spec = pltpu.PrefetchScalarGridSpec(
        num_scalar_prefetch=1,
        grid=(modes,),
        in_specs=in_specs,
        out_specs=out_specs,
        scratch_shapes=[
            pltpu.VMEM((2, 2, slots, parts * nv, width), jnp.float32),
        ],
    )
    kernel = functools.partial(step_kernel, modes_total=modes_total, first=first, ghosts=ghosts, patched=patched)
    return pl.pallas_call(
        kernel,
        grid_spec=grid_spec,
        out_shape=out_shape,
        compiler_params=pltpu.CompilerParams(dimension_semantics=("arbitrary",)),
    )(tbl, *args)


def ghost_term(f, r, ir, u, kp, transpose):
    if transpose:
        return [u * f[0], r * f[0] + u * f[1] + kp * f[4], u * f[2], u * f[3], f[1] * ir + u * f[4]]
    return [u * f[0] + r * f[1], u * f[1] + f[4] * ir, u * f[2], u * f[3], kp * f[1] + u * f[4]]


def fix_rows(partial0, partial7, rlo, rhi, slot_of, face_flip, density, velocity, pressure):
    _, modes, slots, rows, width = partial0.shape
    height = density.shape[1]

    def picked(recv, side):
        plain = jnp.take(recv, slot_of[:, side], axis=2)
        turned = reverse_lanes(plain)
        flag = (face_flip[:, side] != 0)[None, None, :, None, None]
        return jnp.where(flag, turned, plain)

    ghost = {0: picked(rlo, 0), height - 1: picked(rhi, 1)}
    partial = {0: partial0, height - 1: partial7}
    fixed = {}
    sens_rows = {}
    for row in (0, height - 1):
        r = density[:, row, :]
        ir = 1.0 / r
        u = velocity[0][:, row, :]
        kp = HEAT_RATIO * pressure[:, row, :]
        half = 0.5 if row == 0 else -0.5
        out = []
        for arr, sign in ((0, 1.0), (1, -1.0)):
            g = ghost[row][arr].reshape(modes, slots, 2, NV, width)
            res = []
            for p in range(2):
                f = [g[:, :, p, n, :] for n in range(NV)]
                conv = ghost_term(f, r, ir, u, kp, arr == 1)
                for n in range(NV):
                    res.append(sign * half * conv[n] + VISCOSITY * f[n])
            delta = jnp.stack(res, axis=2)
            out.append(partial[row][arr] + TIME_STEP * delta)
        fixed[row] = jnp.stack(out)
        means = jnp.sum(fixed[row] * fixed[row], axis=3) / 10.0
        sens_rows[row] = jnp.sum(means[0] * means[1], axis=0)
    return fixed[0], fixed[height - 1], sens_rows[0], sens_rows[height - 1]


def reverse_lanes(rows):
    width = rows.shape[-1]
    ri = lax.broadcasted_iota(jnp.int32, (width, width), 0)
    ci = lax.broadcasted_iota(jnp.int32, (width, width), 1)
    turn = jnp.where(ri + ci == width - 1, 1.0, 0.0).astype(jnp.float32)
    flat = rows.reshape(-1, width)
    out = jnp.dot(flat, turn, precision=lax.Precision.HIGHEST, preferred_element_type=jnp.float32)
    return out.reshape(rows.shape)


def edge_kernel(x_ref, a_ref, lo_ref, hi_ref):
    nv = x_ref.shape[2]
    height = x_ref.shape[4]
    for arr, src in enumerate((x_ref, a_ref)):
        for p in range(x_ref.shape[1]):
            for n in range(nv):
                k = p * nv + n
                for s in range(x_ref.shape[3]):
                    lo_ref[arr, 0, s, pl.ds(k, 1), :] = src[0, p, n, s, 0:1, :]
                    hi_ref[arr, 0, s, pl.ds(k, 1), :] = src[0, p, n, s, height - 1:height, :]


def edge_rows(x, a):
    modes, parts, nv, slots, height, width = x.shape
    state_spec = pl.BlockSpec((1, parts, nv, slots, height, width), lambda m: (m, 0, 0, 0, 0, 0))
    edge_spec = pl.BlockSpec((2, 1, slots, parts * nv, width), lambda m: (0, m, 0, 0, 0))
    edge_shape = jax.ShapeDtypeStruct((2, modes, slots, parts * nv, width), jnp.float32)
    return pl.pallas_call(
        edge_kernel,
        grid=(modes,),
        in_specs=[state_spec, state_spec],
        out_specs=[edge_spec, edge_spec],
        out_shape=[edge_shape, edge_shape],
    )(x, a)


def per_device(direct, adjoint, density, velocity, pressure, block_home, face_nbr, face_flip):
    modes, parts, nv, slots, height, width = direct.shape
    modes_total = modes * lax.axis_size("mode")
    live = (face_nbr >= 0).astype(jnp.int32)
    positions = jnp.take(block_home, jnp.maximum(face_nbr, 0), axis=0)
    slot_of = positions % slots
    table = jnp.stack(
        [
            slot_of[:, 0], face_flip[:, 0], slot_of[:, 1], face_flip[:, 1],
            slot_of[:, 2], live[:, 2], slot_of[:, 3], live[:, 3],
        ],
        axis=1,
    ).reshape(-1)
    mode_base = (lax.axis_index("mode") * modes).astype(jnp.int32)
    table = jnp.concatenate([table.astype(jnp.int32), mode_base[None]])

    with jax.named_scope("edge_exchange_0"):
        down, up = edge_rows(direct, adjoint)
        rlo = shifted(up, "blk", 1)
        rhi = shifted(down, "blk", -1)
    with jax.named_scope("flow_step_0"):
        q1, a1, sens, elo, ehi = run_step(
            table, direct, adjoint, None, None, None, density, velocity, pressure, None, modes_total, True
        )
    with jax.named_scope("edge_fix_0"):
        c0, c7, s0, s7 = fix_rows(elo, ehi, rlo, rhi, slot_of, face_flip, density, velocity, pressure)
        sens = sens.at[:, 0, :].add(s0).at[:, height - 1, :].add(s7)
    with jax.named_scope("edge_exchange_1"):
        rlo = shifted(c7, "blk", 1)
        rhi = shifted(c0, "blk", -1)
    with jax.named_scope("flow_step_1"):
        q2, a2, sens = run_step(
            table, q1, a1, rlo, rhi, (c0, c7), density, velocity, pressure, sens, modes_total, False
        )
    with jax.named_scope("mode_reduce"):
        count = lax.axis_size("mode")
        me = lax.axis_index("mode")
        stacked = jnp.stack([sens] + [shifted(sens, "mode", k) for k in range(1, count)])
        total = None
        for j in range(count):
            part = lax.dynamic_index_in_dim(stacked, (me - j) % count, axis=0, keepdims=False)
            total = part if total is None else total + part
        sensitivity = total / (STEPS * modes_total)
    return (q2, a2, sensitivity)


def solution(mesh):
    placed = (
        P("mode", None, None, "blk", None, None),
        P("mode", None, None, "blk", None, None),
        P("blk", None, None),
        P(None, "blk", None, None),
        P("blk", None, None),
        P(),
        P("blk", None),
        P("blk", None),
    )
    return jax.shard_map(
        per_device,
        mesh=mesh,
        in_specs=placed,
        out_specs=(
            P("mode", None, None, "blk", None, None),
            P("mode", None, None, "blk", None, None),
            P("blk", None, None),
        ),
        check_vma=False,
    )
```

```python
import functools

import jax
import jax.numpy as jnp
from jax import lax
from jax.experimental import pallas as pl
from jax.experimental.pallas import tpu as pltpu
from jax.sharding import PartitionSpec as P

STEPS = 2

HEAT_RATIO = 1.4
VISCOSITY = 0.25
TIME_STEP = 0.05
SPAN_WAVE = 0.5
BASE_FREQ = 0.2

NV = 5
ENTRIES = 8


def shifted(block, axis, distance):
    n = lax.axis_size(axis)
    route = [((i - distance) % n, i) for i in range(n)]
    return lax.ppermute(block, axis, route)


def direct_rates(bf, X, Y, dsX, dcX, lapX, dsY, dcY, lapY, w):
    r, ir, u, v, kp = bf
    b = SPAN_WAVE
    damp = SPAN_WAVE * SPAN_WAVE

    def conv(ds, dc):
        return [
            u * ds[0] + r * ds[1] + (v * dc[0] + r * dc[2]),
            u * ds[1] + ds[4] * ir + v * dc[1],
            u * ds[2] + (v * dc[2] + dc[4] * ir),
            u * ds[3] + v * dc[3],
            kp * ds[1] + u * ds[4] + (kp * dc[2] + v * dc[4]),
        ]

    def span(f):
        return [r * f[3], None, None, f[4] * ir, kp * f[3]]

    cX = conv(dsX, dcX)
    cY = conv(dsY, dcY)
    sX = span(X)
    sY = span(Y)
    re, im = [], []
    for n in range(NV):
        a = -cX[n] + VISCOSITY * (lapX[n] - damp * X[n])
        if sY[n] is not None:
            a = a + b * sY[n]
        a = a + w * Y[n]
        c = -cY[n] + VISCOSITY * (lapY[n] - damp * Y[n])
        if sX[n] is not None:
            c = c - b * sX[n]
        c = c - w * X[n]
        re.append(a)
        im.append(c)
    return re, im


def adjoint_rates(bf, X, Y, dsX, dcX, lapX, dsY, dcY, lapY, w):
    r, ir, u, v, kp = bf
    b = SPAN_WAVE
    damp = SPAN_WAVE * SPAN_WAVE

    def conv(ds, dc):
        return [
            u * ds[0] + v * dc[0],
            r * ds[0] + u * ds[1] + kp * ds[4] + v * dc[1],
            u * ds[2] + (r * dc[0] + v * dc[2] + kp * dc[4]),
            u * ds[3] + v * dc[3],
            ds[1] * ir + u * ds[4] + (dc[2] * ir + v * dc[4]),
        ]

    def span(f):
        return [None, None, None, r * f[0] + kp * f[4], f[3] * ir]

    cX = conv(dsX, dcX)
    cY = conv(dsY, dcY)
    sX = span(X)
    sY = span(Y)
    re, im = [], []
    for n in range(NV):
        a = cX[n] + VISCOSITY * (lapX[n] - damp * X[n])
        if sY[n] is not None:
            a = a - b * sY[n]
        a = a - w * Y[n]
        c = cY[n] + VISCOSITY * (lapY[n] - damp * Y[n])
        if sX[n] is not None:
            c = c + b * sX[n]
        c = c + w * X[n]
        re.append(a)
        im.append(c)
    return re, im


LANES = 128


def step_kernel(tbl, *refs, modes_total, first, ghosts, patched):
    refs = list(refs)
    x_ref, a_ref = refs[0], refs[1]
    refs = refs[2:]
    if ghosts:
        rlo_ref, rhi_ref, tlo_ref, thi_ref = refs[:4]
        refs = refs[4:]
    if patched:
        c0_ref, c7_ref = refs[:2]
        refs = refs[2:]
    rho_ref, vel_ref, prs_ref = refs[:3]
    refs = refs[3:]
    if not first:
        sin_ref = refs.pop(0)
    if first:
        xo_ref, ao_ref, sens_ref, elo_ref, ehi_ref, gh_ref = refs
    else:
        xo_ref, ao_ref, sens_ref, gh_ref = refs
    m = pl.program_id(0)
    slots = x_ref.shape[3]
    height = x_ref.shape[4]
    width = x_ref.shape[5]
    chunks = width // LANES
    shape = (height, LANES)

    @pl.when(m == 0)
    def _init():
        if first:
            sens_ref[...] = jnp.zeros(sens_ref.shape, jnp.float32)
        else:
            sens_ref[...] = sin_ref[...]

    for s in range(slots):
        for side, (tcol, fcol) in enumerate(((0, 1), (2, 3))):
            t = tbl[s * ENTRIES + tcol]
            f = tbl[s * ENTRIES + fcol]
            for arr in range(2):
                if ghosts:
                    recv_ref, turn_ref = ((rlo_ref, tlo_ref), (rhi_ref, thi_ref))[side]
                    plain = recv_ref[arr, 0, t]
                    turned = turn_ref[arr, 0, t]
                    flag = (jnp.zeros(plain.shape, jnp.int32) + f) != 0
                    gh_ref[arr, side, s] = jnp.where(flag, turned, plain)
                else:
                    gh_ref[arr, side, s] = jnp.zeros(gh_ref.shape[3:], jnp.float32)

    kf = (tbl[slots * ENTRIES] + m).astype(jnp.float32)
    w = BASE_FREQ * (jnp.zeros(shape, jnp.float32) + (kf - modes_total / 2 + 0.5))
    row = lax.broadcasted_iota(jnp.int32, shape, 0)
    lane = lax.broadcasted_iota(jnp.int32, shape, 1)
    zero_i = jnp.zeros(shape, jnp.int32)
    first_row = row == 0
    last_row = row == height - 1
    first_lane = lane == 0
    last_lane = lane == LANES - 1
    def load(src, arr, p, n, slot, k, cols):
        g = src[0, p, n, slot, :, cols]
        if patched:
            top = jnp.broadcast_to(c0_ref[arr, 0, slot, pl.ds(k, 1), cols], shape)
            bottom = jnp.broadcast_to(c7_ref[arr, 0, slot, pl.ds(k, 1), cols], shape)
            g = jnp.where(first_row, top, jnp.where(last_row, bottom, g))
        return g

    inner = (row > 0) & (row < height - 1)

    for s in range(slots):
        base = s * ENTRIES
        jl_s, jl_live = tbl[base + 4], tbl[base + 5]
        jh_s, jh_live = tbl[base + 6], tbl[base + 7]
        jl_mask = (zero_i + jl_live) != 0
        jh_mask = (zero_i + jh_live) != 0
        for b in range(chunks):
            cs = slice(b * LANES, (b + 1) * LANES)
            r = rho_ref[s, :, cs]
            ir = 1.0 / r
            u = vel_ref[0, s, :, cs]
            v = vel_ref[1, s, :, cs]
            kp = HEAT_RATIO * prs_ref[s, :, cs]
            bf = (r, ir, u, v, kp)
            means = []
            for arr, (src, dst, rates) in enumerate(((x_ref, xo_ref, direct_rates), (a_ref, ao_ref, adjoint_rates))):
                vals, dss, dcs, laps = [], [], [], []
                for p in range(2):
                    for n in range(NV):
                        k = p * NV + n
                        g = load(src, arr, p, n, s, k, cs)
                        lo_b = jnp.broadcast_to(gh_ref[arr, 0, s, k:k + 1, cs], shape)
                        hi_b = jnp.broadcast_to(gh_ref[arr, 1, s, k:k + 1, cs], shape)
                        im1 = jnp.where(first_row, lo_b, pltpu.roll(g, 1, 0))
                        ip1 = jnp.where(last_row, hi_b, pltpu.roll(g, height - 1, 0))
                        if b > 0:
                            left = load(src, arr, p, n, s, k, slice((b - 1) * LANES, b * LANES))
                        else:
                            left = jnp.where(jl_mask, load(src, arr, p, n, jl_s, k, slice(width - LANES, width)), 0.0)
                        if b < chunks - 1:
                            right = load(src, arr, p, n, s, k, slice((b + 1) * LANES, (b + 2) * LANES))
                        else:
                            right = jnp.where(jh_mask, load(src, arr, p, n, jh_s, k, slice(0, LANES)), 0.0)
                        jm1 = jnp.where(first_lane, pltpu.roll(left, 1, 1), pltpu.roll(g, 1, 1))
                        jp1 = jnp.where(last_lane, pltpu.roll(right, LANES - 1, 1), pltpu.roll(g, LANES - 1, 1))
                        vals.append(g)
                        dss.append((ip1 - im1) * 0.5)
                        dcs.append((jp1 - jm1) * 0.5)
                        laps.append(ip1 + im1 + jp1 + jm1 - 4.0 * g)
                X, Y = vals[:NV], vals[NV:]
                re, im = rates(bf, X, Y, dss[:NV], dcs[:NV], laps[:NV], dss[NV:], dcs[NV:], laps[NV:], w)
                total = None
                for p, rate in enumerate((re, im)):
                    for n in range(NV):
                        k = p * NV + n
                        nv = vals[k] + TIME_STEP * rate[n]
                        dst[0, p, n, s, :, cs] = nv
                        if first:
                            elo_ref[arr, 0, s, pl.ds(k, 1), cs] = nv[0:1, :]
                            ehi_ref[arr, 0, s, pl.ds(k, 1), cs] = nv[height - 1:height, :]
                        sq = nv * nv
                        total = sq if total is None else total + sq
                means.append(total / 10.0)
            term = means[0] * means[1]
            if not ghosts:
                term = jnp.where(inner, term, 0.0)
            sens_ref[s, :, cs] = sens_ref[s, :, cs] + term


def run_step(tbl, x, a, rlo, rhi, patch, density, velocity, pressure, sens_in, modes_total, first):
    modes, parts, nv, slots, height, width = x.shape
    state_block = (1, parts, nv, slots, height, width)
    edge_block = (2, 1, slots, parts * nv, width)
    state_spec = pl.BlockSpec(state_block, lambda m, t: (m, 0, 0, 0, 0, 0))
    edge_spec = pl.BlockSpec(edge_block, lambda m, t: (0, m, 0, 0, 0))
    flow_spec = pl.BlockSpec((slots, height, width), lambda m, t: (0, 0, 0))
    vel_spec = pl.BlockSpec((2, slots, height, width), lambda m, t: (0, 0, 0, 0))
    ghosts = rlo is not None
    patched = patch is not None
    in_specs = [state_spec, state_spec]
    args = [x, a]
    if ghosts:
        in_specs += [edge_spec] * 4
        args += [rlo, rhi, reverse_lanes(rlo), reverse_lanes(rhi)]
    if patched:
        in_specs += [edge_spec] * 2
        args += list(patch)
    in_specs += [flow_spec, vel_spec, flow_spec]
    args += [density, velocity, pressure]
    if not first:
        in_specs.append(flow_spec)
        args.append(sens_in)
    out_shape = [
        jax.ShapeDtypeStruct(x.shape, jnp.float32),
        jax.ShapeDtypeStruct(a.shape, jnp.float32),
        jax.ShapeDtypeStruct((slots, height, width), jnp.float32),
    ]
    out_specs = [state_spec, state_spec, flow_spec]
    if first:
        edge_shape = jax.ShapeDtypeStruct((2, modes, slots, parts * nv, width), jnp.float32)
        out_shape += [edge_shape, edge_shape]
        out_specs += [edge_spec, edge_spec]
    grid_spec = pltpu.PrefetchScalarGridSpec(
        num_scalar_prefetch=1,
        grid=(modes,),
        in_specs=in_specs,
        out_specs=out_specs,
        scratch_shapes=[
            pltpu.VMEM((2, 2, slots, parts * nv, width), jnp.float32),
        ],
    )
    kernel = functools.partial(step_kernel, modes_total=modes_total, first=first, ghosts=ghosts, patched=patched)
    return pl.pallas_call(
        kernel,
        grid_spec=grid_spec,
        out_shape=out_shape,
        compiler_params=pltpu.CompilerParams(dimension_semantics=("arbitrary",)),
    )(tbl, *args)


def ghost_term(f, r, ir, u, kp, transpose):
    if transpose:
        return [u * f[0], r * f[0] + u * f[1] + kp * f[4], u * f[2], u * f[3], f[1] * ir + u * f[4]]
    return [u * f[0] + r * f[1], u * f[1] + f[4] * ir, u * f[2], u * f[3], kp * f[1] + u * f[4]]


def fix_rows(partial0, partial7, rlo, rhi, slot_of, face_flip, density, velocity, pressure):
    _, modes, slots, rows, width = partial0.shape
    height = density.shape[1]

    def picked(recv, side):
        plain = jnp.take(recv, slot_of[:, side], axis=2)
        turned = reverse_lanes(plain)
        flag = (face_flip[:, side] != 0)[None, None, :, None, None]
        return jnp.where(flag, turned, plain)

    ghost = {0: picked(rlo, 0), height - 1: picked(rhi, 1)}
    partial = {0: partial0, height - 1: partial7}
    fixed = {}
    sens_rows = {}
    for row in (0, height - 1):
        r = density[:, row, :]
        ir = 1.0 / r
        u = velocity[0][:, row, :]
        kp = HEAT_RATIO * pressure[:, row, :]
        half = 0.5 if row == 0 else -0.5
        out = []
        for arr, sign in ((0, 1.0), (1, -1.0)):
            g = ghost[row][arr].reshape(modes, slots, 2, NV, width)
            res = []
            for p in range(2):
                f = [g[:, :, p, n, :] for n in range(NV)]
                conv = ghost_term(f, r, ir, u, kp, arr == 1)
                for n in range(NV):
                    res.append(sign * half * conv[n] + VISCOSITY * f[n])
            delta = jnp.stack(res, axis=2)
            out.append(partial[row][arr] + TIME_STEP * delta)
        fixed[row] = jnp.stack(out)
        means = jnp.sum(fixed[row] * fixed[row], axis=3) / 10.0
        sens_rows[row] = jnp.sum(means[0] * means[1], axis=0)
    return fixed[0], fixed[height - 1], sens_rows[0], sens_rows[height - 1]


def reverse_lanes(rows):
    width = rows.shape[-1]
    ri = lax.broadcasted_iota(jnp.int32, (width, width), 0)
    ci = lax.broadcasted_iota(jnp.int32, (width, width), 1)
    turn = jnp.where(ri + ci == width - 1, 1.0, 0.0).astype(jnp.float32)
    flat = rows.reshape(-1, width)
    out = jnp.dot(flat, turn, precision=lax.Precision.HIGHEST, preferred_element_type=jnp.float32)
    return out.reshape(rows.shape)


def edge_kernel(x_ref, a_ref, lo_ref, hi_ref):
    nv = x_ref.shape[2]
    height = x_ref.shape[4]
    for arr, src in enumerate((x_ref, a_ref)):
        for p in range(x_ref.shape[1]):
            for n in range(nv):
                k = p * nv + n
                for s in range(x_ref.shape[3]):
                    lo_ref[arr, 0, s, pl.ds(k, 1), :] = src[0, p, n, s, 0:1, :]
                    hi_ref[arr, 0, s, pl.ds(k, 1), :] = src[0, p, n, s, height - 1:height, :]


def edge_rows(x, a):
    modes, parts, nv, slots, height, width = x.shape
    state_spec = pl.BlockSpec((1, parts, nv, slots, height, width), lambda m: (m, 0, 0, 0, 0, 0))
    edge_spec = pl.BlockSpec((2, 1, slots, parts * nv, width), lambda m: (0, m, 0, 0, 0))
    edge_shape = jax.ShapeDtypeStruct((2, modes, slots, parts * nv, width), jnp.float32)
    return pl.pallas_call(
        edge_kernel,
        grid=(modes,),
        in_specs=[state_spec, state_spec],
        out_specs=[edge_spec, edge_spec],
        out_shape=[edge_shape, edge_shape],
    )(x, a)


def per_device(direct, adjoint, density, velocity, pressure, block_home, face_nbr, face_flip):
    modes, parts, nv, slots, height, width = direct.shape
    modes_total = modes * lax.axis_size("mode")
    live = (face_nbr >= 0).astype(jnp.int32)
    positions = jnp.take(block_home, jnp.maximum(face_nbr, 0), axis=0)
    slot_of = positions % slots
    table = jnp.stack(
        [
            slot_of[:, 0], face_flip[:, 0], slot_of[:, 1], face_flip[:, 1],
            slot_of[:, 2], live[:, 2], slot_of[:, 3], live[:, 3],
        ],
        axis=1,
    ).reshape(-1)
    mode_base = (lax.axis_index("mode") * modes).astype(jnp.int32)
    table = jnp.concatenate([table.astype(jnp.int32), mode_base[None]])

    with jax.named_scope("edge_exchange_0"):
        down, up = edge_rows(direct, adjoint)
        rlo = shifted(up, "blk", 1)
        rhi = shifted(down, "blk", -1)
    with jax.named_scope("flow_step_0"):
        q1, a1, sens, elo, ehi = run_step(
            table, direct, adjoint, None, None, None, density, velocity, pressure, None, modes_total, True
        )
    with jax.named_scope("edge_fix_0"):
        c0, c7, s0, s7 = fix_rows(elo, ehi, rlo, rhi, slot_of, face_flip, density, velocity, pressure)
        sens = sens.at[:, 0, :].add(s0).at[:, height - 1, :].add(s7)
    with jax.named_scope("edge_exchange_1"):
        rlo = shifted(c7, "blk", 1)
        rhi = shifted(c0, "blk", -1)
    with jax.named_scope("flow_step_1"):
        q2, a2, sens = run_step(
            table, q1, a1, rlo, rhi, (c0, c7), density, velocity, pressure, sens, modes_total, False
        )
    with jax.named_scope("mode_reduce"):
        count = lax.axis_size("mode")
        total = sens
        span = 1
        while span < count:
            route = [(i, i ^ span) for i in range(count)]
            total = total + lax.ppermute(total, "mode", route)
            span *= 2
        sensitivity = total / (STEPS * modes_total)
    return (q2, a2, sensitivity)


def solution(mesh):
    placed = (
        P("mode", None, None, "blk", None, None),
        P("mode", None, None, "blk", None, None),
        P("blk", None, None),
        P(None, "blk", None, None),
        P("blk", None, None),
        P(),
        P("blk", None),
        P("blk", None),
    )
    return jax.shard_map(
        per_device,
        mesh=mesh,
        in_specs=placed,
        out_specs=(
            P("mode", None, None, "blk", None, None),
            P("mode", None, None, "blk", None, None),
            P("blk", None, None),
        ),
        check_vma=False,
    )
```

```python
import functools

import jax
import jax.numpy as jnp
from jax import lax
from jax.experimental import pallas as pl
from jax.experimental.pallas import tpu as pltpu
from jax.sharding import PartitionSpec as P

STEPS = 2

HEAT_RATIO = 1.4
VISCOSITY = 0.25
TIME_STEP = 0.05
SPAN_WAVE = 0.5
BASE_FREQ = 0.2

NV = 5
ENTRIES = 8


def shifted(block, axis, distance):
    n = lax.axis_size(axis)
    route = [((i - distance) % n, i) for i in range(n)]
    return lax.ppermute(block, axis, route)


def direct_rates(bf, X, Y, dsX, dcX, lapX, dsY, dcY, lapY, w):
    r, ir, u, v, kp = bf
    b = SPAN_WAVE
    damp = SPAN_WAVE * SPAN_WAVE

    def conv(ds, dc):
        return [
            u * ds[0] + r * ds[1] + (v * dc[0] + r * dc[2]),
            u * ds[1] + ds[4] * ir + v * dc[1],
            u * ds[2] + (v * dc[2] + dc[4] * ir),
            u * ds[3] + v * dc[3],
            kp * ds[1] + u * ds[4] + (kp * dc[2] + v * dc[4]),
        ]

    def span(f):
        return [r * f[3], None, None, f[4] * ir, kp * f[3]]

    cX = conv(dsX, dcX)
    cY = conv(dsY, dcY)
    sX = span(X)
    sY = span(Y)
    re, im = [], []
    for n in range(NV):
        a = -cX[n] + VISCOSITY * (lapX[n] - damp * X[n])
        if sY[n] is not None:
            a = a + b * sY[n]
        a = a + w * Y[n]
        c = -cY[n] + VISCOSITY * (lapY[n] - damp * Y[n])
        if sX[n] is not None:
            c = c - b * sX[n]
        c = c - w * X[n]
        re.append(a)
        im.append(c)
    return re, im


def adjoint_rates(bf, X, Y, dsX, dcX, lapX, dsY, dcY, lapY, w):
    r, ir, u, v, kp = bf
    b = SPAN_WAVE
    damp = SPAN_WAVE * SPAN_WAVE

    def conv(ds, dc):
        return [
            u * ds[0] + v * dc[0],
            r * ds[0] + u * ds[1] + kp * ds[4] + v * dc[1],
            u * ds[2] + (r * dc[0] + v * dc[2] + kp * dc[4]),
            u * ds[3] + v * dc[3],
            ds[1] * ir + u * ds[4] + (dc[2] * ir + v * dc[4]),
        ]

    def span(f):
        return [None, None, None, r * f[0] + kp * f[4], f[3] * ir]

    cX = conv(dsX, dcX)
    cY = conv(dsY, dcY)
    sX = span(X)
    sY = span(Y)
    re, im = [], []
    for n in range(NV):
        a = cX[n] + VISCOSITY * (lapX[n] - damp * X[n])
        if sY[n] is not None:
            a = a - b * sY[n]
        a = a - w * Y[n]
        c = cY[n] + VISCOSITY * (lapY[n] - damp * Y[n])
        if sX[n] is not None:
            c = c + b * sX[n]
        c = c + w * X[n]
        re.append(a)
        im.append(c)
    return re, im


LANES = 128


def step_kernel(tbl, *refs, modes_total, first, ghosts, patched):
    refs = list(refs)
    x_ref, a_ref = refs[0], refs[1]
    refs = refs[2:]
    if ghosts:
        rlo_ref, rhi_ref, tlo_ref, thi_ref = refs[:4]
        refs = refs[4:]
    if patched:
        c0_ref, c7_ref = refs[:2]
        refs = refs[2:]
    rho_ref, vel_ref, prs_ref = refs[:3]
    refs = refs[3:]
    if not first:
        sin_ref = refs.pop(0)
    if first:
        xo_ref, ao_ref, sens_ref, elo_ref, ehi_ref, gh_ref = refs
    else:
        xo_ref, ao_ref, sens_ref, gh_ref = refs
    m = pl.program_id(0)
    slots = x_ref.shape[3]
    height = x_ref.shape[4]
    width = x_ref.shape[5]
    chunks = width // LANES
    shape = (height, LANES)

    @pl.when(m == 0)
    def _init():
        if first:
            sens_ref[...] = jnp.zeros(sens_ref.shape, jnp.float32)
        else:
            sens_ref[...] = sin_ref[...]

    for s in range(slots):
        for side, (tcol, fcol) in enumerate(((0, 1), (2, 3))):
            t = tbl[s * ENTRIES + tcol]
            f = tbl[s * ENTRIES + fcol]
            for arr in range(2):
                if ghosts:
                    recv_ref, turn_ref = ((rlo_ref, tlo_ref), (rhi_ref, thi_ref))[side]
                    plain = recv_ref[arr, 0, t]
                    turned = turn_ref[arr, 0, t]
                    flag = (jnp.zeros(plain.shape, jnp.int32) + f) != 0
                    gh_ref[arr, side, s] = jnp.where(flag, turned, plain)
                else:
                    gh_ref[arr, side, s] = jnp.zeros(gh_ref.shape[3:], jnp.float32)

    kf = (tbl[slots * ENTRIES] + m).astype(jnp.float32)
    w = BASE_FREQ * (jnp.zeros(shape, jnp.float32) + (kf - modes_total / 2 + 0.5))
    row = lax.broadcasted_iota(jnp.int32, shape, 0)
    lane = lax.broadcasted_iota(jnp.int32, shape, 1)
    zero_i = jnp.zeros(shape, jnp.int32)
    first_row = row == 0
    last_row = row == height - 1
    first_lane = lane == 0
    last_lane = lane == LANES - 1
    def load(src, arr, p, n, slot, k, cols):
        g = src[0, p, n, slot, :, cols]
        if patched:
            top = jnp.broadcast_to(c0_ref[arr, 0, slot, pl.ds(k, 1), cols], shape)
            bottom = jnp.broadcast_to(c7_ref[arr, 0, slot, pl.ds(k, 1), cols], shape)
            g = jnp.where(first_row, top, jnp.where(last_row, bottom, g))
        return g

    inner = (row > 0) & (row < height - 1)

    for s in range(slots):
        base = s * ENTRIES
        jl_s, jl_live = tbl[base + 4], tbl[base + 5]
        jh_s, jh_live = tbl[base + 6], tbl[base + 7]
        jl_mask = (zero_i + jl_live) != 0
        jh_mask = (zero_i + jh_live) != 0
        for b in range(chunks):
            cs = slice(b * LANES, (b + 1) * LANES)
            r = rho_ref[s, :, cs]
            ir = 1.0 / r
            u = vel_ref[0, s, :, cs]
            v = vel_ref[1, s, :, cs]
            kp = HEAT_RATIO * prs_ref[s, :, cs]
            bf = (r, ir, u, v, kp)
            means = []
            for arr, (src, dst, rates) in enumerate(((x_ref, xo_ref, direct_rates), (a_ref, ao_ref, adjoint_rates))):
                vals, dss, dcs, laps = [], [], [], []
                for p in range(2):
                    for n in range(NV):
                        k = p * NV + n
                        g = load(src, arr, p, n, s, k, cs)
                        lo_b = jnp.broadcast_to(gh_ref[arr, 0, s, k:k + 1, cs], shape)
                        hi_b = jnp.broadcast_to(gh_ref[arr, 1, s, k:k + 1, cs], shape)
                        im1 = jnp.where(first_row, lo_b, pltpu.roll(g, 1, 0))
                        ip1 = jnp.where(last_row, hi_b, pltpu.roll(g, height - 1, 0))
                        if b > 0:
                            left = load(src, arr, p, n, s, k, slice((b - 1) * LANES, b * LANES))
                        else:
                            left = jnp.where(jl_mask, load(src, arr, p, n, jl_s, k, slice(width - LANES, width)), 0.0)
                        if b < chunks - 1:
                            right = load(src, arr, p, n, s, k, slice((b + 1) * LANES, (b + 2) * LANES))
                        else:
                            right = jnp.where(jh_mask, load(src, arr, p, n, jh_s, k, slice(0, LANES)), 0.0)
                        jm1 = jnp.where(first_lane, pltpu.roll(left, 1, 1), pltpu.roll(g, 1, 1))
                        jp1 = jnp.where(last_lane, pltpu.roll(right, LANES - 1, 1), pltpu.roll(g, LANES - 1, 1))
                        vals.append(g)
                        dss.append((ip1 - im1) * 0.5)
                        dcs.append((jp1 - jm1) * 0.5)
                        laps.append(ip1 + im1 + jp1 + jm1 - 4.0 * g)
                X, Y = vals[:NV], vals[NV:]
                re, im = rates(bf, X, Y, dss[:NV], dcs[:NV], laps[:NV], dss[NV:], dcs[NV:], laps[NV:], w)
                total = None
                for p, rate in enumerate((re, im)):
                    for n in range(NV):
                        k = p * NV + n
                        nv = vals[k] + TIME_STEP * rate[n]
                        dst[0, p, n, s, :, cs] = nv
                        if first:
                            elo_ref[arr, 0, s, pl.ds(k, 1), cs] = nv[0:1, :]
                            ehi_ref[arr, 0, s, pl.ds(k, 1), cs] = nv[height - 1:height, :]
                        sq = nv * nv
                        total = sq if total is None else total + sq
                means.append(total / 10.0)
            term = means[0] * means[1]
            if not ghosts:
                term = jnp.where(inner, term, 0.0)
            sens_ref[s, :, cs] = sens_ref[s, :, cs] + term


def run_step(tbl, x, a, rlo, rhi, patch, density, velocity, pressure, sens_in, modes_total, first):
    modes, parts, nv, slots, height, width = x.shape
    state_block = (1, parts, nv, slots, height, width)
    edge_block = (2, 1, slots, parts * nv, width)
    state_spec = pl.BlockSpec(state_block, lambda m, t: (m, 0, 0, 0, 0, 0))
    edge_spec = pl.BlockSpec(edge_block, lambda m, t: (0, m, 0, 0, 0))
    flow_spec = pl.BlockSpec((slots, height, width), lambda m, t: (0, 0, 0))
    vel_spec = pl.BlockSpec((2, slots, height, width), lambda m, t: (0, 0, 0, 0))
    ghosts = rlo is not None
    patched = patch is not None
    in_specs = [state_spec, state_spec]
    args = [x, a]
    if ghosts:
        in_specs += [edge_spec] * 4
        args += [rlo, rhi, reverse_lanes(rlo), reverse_lanes(rhi)]
    if patched:
        in_specs += [edge_spec] * 2
        args += list(patch)
    in_specs += [flow_spec, vel_spec, flow_spec]
    args += [density, velocity, pressure]
    if not first:
        in_specs.append(flow_spec)
        args.append(sens_in)
    out_shape = [
        jax.ShapeDtypeStruct(x.shape, jnp.float32),
        jax.ShapeDtypeStruct(a.shape, jnp.float32),
        jax.ShapeDtypeStruct((slots, height, width), jnp.float32),
    ]
    out_specs = [state_spec, state_spec, flow_spec]
    if first:
        edge_shape = jax.ShapeDtypeStruct((2, modes, slots, parts * nv, width), jnp.float32)
        out_shape += [edge_shape, edge_shape]
        out_specs += [edge_spec, edge_spec]
    grid_spec = pltpu.PrefetchScalarGridSpec(
        num_scalar_prefetch=1,
        grid=(modes,),
        in_specs=in_specs,
        out_specs=out_specs,
        scratch_shapes=[
            pltpu.VMEM((2, 2, slots, parts * nv, width), jnp.float32),
        ],
    )
    kernel = functools.partial(step_kernel, modes_total=modes_total, first=first, ghosts=ghosts, patched=patched)
    return pl.pallas_call(
        kernel,
        grid_spec=grid_spec,
        out_shape=out_shape,
        compiler_params=pltpu.CompilerParams(dimension_semantics=("arbitrary",)),
    )(tbl, *args)


def ghost_term(f, r, ir, u, kp, transpose):
    if transpose:
        return [u * f[0], r * f[0] + u * f[1] + kp * f[4], u * f[2], u * f[3], f[1] * ir + u * f[4]]
    return [u * f[0] + r * f[1], u * f[1] + f[4] * ir, u * f[2], u * f[3], kp * f[1] + u * f[4]]


def fix_rows(partial0, partial7, rlo, rhi, slot_of, face_flip, density, velocity, pressure):
    _, modes, slots, rows, width = partial0.shape
    height = density.shape[1]

    def picked(recv, side):
        plain = jnp.take(recv, slot_of[:, side], axis=2)
        turned = reverse_lanes(plain)
        flag = (face_flip[:, side] != 0)[None, None, :, None, None]
        return jnp.where(flag, turned, plain)

    ghost = {0: picked(rlo, 0), height - 1: picked(rhi, 1)}
    partial = {0: partial0, height - 1: partial7}
    fixed = {}
    sens_rows = {}
    for row in (0, height - 1):
        r = density[:, row, :]
        ir = 1.0 / r
        u = velocity[0][:, row, :]
        kp = HEAT_RATIO * pressure[:, row, :]
        half = 0.5 if row == 0 else -0.5
        out = []
        for arr, sign in ((0, 1.0), (1, -1.0)):
            g = ghost[row][arr].reshape(modes, slots, 2, NV, width)
            res = []
            for p in range(2):
                f = [g[:, :, p, n, :] for n in range(NV)]
                conv = ghost_term(f, r, ir, u, kp, arr == 1)
                for n in range(NV):
                    res.append(sign * half * conv[n] + VISCOSITY * f[n])
            delta = jnp.stack(res, axis=2)
            out.append(partial[row][arr] + TIME_STEP * delta)
        fixed[row] = jnp.stack(out)
        means = jnp.sum(fixed[row] * fixed[row], axis=3) / 10.0
        sens_rows[row] = jnp.sum(means[0] * means[1], axis=0)
    return fixed[0], fixed[height - 1], sens_rows[0], sens_rows[height - 1]


def reverse_lanes(rows):
    width = rows.shape[-1]
    ri = lax.broadcasted_iota(jnp.int32, (width, width), 0)
    ci = lax.broadcasted_iota(jnp.int32, (width, width), 1)
    turn = jnp.where(ri + ci == width - 1, 1.0, 0.0).astype(jnp.float32)
    flat = rows.reshape(-1, width)
    out = jnp.dot(flat, turn, precision=lax.Precision.HIGHEST, preferred_element_type=jnp.float32)
    return out.reshape(rows.shape)


def edge_kernel(x_ref, a_ref, lo_ref, hi_ref):
    modes, parts, nv, slots, height, _ = x_ref.shape
    for arr, src in enumerate((x_ref, a_ref)):
        for m in range(modes):
            for p in range(parts):
                for n in range(nv):
                    k = p * nv + n
                    for s in range(slots):
                        lo_ref[arr, m, s, pl.ds(k, 1), :] = src[m, p, n, s, 0:1, :]
                        hi_ref[arr, m, s, pl.ds(k, 1), :] = src[m, p, n, s, height - 1:height, :]


def edge_rows(x, a):
    modes, parts, nv, slots, height, width = x.shape
    edge_shape = jax.ShapeDtypeStruct((2, modes, slots, parts * nv, width), jnp.float32)
    return pl.pallas_call(edge_kernel, out_shape=[edge_shape, edge_shape])(x, a)


def per_device(direct, adjoint, density, velocity, pressure, block_home, face_nbr, face_flip):
    modes, parts, nv, slots, height, width = direct.shape
    modes_total = modes * lax.axis_size("mode")
    live = (face_nbr >= 0).astype(jnp.int32)
    positions = jnp.take(block_home, jnp.maximum(face_nbr, 0), axis=0)
    slot_of = positions % slots
    table = jnp.stack(
        [
            slot_of[:, 0], face_flip[:, 0], slot_of[:, 1], face_flip[:, 1],
            slot_of[:, 2], live[:, 2], slot_of[:, 3], live[:, 3],
        ],
        axis=1,
    ).reshape(-1)
    mode_base = (lax.axis_index("mode") * modes).astype(jnp.int32)
    table = jnp.concatenate([table.astype(jnp.int32), mode_base[None]])

    with jax.named_scope("edge_exchange_0"):
        down, up = edge_rows(direct, adjoint)
        rlo = shifted(up, "blk", 1)
        rhi = shifted(down, "blk", -1)
    with jax.named_scope("flow_step_0"):
        q1, a1, sens, elo, ehi = run_step(
            table, direct, adjoint, None, None, None, density, velocity, pressure, None, modes_total, True
        )
    with jax.named_scope("edge_fix_0"):
        c0, c7, s0, s7 = fix_rows(elo, ehi, rlo, rhi, slot_of, face_flip, density, velocity, pressure)
        sens = sens.at[:, 0, :].add(s0).at[:, height - 1, :].add(s7)
    with jax.named_scope("edge_exchange_1"):
        rlo = shifted(c7, "blk", 1)
        rhi = shifted(c0, "blk", -1)
    with jax.named_scope("flow_step_1"):
        q2, a2, sens = run_step(
            table, q1, a1, rlo, rhi, (c0, c7), density, velocity, pressure, sens, modes_total, False
        )
    with jax.named_scope("mode_reduce"):
        count = lax.axis_size("mode")
        me = lax.axis_index("mode")
        stacked = jnp.stack([sens] + [shifted(sens, "mode", k) for k in range(1, count)])
        total = None
        for j in range(count):
            part = lax.dynamic_index_in_dim(stacked, (me - j) % count, axis=0, keepdims=False)
            total = part if total is None else total + part
        sensitivity = total / (STEPS * modes_total)
    return (q2, a2, sensitivity)


def solution(mesh):
    placed = (
        P("mode", None, None, "blk", None, None),
        P("mode", None, None, "blk", None, None),
        P("blk", None, None),
        P(None, "blk", None, None),
        P("blk", None, None),
        P(),
        P("blk", None),
        P("blk", None),
    )
    return jax.shard_map(
        per_device,
        mesh=mesh,
        in_specs=placed,
        out_specs=(
            P("mode", None, None, "blk", None, None),
            P("mode", None, None, "blk", None, None),
            P("blk", None, None),
        ),
        check_vma=False,
    )
```

```python
import functools

import jax
import jax.numpy as jnp
from jax import lax
from jax.experimental import pallas as pl
from jax.experimental.pallas import tpu as pltpu
from jax.sharding import PartitionSpec as P

STEPS = 2

HEAT_RATIO = 1.4
VISCOSITY = 0.25
TIME_STEP = 0.05
SPAN_WAVE = 0.5
BASE_FREQ = 0.2

NV = 5
ENTRIES = 8


def shifted(block, axis, distance):
    n = lax.axis_size(axis)
    route = [((i - distance) % n, i) for i in range(n)]
    return lax.ppermute(block, axis, route)


def direct_rates(bf, X, Y, dsX, dcX, lapX, dsY, dcY, lapY, w):
    r, ir, u, v, kp = bf
    b = SPAN_WAVE
    damp = SPAN_WAVE * SPAN_WAVE

    def conv(ds, dc):
        return [
            u * ds[0] + r * ds[1] + (v * dc[0] + r * dc[2]),
            u * ds[1] + ds[4] * ir + v * dc[1],
            u * ds[2] + (v * dc[2] + dc[4] * ir),
            u * ds[3] + v * dc[3],
            kp * ds[1] + u * ds[4] + (kp * dc[2] + v * dc[4]),
        ]

    def span(f):
        return [r * f[3], None, None, f[4] * ir, kp * f[3]]

    cX = conv(dsX, dcX)
    cY = conv(dsY, dcY)
    sX = span(X)
    sY = span(Y)
    re, im = [], []
    for n in range(NV):
        a = -cX[n] + VISCOSITY * (lapX[n] - damp * X[n])
        if sY[n] is not None:
            a = a + b * sY[n]
        a = a + w * Y[n]
        c = -cY[n] + VISCOSITY * (lapY[n] - damp * Y[n])
        if sX[n] is not None:
            c = c - b * sX[n]
        c = c - w * X[n]
        re.append(a)
        im.append(c)
    return re, im


def adjoint_rates(bf, X, Y, dsX, dcX, lapX, dsY, dcY, lapY, w):
    r, ir, u, v, kp = bf
    b = SPAN_WAVE
    damp = SPAN_WAVE * SPAN_WAVE

    def conv(ds, dc):
        return [
            u * ds[0] + v * dc[0],
            r * ds[0] + u * ds[1] + kp * ds[4] + v * dc[1],
            u * ds[2] + (r * dc[0] + v * dc[2] + kp * dc[4]),
            u * ds[3] + v * dc[3],
            ds[1] * ir + u * ds[4] + (dc[2] * ir + v * dc[4]),
        ]

    def span(f):
        return [None, None, None, r * f[0] + kp * f[4], f[3] * ir]

    cX = conv(dsX, dcX)
    cY = conv(dsY, dcY)
    sX = span(X)
    sY = span(Y)
    re, im = [], []
    for n in range(NV):
        a = cX[n] + VISCOSITY * (lapX[n] - damp * X[n])
        if sY[n] is not None:
            a = a - b * sY[n]
        a = a - w * Y[n]
        c = cY[n] + VISCOSITY * (lapY[n] - damp * Y[n])
        if sX[n] is not None:
            c = c + b * sX[n]
        c = c + w * X[n]
        re.append(a)
        im.append(c)
    return re, im


LANES = 128


def step_kernel(tbl, *refs, modes_total, first, ghosts, patched):
    refs = list(refs)
    x_ref, a_ref = refs[0], refs[1]
    refs = refs[2:]
    if ghosts:
        rlo_ref, rhi_ref, tlo_ref, thi_ref = refs[:4]
        refs = refs[4:]
    if patched:
        c0_ref, c7_ref = refs[:2]
        refs = refs[2:]
    rho_ref, vel_ref, prs_ref = refs[:3]
    refs = refs[3:]
    if not first:
        sin_ref = refs.pop(0)
    if first:
        xo_ref, ao_ref, sens_ref, elo_ref, ehi_ref, gh_ref = refs
    else:
        xo_ref, ao_ref, sens_ref, gh_ref = refs
    m = pl.program_id(0)
    slots = x_ref.shape[3]
    height = x_ref.shape[4]
    width = x_ref.shape[5]
    chunks = width // LANES
    shape = (height, LANES)

    @pl.when(m == 0)
    def _init():
        if first:
            sens_ref[...] = jnp.zeros(sens_ref.shape, jnp.float32)
        else:
            sens_ref[...] = sin_ref[...]

    for s in range(slots):
        for side, (tcol, fcol) in enumerate(((0, 1), (2, 3))):
            t = tbl[s * ENTRIES + tcol]
            f = tbl[s * ENTRIES + fcol]
            for arr in range(2):
                if ghosts:
                    recv_ref, turn_ref = ((rlo_ref, tlo_ref), (rhi_ref, thi_ref))[side]
                    plain = recv_ref[arr, 0, t]
                    turned = turn_ref[arr, 0, t]
                    flag = (jnp.zeros(plain.shape, jnp.int32) + f) != 0
                    gh_ref[arr, side, s] = jnp.where(flag, turned, plain)
                else:
                    gh_ref[arr, side, s] = jnp.zeros(gh_ref.shape[3:], jnp.float32)

    kf = (tbl[slots * ENTRIES] + m).astype(jnp.float32)
    w = BASE_FREQ * (jnp.zeros(shape, jnp.float32) + (kf - modes_total / 2 + 0.5))
    row = lax.broadcasted_iota(jnp.int32, shape, 0)
    lane = lax.broadcasted_iota(jnp.int32, shape, 1)
    zero_i = jnp.zeros(shape, jnp.int32)
    first_row = row == 0
    last_row = row == height - 1
    first_lane = lane == 0
    last_lane = lane == LANES - 1
    def load(src, arr, p, n, slot, k, cols):
        g = src[0, p, n, slot, :, cols]
        if patched:
            top = jnp.broadcast_to(c0_ref[arr, 0, slot, pl.ds(k, 1), cols], shape)
            bottom = jnp.broadcast_to(c7_ref[arr, 0, slot, pl.ds(k, 1), cols], shape)
            g = jnp.where(first_row, top, jnp.where(last_row, bottom, g))
        return g

    inner = (row > 0) & (row < height - 1)

    for s in range(slots):
        base = s * ENTRIES
        jl_s, jl_live = tbl[base + 4], tbl[base + 5]
        jh_s, jh_live = tbl[base + 6], tbl[base + 7]
        jl_mask = (zero_i + jl_live) != 0
        jh_mask = (zero_i + jh_live) != 0
        for b in range(chunks):
            cs = slice(b * LANES, (b + 1) * LANES)
            r = rho_ref[s, :, cs]
            ir = 1.0 / r
            u = vel_ref[0, s, :, cs]
            v = vel_ref[1, s, :, cs]
            kp = HEAT_RATIO * prs_ref[s, :, cs]
            bf = (r, ir, u, v, kp)
            means = []
            for arr, (src, dst, rates) in enumerate(((x_ref, xo_ref, direct_rates), (a_ref, ao_ref, adjoint_rates))):
                vals, dss, dcs, laps = [], [], [], []
                for p in range(2):
                    for n in range(NV):
                        k = p * NV + n
                        g = load(src, arr, p, n, s, k, cs)
                        lo_b = jnp.broadcast_to(gh_ref[arr, 0, s, k:k + 1, cs], shape)
                        hi_b = jnp.broadcast_to(gh_ref[arr, 1, s, k:k + 1, cs], shape)
                        im1 = jnp.where(first_row, lo_b, pltpu.roll(g, 1, 0))
                        ip1 = jnp.where(last_row, hi_b, pltpu.roll(g, height - 1, 0))
                        if b > 0:
                            left = load(src, arr, p, n, s, k, slice((b - 1) * LANES, b * LANES))
                        else:
                            left = jnp.where(jl_mask, load(src, arr, p, n, jl_s, k, slice(width - LANES, width)), 0.0)
                        if b < chunks - 1:
                            right = load(src, arr, p, n, s, k, slice((b + 1) * LANES, (b + 2) * LANES))
                        else:
                            right = jnp.where(jh_mask, load(src, arr, p, n, jh_s, k, slice(0, LANES)), 0.0)
                        jm1 = jnp.where(first_lane, pltpu.roll(left, 1, 1), pltpu.roll(g, 1, 1))
                        jp1 = jnp.where(last_lane, pltpu.roll(right, LANES - 1, 1), pltpu.roll(g, LANES - 1, 1))
                        vals.append(g)
                        dss.append((ip1 - im1) * 0.5)
                        dcs.append((jp1 - jm1) * 0.5)
                        laps.append(ip1 + im1 + jp1 + jm1 - 4.0 * g)
                X, Y = vals[:NV], vals[NV:]
                re, im = rates(bf, X, Y, dss[:NV], dcs[:NV], laps[:NV], dss[NV:], dcs[NV:], laps[NV:], w)
                total = None
                for p, rate in enumerate((re, im)):
                    for n in range(NV):
                        k = p * NV + n
                        nv = vals[k] + TIME_STEP * rate[n]
                        dst[0, p, n, s, :, cs] = nv
                        if first:
                            elo_ref[arr, 0, s, pl.ds(k, 1), cs] = nv[0:1, :]
                            ehi_ref[arr, 0, s, pl.ds(k, 1), cs] = nv[height - 1:height, :]
                        sq = nv * nv
                        total = sq if total is None else total + sq
                means.append(total / 10.0)
            term = means[0] * means[1]
            if not ghosts:
                term = jnp.where(inner, term, 0.0)
            sens_ref[s, :, cs] = sens_ref[s, :, cs] + term


def run_step(tbl, x, a, rlo, rhi, patch, density, velocity, pressure, sens_in, modes_total, first):
    modes, parts, nv, slots, height, width = x.shape
    state_block = (1, parts, nv, slots, height, width)
    edge_block = (2, 1, slots, parts * nv, width)
    state_spec = pl.BlockSpec(state_block, lambda m, t: (m, 0, 0, 0, 0, 0))
    edge_spec = pl.BlockSpec(edge_block, lambda m, t: (0, m, 0, 0, 0))
    flow_spec = pl.BlockSpec((slots, height, width), lambda m, t: (0, 0, 0))
    vel_spec = pl.BlockSpec((2, slots, height, width), lambda m, t: (0, 0, 0, 0))
    ghosts = rlo is not None
    patched = patch is not None
    in_specs = [state_spec, state_spec]
    args = [x, a]
    if ghosts:
        in_specs += [edge_spec] * 4
        args += [rlo, rhi, reverse_lanes(rlo), reverse_lanes(rhi)]
    if patched:
        in_specs += [edge_spec] * 2
        args += list(patch)
    in_specs += [flow_spec, vel_spec, flow_spec]
    args += [density, velocity, pressure]
    if not first:
        in_specs.append(flow_spec)
        args.append(sens_in)
    out_shape = [
        jax.ShapeDtypeStruct(x.shape, jnp.float32),
        jax.ShapeDtypeStruct(a.shape, jnp.float32),
        jax.ShapeDtypeStruct((slots, height, width), jnp.float32),
    ]
    out_specs = [state_spec, state_spec, flow_spec]
    if first:
        edge_shape = jax.ShapeDtypeStruct((2, modes, slots, parts * nv, width), jnp.float32)
        out_shape += [edge_shape, edge_shape]
        out_specs += [edge_spec, edge_spec]
    grid_spec = pltpu.PrefetchScalarGridSpec(
        num_scalar_prefetch=1,
        grid=(modes,),
        in_specs=in_specs,
        out_specs=out_specs,
        scratch_shapes=[
            pltpu.VMEM((2, 2, slots, parts * nv, width), jnp.float32),
        ],
    )
    kernel = functools.partial(step_kernel, modes_total=modes_total, first=first, ghosts=ghosts, patched=patched)
    return pl.pallas_call(
        kernel,
        grid_spec=grid_spec,
        out_shape=out_shape,
        compiler_params=pltpu.CompilerParams(dimension_semantics=("arbitrary",)),
    )(tbl, *args)


def ghost_term(f, r, ir, u, kp, transpose):
    if transpose:
        return [u * f[0], r * f[0] + u * f[1] + kp * f[4], u * f[2], u * f[3], f[1] * ir + u * f[4]]
    return [u * f[0] + r * f[1], u * f[1] + f[4] * ir, u * f[2], u * f[3], kp * f[1] + u * f[4]]


def fix_rows(partial0, partial7, rlo, rhi, slot_of, face_flip, density, velocity, pressure):
    _, modes, slots, rows, width = partial0.shape
    height = density.shape[1]

    def picked(recv, side):
        plain = jnp.take(recv, slot_of[:, side], axis=2)
        turned = reverse_lanes(plain)
        flag = (face_flip[:, side] != 0)[None, None, :, None, None]
        return jnp.where(flag, turned, plain)

    ghost = {0: picked(rlo, 0), height - 1: picked(rhi, 1)}
    partial = {0: partial0, height - 1: partial7}
    fixed = {}
    sens_rows = {}
    for row in (0, height - 1):
        r = density[:, row, :]
        ir = 1.0 / r
        u = velocity[0][:, row, :]
        kp = HEAT_RATIO * pressure[:, row, :]
        half = 0.5 if row == 0 else -0.5
        out = []
        for arr, sign in ((0, 1.0), (1, -1.0)):
            g = ghost[row][arr].reshape(modes, slots, 2, NV, width)
            res = []
            for p in range(2):
                f = [g[:, :, p, n, :] for n in range(NV)]
                conv = ghost_term(f, r, ir, u, kp, arr == 1)
                for n in range(NV):
                    res.append(sign * half * conv[n] + VISCOSITY * f[n])
            delta = jnp.stack(res, axis=2)
            out.append(partial[row][arr] + TIME_STEP * delta)
        fixed[row] = jnp.stack(out)
        means = jnp.sum(fixed[row] * fixed[row], axis=3) / 10.0
        sens_rows[row] = jnp.sum(means[0] * means[1], axis=0)
    return fixed[0], fixed[height - 1], sens_rows[0], sens_rows[height - 1]


def reverse_lanes(rows):
    width = rows.shape[-1]
    ri = lax.broadcasted_iota(jnp.int32, (width, width), 0)
    ci = lax.broadcasted_iota(jnp.int32, (width, width), 1)
    turn = jnp.where(ri + ci == width - 1, 1.0, 0.0).astype(jnp.float32)
    flat = rows.reshape(-1, width)
    out = jnp.dot(flat, turn, precision=lax.Precision.HIGHEST, preferred_element_type=jnp.float32)
    return out.reshape(rows.shape)


def edge_kernel(x_ref, a_ref, lo_ref, hi_ref):
    modes, parts, nv, slots, height, _ = x_ref.shape
    for arr, src in enumerate((x_ref, a_ref)):
        for m in range(modes):
            for p in range(parts):
                for n in range(nv):
                    k = p * nv + n
                    for s in range(slots):
                        lo_ref[arr, m, s, pl.ds(k, 1), :] = src[m, p, n, s, 0:1, :]
                        hi_ref[arr, m, s, pl.ds(k, 1), :] = src[m, p, n, s, height - 1:height, :]


def edge_rows(x, a):
    modes, parts, nv, slots, height, width = x.shape
    edge_shape = jax.ShapeDtypeStruct((2, modes, slots, parts * nv, width), jnp.float32)
    return pl.pallas_call(edge_kernel, out_shape=[edge_shape, edge_shape])(x, a)


def per_device(direct, adjoint, density, velocity, pressure, block_home, face_nbr, face_flip):
    modes, parts, nv, slots, height, width = direct.shape
    modes_total = modes * lax.axis_size("mode")
    live = (face_nbr >= 0).astype(jnp.int32)
    positions = jnp.take(block_home, jnp.maximum(face_nbr, 0), axis=0)
    slot_of = positions % slots
    table = jnp.stack(
        [
            slot_of[:, 0], face_flip[:, 0], slot_of[:, 1], face_flip[:, 1],
            slot_of[:, 2], live[:, 2], slot_of[:, 3], live[:, 3],
        ],
        axis=1,
    ).reshape(-1)
    mode_base = (lax.axis_index("mode") * modes).astype(jnp.int32)
    table = jnp.concatenate([table.astype(jnp.int32), mode_base[None]])

    with jax.named_scope("edge_exchange_0"):
        down, up = edge_rows(direct, adjoint)
        rlo = shifted(up, "blk", 1)
        rhi = shifted(down, "blk", -1)
    with jax.named_scope("flow_step_0"):
        q1, a1, sens, elo, ehi = run_step(
            table, direct, adjoint, None, None, None, density, velocity, pressure, None, modes_total, True
        )
    with jax.named_scope("edge_fix_0"):
        c0, c7, s0, s7 = fix_rows(elo, ehi, rlo, rhi, slot_of, face_flip, density, velocity, pressure)
        sens = sens.at[:, 0, :].add(s0).at[:, height - 1, :].add(s7)
    with jax.named_scope("edge_exchange_1"):
        rlo = shifted(c7, "blk", 1)
        rhi = shifted(c0, "blk", -1)
    with jax.named_scope("flow_step_1"):
        q2, a2, sens = run_step(
            table, q1, a1, rlo, rhi, (c0, c7), density, velocity, pressure, sens, modes_total, False
        )
    with jax.named_scope("mode_reduce"):
        count = lax.axis_size("mode")
        copies = jnp.broadcast_to(sens[None], (count,) + sens.shape)
        gathered = lax.all_to_all(copies, "mode", 0, 0)
        total = gathered[0]
        for j in range(1, count):
            total = total + gathered[j]
        sensitivity = total / (STEPS * modes_total)
    return (q2, a2, sensitivity)


def solution(mesh):
    placed = (
        P("mode", None, None, "blk", None, None),
        P("mode", None, None, "blk", None, None),
        P("blk", None, None),
        P(None, "blk", None, None),
        P("blk", None, None),
        P(),
        P("blk", None),
        P("blk", None),
    )
    return jax.shard_map(
        per_device,
        mesh=mesh,
        in_specs=placed,
        out_specs=(
            P("mode", None, None, "blk", None, None),
            P("mode", None, None, "blk", None, None),
            P("blk", None, None),
        ),
        check_vma=False,
    )
```

```python
import functools

import jax
import jax.numpy as jnp
from jax import lax
from jax.experimental import pallas as pl
from jax.experimental.pallas import tpu as pltpu
from jax.sharding import PartitionSpec as P

STEPS = 2

HEAT_RATIO = 1.4
VISCOSITY = 0.25
TIME_STEP = 0.05
SPAN_WAVE = 0.5
BASE_FREQ = 0.2

NV = 5
ENTRIES = 8


def shifted(block, axis, distance):
    n = lax.axis_size(axis)
    route = [((i - distance) % n, i) for i in range(n)]
    return lax.ppermute(block, axis, route)


def direct_rates(bf, X, Y, dsX, dcX, lapX, dsY, dcY, lapY, w):
    r, ir, u, v, kp = bf
    b = SPAN_WAVE
    damp = SPAN_WAVE * SPAN_WAVE

    def conv(ds, dc):
        return [
            u * ds[0] + r * ds[1] + (v * dc[0] + r * dc[2]),
            u * ds[1] + ds[4] * ir + v * dc[1],
            u * ds[2] + (v * dc[2] + dc[4] * ir),
            u * ds[3] + v * dc[3],
            kp * ds[1] + u * ds[4] + (kp * dc[2] + v * dc[4]),
        ]

    def span(f):
        return [r * f[3], None, None, f[4] * ir, kp * f[3]]

    cX = conv(dsX, dcX)
    cY = conv(dsY, dcY)
    sX = span(X)
    sY = span(Y)
    re, im = [], []
    for n in range(NV):
        a = -cX[n] + VISCOSITY * (lapX[n] - damp * X[n])
        if sY[n] is not None:
            a = a + b * sY[n]
        a = a + w * Y[n]
        c = -cY[n] + VISCOSITY * (lapY[n] - damp * Y[n])
        if sX[n] is not None:
            c = c - b * sX[n]
        c = c - w * X[n]
        re.append(a)
        im.append(c)
    return re, im


def adjoint_rates(bf, X, Y, dsX, dcX, lapX, dsY, dcY, lapY, w):
    r, ir, u, v, kp = bf
    b = SPAN_WAVE
    damp = SPAN_WAVE * SPAN_WAVE

    def conv(ds, dc):
        return [
            u * ds[0] + v * dc[0],
            r * ds[0] + u * ds[1] + kp * ds[4] + v * dc[1],
            u * ds[2] + (r * dc[0] + v * dc[2] + kp * dc[4]),
            u * ds[3] + v * dc[3],
            ds[1] * ir + u * ds[4] + (dc[2] * ir + v * dc[4]),
        ]

    def span(f):
        return [None, None, None, r * f[0] + kp * f[4], f[3] * ir]

    cX = conv(dsX, dcX)
    cY = conv(dsY, dcY)
    sX = span(X)
    sY = span(Y)
    re, im = [], []
    for n in range(NV):
        a = cX[n] + VISCOSITY * (lapX[n] - damp * X[n])
        if sY[n] is not None:
            a = a - b * sY[n]
        a = a - w * Y[n]
        c = cY[n] + VISCOSITY * (lapY[n] - damp * Y[n])
        if sX[n] is not None:
            c = c + b * sX[n]
        c = c + w * X[n]
        re.append(a)
        im.append(c)
    return re, im


LANES = 128


def pick_rows(ref, arr, slot, slots):
    rows = NV * 2
    out = ref[0, pl.ds(arr * slots * rows, rows), :]
    for other in range(1, slots):
        cand = ref[0, pl.ds((arr * slots + other) * rows, rows), :]
        out = jnp.where((jnp.zeros(out.shape, jnp.int32) + slot) == other, cand, out)
    return out


def step_kernel(tbl, *refs, modes_total, first, ghosts, patched):
    refs = list(refs)
    x_ref, a_ref = refs[0], refs[1]
    refs = refs[2:]
    if ghosts:
        rlo_ref, rhi_ref, tlo_ref, thi_ref = refs[:4]
        refs = refs[4:]
    if patched:
        c0_ref, c7_ref = refs[:2]
        refs = refs[2:]
    rho_ref, vel_ref, prs_ref = refs[:3]
    refs = refs[3:]
    if not first:
        sin_ref = refs.pop(0)
    if first:
        xo_ref, ao_ref, sens_ref, elo_ref, ehi_ref, gh_ref = refs
    else:
        xo_ref, ao_ref, sens_ref, gh_ref = refs
    m = pl.program_id(0)
    slots = x_ref.shape[3]
    height = x_ref.shape[4]
    width = x_ref.shape[5]
    chunks = width // LANES
    shape = (height, LANES)

    @pl.when(m == 0)
    def _init():
        if first:
            sens_ref[...] = jnp.zeros(sens_ref.shape, jnp.float32)
        else:
            sens_ref[...] = sin_ref[...]

    for s in range(slots):
        for side, (tcol, fcol) in enumerate(((0, 1), (2, 3))):
            t = tbl[s * ENTRIES + tcol]
            f = tbl[s * ENTRIES + fcol]
            for arr in range(2):
                if ghosts:
                    recv_ref, turn_ref = ((rlo_ref, tlo_ref), (rhi_ref, thi_ref))[side]
                    plain = pick_rows(recv_ref, arr, t, slots)
                    turned = pick_rows(turn_ref, arr, t, slots)
                    flag = (jnp.zeros(plain.shape, jnp.int32) + f) != 0
                    gh_ref[arr, side, s] = jnp.where(flag, turned, plain)
                else:
                    gh_ref[arr, side, s] = jnp.zeros(gh_ref.shape[3:], jnp.float32)

    kf = (tbl[slots * ENTRIES] + m).astype(jnp.float32)
    w = BASE_FREQ * (jnp.zeros(shape, jnp.float32) + (kf - modes_total / 2 + 0.5))
    row = lax.broadcasted_iota(jnp.int32, shape, 0)
    lane = lax.broadcasted_iota(jnp.int32, shape, 1)
    zero_i = jnp.zeros(shape, jnp.int32)
    first_row = row == 0
    last_row = row == height - 1
    first_lane = lane == 0
    last_lane = lane == LANES - 1
    def edge_row(ref, arr, slot, k, cols):
        if isinstance(slot, int):
            return ref[0, pl.ds((arr * slots + slot) * 2 * NV + k, 1), cols]
        out = ref[0, pl.ds(arr * slots * 2 * NV + k, 1), cols]
        for other in range(1, slots):
            cand = ref[0, pl.ds((arr * slots + other) * 2 * NV + k, 1), cols]
            out = jnp.where((jnp.zeros(out.shape, jnp.int32) + slot) == other, cand, out)
        return out

    def load(src, arr, p, n, slot, k, cols):
        g = src[0, p, n, slot, :, cols]
        if patched:
            top = jnp.broadcast_to(edge_row(c0_ref, arr, slot, k, cols), shape)
            bottom = jnp.broadcast_to(edge_row(c7_ref, arr, slot, k, cols), shape)
            g = jnp.where(first_row, top, jnp.where(last_row, bottom, g))
        return g

    inner = (row > 0) & (row < height - 1)

    for s in range(slots):
        base = s * ENTRIES
        jl_s, jl_live = tbl[base + 4], tbl[base + 5]
        jh_s, jh_live = tbl[base + 6], tbl[base + 7]
        jl_mask = (zero_i + jl_live) != 0
        jh_mask = (zero_i + jh_live) != 0
        for b in range(chunks):
            cs = slice(b * LANES, (b + 1) * LANES)
            r = rho_ref[s, :, cs]
            ir = 1.0 / r
            u = vel_ref[0, s, :, cs]
            v = vel_ref[1, s, :, cs]
            kp = HEAT_RATIO * prs_ref[s, :, cs]
            bf = (r, ir, u, v, kp)
            means = []
            for arr, (src, dst, rates) in enumerate(((x_ref, xo_ref, direct_rates), (a_ref, ao_ref, adjoint_rates))):
                vals, dss, dcs, laps = [], [], [], []
                for p in range(2):
                    for n in range(NV):
                        k = p * NV + n
                        g = load(src, arr, p, n, s, k, cs)
                        lo_b = jnp.broadcast_to(gh_ref[arr, 0, s, k:k + 1, cs], shape)
                        hi_b = jnp.broadcast_to(gh_ref[arr, 1, s, k:k + 1, cs], shape)
                        im1 = jnp.where(first_row, lo_b, pltpu.roll(g, 1, 0))
                        ip1 = jnp.where(last_row, hi_b, pltpu.roll(g, height - 1, 0))
                        if b > 0:
                            left = load(src, arr, p, n, s, k, slice((b - 1) * LANES, b * LANES))
                        else:
                            left = jnp.where(jl_mask, load(src, arr, p, n, jl_s, k, slice(width - LANES, width)), 0.0)
                        if b < chunks - 1:
                            right = load(src, arr, p, n, s, k, slice((b + 1) * LANES, (b + 2) * LANES))
                        else:
                            right = jnp.where(jh_mask, load(src, arr, p, n, jh_s, k, slice(0, LANES)), 0.0)
                        jm1 = jnp.where(first_lane, pltpu.roll(left, 1, 1), pltpu.roll(g, 1, 1))
                        jp1 = jnp.where(last_lane, pltpu.roll(right, LANES - 1, 1), pltpu.roll(g, LANES - 1, 1))
                        vals.append(g)
                        dss.append((ip1 - im1) * 0.5)
                        dcs.append((jp1 - jm1) * 0.5)
                        laps.append(ip1 + im1 + jp1 + jm1 - 4.0 * g)
                X, Y = vals[:NV], vals[NV:]
                re, im = rates(bf, X, Y, dss[:NV], dcs[:NV], laps[:NV], dss[NV:], dcs[NV:], laps[NV:], w)
                total = None
                for p, rate in enumerate((re, im)):
                    for n in range(NV):
                        k = p * NV + n
                        nv = vals[k] + TIME_STEP * rate[n]
                        dst[0, p, n, s, :, cs] = nv
                        if first:
                            at = (arr * slots + s) * 2 * NV + k
                            elo_ref[0, pl.ds(at, 1), cs] = nv[0:1, :]
                            ehi_ref[0, pl.ds(at, 1), cs] = nv[height - 1:height, :]
                        sq = nv * nv
                        total = sq if total is None else total + sq
                means.append(total / 10.0)
            term = means[0] * means[1]
            if not ghosts:
                term = jnp.where(inner, term, 0.0)
            sens_ref[s, :, cs] = sens_ref[s, :, cs] + term


def run_step(tbl, x, a, rlo, rhi, patch, density, velocity, pressure, sens_in, modes_total, first):
    modes, parts, nv, slots, height, width = x.shape
    state_block = (1, parts, nv, slots, height, width)
    edge_block = (1, 2 * slots * parts * nv, width)
    state_spec = pl.BlockSpec(state_block, lambda m, t: (m, 0, 0, 0, 0, 0))
    edge_spec = pl.BlockSpec(edge_block, lambda m, t: (m, 0, 0))
    flow_spec = pl.BlockSpec((slots, height, width), lambda m, t: (0, 0, 0))
    vel_spec = pl.BlockSpec((2, slots, height, width), lambda m, t: (0, 0, 0, 0))
    ghosts = rlo is not None
    patched = patch is not None
    in_specs = [state_spec, state_spec]
    args = [x, a]
    if ghosts:
        in_specs += [edge_spec] * 4
        args += [rlo, rhi, reverse_lanes(rlo), reverse_lanes(rhi)]
    if patched:
        in_specs += [edge_spec] * 2
        args += list(patch)
    in_specs += [flow_spec, vel_spec, flow_spec]
    args += [density, velocity, pressure]
    if not first:
        in_specs.append(flow_spec)
        args.append(sens_in)
    out_shape = [
        jax.ShapeDtypeStruct(x.shape, jnp.float32),
        jax.ShapeDtypeStruct(a.shape, jnp.float32),
        jax.ShapeDtypeStruct((slots, height, width), jnp.float32),
    ]
    out_specs = [state_spec, state_spec, flow_spec]
    if first:
        edge_shape = jax.ShapeDtypeStruct((modes, 2 * slots * parts * nv, width), jnp.float32)
        out_shape += [edge_shape, edge_shape]
        out_specs += [edge_spec, edge_spec]
    grid_spec = pltpu.PrefetchScalarGridSpec(
        num_scalar_prefetch=1,
        grid=(modes,),
        in_specs=in_specs,
        out_specs=out_specs,
        scratch_shapes=[
            pltpu.VMEM((2, 2, slots, parts * nv, width), jnp.float32),
        ],
    )
    kernel = functools.partial(step_kernel, modes_total=modes_total, first=first, ghosts=ghosts, patched=patched)
    return pl.pallas_call(
        kernel,
        grid_spec=grid_spec,
        out_shape=out_shape,
        compiler_params=pltpu.CompilerParams(dimension_semantics=("arbitrary",)),
    )(tbl, *args)


def ghost_term(f, r, ir, u, kp, transpose):
    if transpose:
        return [u * f[0], r * f[0] + u * f[1] + kp * f[4], u * f[2], u * f[3], f[1] * ir + u * f[4]]
    return [u * f[0] + r * f[1], u * f[1] + f[4] * ir, u * f[2], u * f[3], kp * f[1] + u * f[4]]


def unflat(e, slots):
    modes, _, width = e.shape
    return jnp.transpose(e.reshape(modes, 2, slots, 2 * NV, width), (1, 0, 2, 3, 4))


def flat(e):
    _, modes, slots, rows, width = e.shape
    return jnp.transpose(e, (1, 0, 2, 3, 4)).reshape(modes, 2 * slots * rows, width)


def fix_rows(partial0, partial7, rlo, rhi, slot_of, face_flip, density, velocity, pressure):
    slots = density.shape[0]
    partial0, partial7, rlo, rhi = (unflat(e, slots) for e in (partial0, partial7, rlo, rhi))
    _, modes, slots, rows, width = partial0.shape
    height = density.shape[1]

    def picked(recv, side):
        plain = jnp.take(recv, slot_of[:, side], axis=2)
        turned = reverse_lanes(plain)
        flag = (face_flip[:, side] != 0)[None, None, :, None, None]
        return jnp.where(flag, turned, plain)

    ghost = {0: picked(rlo, 0), height - 1: picked(rhi, 1)}
    partial = {0: partial0, height - 1: partial7}
    fixed = {}
    sens_rows = {}
    for row in (0, height - 1):
        r = density[:, row, :]
        ir = 1.0 / r
        u = velocity[0][:, row, :]
        kp = HEAT_RATIO * pressure[:, row, :]
        half = 0.5 if row == 0 else -0.5
        out = []
        for arr, sign in ((0, 1.0), (1, -1.0)):
            g = ghost[row][arr].reshape(modes, slots, 2, NV, width)
            res = []
            for p in range(2):
                f = [g[:, :, p, n, :] for n in range(NV)]
                conv = ghost_term(f, r, ir, u, kp, arr == 1)
                for n in range(NV):
                    res.append(sign * half * conv[n] + VISCOSITY * f[n])
            delta = jnp.stack(res, axis=2)
            out.append(partial[row][arr] + TIME_STEP * delta)
        fixed[row] = jnp.stack(out)
        means = jnp.sum(fixed[row] * fixed[row], axis=3) / 10.0
        sens_rows[row] = jnp.sum(means[0] * means[1], axis=0)
    return flat(fixed[0]), flat(fixed[height - 1]), sens_rows[0], sens_rows[height - 1]


def reverse_lanes(rows):
    width = rows.shape[-1]
    ri = lax.broadcasted_iota(jnp.int32, (width, width), 0)
    ci = lax.broadcasted_iota(jnp.int32, (width, width), 1)
    turn = jnp.where(ri + ci == width - 1, 1.0, 0.0).astype(jnp.float32)
    flat = rows.reshape(-1, width)
    out = jnp.dot(flat, turn, precision=lax.Precision.HIGHEST, preferred_element_type=jnp.float32)
    return out.reshape(rows.shape)


def edge_kernel(x_ref, a_ref, lo_ref, hi_ref):
    modes, parts, nv, slots, height, _ = x_ref.shape
    for arr, src in enumerate((x_ref, a_ref)):
        for m in range(modes):
            for p in range(parts):
                for n in range(nv):
                    k = p * nv + n
                    for s in range(slots):
                        at = (arr * slots + s) * parts * nv + k
                        lo_ref[m, pl.ds(at, 1), :] = src[m, p, n, s, 0:1, :]
                        hi_ref[m, pl.ds(at, 1), :] = src[m, p, n, s, height - 1:height, :]


def edge_rows(x, a):
    modes, parts, nv, slots, height, width = x.shape
    edge_shape = jax.ShapeDtypeStruct((modes, 2 * slots * parts * nv, width), jnp.float32)
    return pl.pallas_call(edge_kernel, out_shape=[edge_shape, edge_shape])(x, a)


def per_device(direct, adjoint, density, velocity, pressure, block_home, face_nbr, face_flip):
    modes, parts, nv, slots, height, width = direct.shape
    modes_total = modes * lax.axis_size("mode")
    live = (face_nbr >= 0).astype(jnp.int32)
    positions = jnp.take(block_home, jnp.maximum(face_nbr, 0), axis=0)
    slot_of = positions % slots
    table = jnp.stack(
        [
            slot_of[:, 0], face_flip[:, 0], slot_of[:, 1], face_flip[:, 1],
            slot_of[:, 2], live[:, 2], slot_of[:, 3], live[:, 3],
        ],
        axis=1,
    ).reshape(-1)
    mode_base = (lax.axis_index("mode") * modes).astype(jnp.int32)
    table = jnp.concatenate([table.astype(jnp.int32), mode_base[None]])

    with jax.named_scope("edge_exchange_0"):
        down, up = edge_rows(direct, adjoint)
        rlo = shifted(up, "blk", 1)
        rhi = shifted(down, "blk", -1)
    with jax.named_scope("flow_step_0"):
        q1, a1, sens, elo, ehi = run_step(
            table, direct, adjoint, None, None, None, density, velocity, pressure, None, modes_total, True
        )
    with jax.named_scope("edge_fix_0"):
        c0, c7, s0, s7 = fix_rows(elo, ehi, rlo, rhi, slot_of, face_flip, density, velocity, pressure)
        sens = sens.at[:, 0, :].add(s0).at[:, height - 1, :].add(s7)
    with jax.named_scope("edge_exchange_1"):
        rlo = shifted(c7, "blk", 1)
        rhi = shifted(c0, "blk", -1)
    with jax.named_scope("flow_step_1"):
        q2, a2, sens = run_step(
            table, q1, a1, rlo, rhi, (c0, c7), density, velocity, pressure, sens, modes_total, False
        )
    with jax.named_scope("mode_reduce"):
        count = lax.axis_size("mode")
        me = lax.axis_index("mode")
        stacked = jnp.stack([sens] + [shifted(sens, "mode", k) for k in range(1, count)])
        total = None
        for j in range(count):
            part = lax.dynamic_index_in_dim(stacked, (me - j) % count, axis=0, keepdims=False)
            total = part if total is None else total + part
        sensitivity = total / (STEPS * modes_total)
    return (q2, a2, sensitivity)


def solution(mesh):
    placed = (
        P("mode", None, None, "blk", None, None),
        P("mode", None, None, "blk", None, None),
        P("blk", None, None),
        P(None, "blk", None, None),
        P("blk", None, None),
        P(),
        P("blk", None),
        P("blk", None),
    )
    return jax.shard_map(
        per_device,
        mesh=mesh,
        in_specs=placed,
        out_specs=(
            P("mode", None, None, "blk", None, None),
            P("mode", None, None, "blk", None, None),
            P("blk", None, None),
        ),
        check_vma=False,
    )
```

```python
import functools

import jax
import jax.numpy as jnp
from jax import lax
from jax.experimental import pallas as pl
from jax.experimental.pallas import tpu as pltpu
from jax.sharding import PartitionSpec as P

STEPS = 2

HEAT_RATIO = 1.4
VISCOSITY = 0.25
TIME_STEP = 0.05
SPAN_WAVE = 0.5
BASE_FREQ = 0.2

NV = 5
ENTRIES = 8


def shifted(block, axis, distance):
    n = lax.axis_size(axis)
    route = [((i - distance) % n, i) for i in range(n)]
    return lax.ppermute(block, axis, route)


def direct_rates(bf, X, Y, dsX, dcX, lapX, dsY, dcY, lapY, w):
    r, ir, u, v, kp = bf
    b = SPAN_WAVE
    damp = SPAN_WAVE * SPAN_WAVE

    def conv(ds, dc):
        return [
            u * ds[0] + r * ds[1] + (v * dc[0] + r * dc[2]),
            u * ds[1] + ds[4] * ir + v * dc[1],
            u * ds[2] + (v * dc[2] + dc[4] * ir),
            u * ds[3] + v * dc[3],
            kp * ds[1] + u * ds[4] + (kp * dc[2] + v * dc[4]),
        ]

    def span(f):
        return [r * f[3], None, None, f[4] * ir, kp * f[3]]

    cX = conv(dsX, dcX)
    cY = conv(dsY, dcY)
    sX = span(X)
    sY = span(Y)
    re, im = [], []
    for n in range(NV):
        a = -cX[n] + VISCOSITY * (lapX[n] - damp * X[n])
        if sY[n] is not None:
            a = a + b * sY[n]
        a = a + w * Y[n]
        c = -cY[n] + VISCOSITY * (lapY[n] - damp * Y[n])
        if sX[n] is not None:
            c = c - b * sX[n]
        c = c - w * X[n]
        re.append(a)
        im.append(c)
    return re, im


def adjoint_rates(bf, X, Y, dsX, dcX, lapX, dsY, dcY, lapY, w):
    r, ir, u, v, kp = bf
    b = SPAN_WAVE
    damp = SPAN_WAVE * SPAN_WAVE

    def conv(ds, dc):
        return [
            u * ds[0] + v * dc[0],
            r * ds[0] + u * ds[1] + kp * ds[4] + v * dc[1],
            u * ds[2] + (r * dc[0] + v * dc[2] + kp * dc[4]),
            u * ds[3] + v * dc[3],
            ds[1] * ir + u * ds[4] + (dc[2] * ir + v * dc[4]),
        ]

    def span(f):
        return [None, None, None, r * f[0] + kp * f[4], f[3] * ir]

    cX = conv(dsX, dcX)
    cY = conv(dsY, dcY)
    sX = span(X)
    sY = span(Y)
    re, im = [], []
    for n in range(NV):
        a = cX[n] + VISCOSITY * (lapX[n] - damp * X[n])
        if sY[n] is not None:
            a = a - b * sY[n]
        a = a - w * Y[n]
        c = cY[n] + VISCOSITY * (lapY[n] - damp * Y[n])
        if sX[n] is not None:
            c = c + b * sX[n]
        c = c + w * X[n]
        re.append(a)
        im.append(c)
    return re, im


LANES = 128


def pick_rows(ref, arr, slot, slots):
    rows = NV * 2
    out = ref[0, pl.ds(arr * slots * rows, rows), :]
    for other in range(1, slots):
        cand = ref[0, pl.ds((arr * slots + other) * rows, rows), :]
        out = jnp.where((jnp.zeros(out.shape, jnp.int32) + slot) == other, cand, out)
    return out


def step_kernel(tbl, *refs, modes_total, first, ghosts, patched):
    refs = list(refs)
    x_ref, a_ref = refs[0], refs[1]
    refs = refs[2:]
    if ghosts:
        rlo_ref, rhi_ref, tlo_ref, thi_ref = refs[:4]
        refs = refs[4:]
    if patched:
        c0_ref, c7_ref = refs[:2]
        refs = refs[2:]
    rho_ref, vel_ref, prs_ref = refs[:3]
    refs = refs[3:]
    if not first:
        sin_ref = refs.pop(0)
    if first:
        xo_ref, ao_ref, sens_ref, elo_ref, ehi_ref, gh_ref = refs
    else:
        xo_ref, ao_ref, sens_ref, gh_ref = refs
    m = pl.program_id(0)
    slots = x_ref.shape[3]
    height = x_ref.shape[4]
    width = x_ref.shape[5]
    chunks = width // LANES
    shape = (height, LANES)

    @pl.when(m == 0)
    def _init():
        if first:
            sens_ref[...] = jnp.zeros(sens_ref.shape, jnp.float32)
        else:
            sens_ref[...] = sin_ref[...]

    for s in range(slots):
        for side, (tcol, fcol) in enumerate(((0, 1), (2, 3))):
            t = tbl[s * ENTRIES + tcol]
            f = tbl[s * ENTRIES + fcol]
            for arr in range(2):
                if ghosts:
                    recv_ref, turn_ref = ((rlo_ref, tlo_ref), (rhi_ref, thi_ref))[side]
                    plain = pick_rows(recv_ref, arr, t, slots)
                    turned = pick_rows(turn_ref, arr, t, slots)
                    flag = (jnp.zeros(plain.shape, jnp.int32) + f) != 0
                    gh_ref[arr, side, s] = jnp.where(flag, turned, plain)
                else:
                    gh_ref[arr, side, s] = jnp.zeros(gh_ref.shape[3:], jnp.float32)

    kf = (tbl[slots * ENTRIES] + m).astype(jnp.float32)
    w = BASE_FREQ * (jnp.zeros(shape, jnp.float32) + (kf - modes_total / 2 + 0.5))
    row = lax.broadcasted_iota(jnp.int32, shape, 0)
    lane = lax.broadcasted_iota(jnp.int32, shape, 1)
    zero_i = jnp.zeros(shape, jnp.int32)
    first_row = row == 0
    last_row = row == height - 1
    first_lane = lane == 0
    last_lane = lane == LANES - 1
    def edge_row(ref, arr, slot, k, cols):
        if isinstance(slot, int):
            return ref[0, pl.ds((arr * slots + slot) * 2 * NV + k, 1), cols]
        out = ref[0, pl.ds(arr * slots * 2 * NV + k, 1), cols]
        for other in range(1, slots):
            cand = ref[0, pl.ds((arr * slots + other) * 2 * NV + k, 1), cols]
            out = jnp.where((jnp.zeros(out.shape, jnp.int32) + slot) == other, cand, out)
        return out

    def load(src, arr, p, n, slot, k, cols):
        g = src[0, p, n, slot, :, cols]
        if patched:
            top = jnp.broadcast_to(edge_row(c0_ref, arr, slot, k, cols), shape)
            bottom = jnp.broadcast_to(edge_row(c7_ref, arr, slot, k, cols), shape)
            g = jnp.where(first_row, top, jnp.where(last_row, bottom, g))
        return g

    inner = (row > 0) & (row < height - 1)

    for s in range(slots):
        base = s * ENTRIES
        jl_s, jl_live = tbl[base + 4], tbl[base + 5]
        jh_s, jh_live = tbl[base + 6], tbl[base + 7]
        jl_mask = (zero_i + jl_live) != 0
        jh_mask = (zero_i + jh_live) != 0
        for b in range(chunks):
            cs = slice(b * LANES, (b + 1) * LANES)
            r = rho_ref[s, :, cs]
            ir = 1.0 / r
            u = vel_ref[0, s, :, cs]
            v = vel_ref[1, s, :, cs]
            kp = HEAT_RATIO * prs_ref[s, :, cs]
            bf = (r, ir, u, v, kp)
            means = []
            for arr, (src, dst, rates) in enumerate(((x_ref, xo_ref, direct_rates), (a_ref, ao_ref, adjoint_rates))):
                vals, dss, dcs, laps = [], [], [], []
                for p in range(2):
                    for n in range(NV):
                        k = p * NV + n
                        g = load(src, arr, p, n, s, k, cs)
                        lo_b = jnp.broadcast_to(gh_ref[arr, 0, s, k:k + 1, cs], shape)
                        hi_b = jnp.broadcast_to(gh_ref[arr, 1, s, k:k + 1, cs], shape)
                        im1 = jnp.where(first_row, lo_b, pltpu.roll(g, 1, 0))
                        ip1 = jnp.where(last_row, hi_b, pltpu.roll(g, height - 1, 0))
                        if b > 0:
                            left = load(src, arr, p, n, s, k, slice((b - 1) * LANES, b * LANES))
                        else:
                            left = jnp.where(jl_mask, load(src, arr, p, n, jl_s, k, slice(width - LANES, width)), 0.0)
                        if b < chunks - 1:
                            right = load(src, arr, p, n, s, k, slice((b + 1) * LANES, (b + 2) * LANES))
                        else:
                            right = jnp.where(jh_mask, load(src, arr, p, n, jh_s, k, slice(0, LANES)), 0.0)
                        jm1 = jnp.where(first_lane, pltpu.roll(left, 1, 1), pltpu.roll(g, 1, 1))
                        jp1 = jnp.where(last_lane, pltpu.roll(right, LANES - 1, 1), pltpu.roll(g, LANES - 1, 1))
                        vals.append(g)
                        dss.append((ip1 - im1) * 0.5)
                        dcs.append((jp1 - jm1) * 0.5)
                        laps.append(ip1 + im1 + jp1 + jm1 - 4.0 * g)
                X, Y = vals[:NV], vals[NV:]
                re, im = rates(bf, X, Y, dss[:NV], dcs[:NV], laps[:NV], dss[NV:], dcs[NV:], laps[NV:], w)
                total = None
                for p, rate in enumerate((re, im)):
                    for n in range(NV):
                        k = p * NV + n
                        nv = vals[k] + TIME_STEP * rate[n]
                        dst[0, p, n, s, :, cs] = nv
                        if first:
                            at = (arr * slots + s) * 2 * NV + k
                            elo_ref[0, pl.ds(at, 1), cs] = nv[0:1, :]
                            ehi_ref[0, pl.ds(at, 1), cs] = nv[height - 1:height, :]
                        sq = nv * nv
                        total = sq if total is None else total + sq
                means.append(total / 10.0)
            term = means[0] * means[1]
            if not ghosts:
                term = jnp.where(inner, term, 0.0)
            sens_ref[s, :, cs] = sens_ref[s, :, cs] + term


def run_step(tbl, x, a, rlo, rhi, patch, density, velocity, pressure, sens_in, modes_total, first):
    modes, parts, nv, slots, height, width = x.shape
    state_block = (1, parts, nv, slots, height, width)
    edge_block = (1, 2 * slots * parts * nv, width)
    state_spec = pl.BlockSpec(state_block, lambda m, t: (m, 0, 0, 0, 0, 0))
    edge_spec = pl.BlockSpec(edge_block, lambda m, t: (m, 0, 0))
    flow_spec = pl.BlockSpec((slots, height, width), lambda m, t: (0, 0, 0))
    vel_spec = pl.BlockSpec((2, slots, height, width), lambda m, t: (0, 0, 0, 0))
    ghosts = rlo is not None
    patched = patch is not None
    in_specs = [state_spec, state_spec]
    args = [x, a]
    if ghosts:
        in_specs += [edge_spec] * 4
        args += [rlo, rhi, reverse_lanes(rlo), reverse_lanes(rhi)]
    if patched:
        in_specs += [edge_spec] * 2
        args += list(patch)
    in_specs += [flow_spec, vel_spec, flow_spec]
    args += [density, velocity, pressure]
    if not first:
        in_specs.append(flow_spec)
        args.append(sens_in)
    out_shape = [
        jax.ShapeDtypeStruct(x.shape, jnp.float32),
        jax.ShapeDtypeStruct(a.shape, jnp.float32),
        jax.ShapeDtypeStruct((slots, height, width), jnp.float32),
    ]
    out_specs = [state_spec, state_spec, flow_spec]
    if first:
        edge_shape = jax.ShapeDtypeStruct((modes, 2 * slots * parts * nv, width), jnp.float32)
        out_shape += [edge_shape, edge_shape]
        out_specs += [edge_spec, edge_spec]
    grid_spec = pltpu.PrefetchScalarGridSpec(
        num_scalar_prefetch=1,
        grid=(modes,),
        in_specs=in_specs,
        out_specs=out_specs,
        scratch_shapes=[
            pltpu.VMEM((2, 2, slots, parts * nv, width), jnp.float32),
        ],
    )
    kernel = functools.partial(step_kernel, modes_total=modes_total, first=first, ghosts=ghosts, patched=patched)
    return pl.pallas_call(
        kernel,
        grid_spec=grid_spec,
        out_shape=out_shape,
        compiler_params=pltpu.CompilerParams(dimension_semantics=("arbitrary",)),
    )(tbl, *args)


def ghost_term(f, r, ir, u, kp, transpose):
    if transpose:
        return [u * f[0], r * f[0] + u * f[1] + kp * f[4], u * f[2], u * f[3], f[1] * ir + u * f[4]]
    return [u * f[0] + r * f[1], u * f[1] + f[4] * ir, u * f[2], u * f[3], kp * f[1] + u * f[4]]


def fix_rows(partial0, partial7, rlo, rhi, slot_of, face_flip, density, velocity, pressure):
    slots, height, width = density.shape
    rows = 2 * NV
    received = {0: (rlo, reverse_lanes(rlo)), height - 1: (rhi, reverse_lanes(rhi))}
    partial = {0: partial0, height - 1: partial7}
    fixed, sens_rows = {}, {}
    for side, row in enumerate((0, height - 1)):
        plain_all, turned_all = received[row]
        r_all = density[:, row, :]
        u_all = velocity[0][:, row, :]
        kp_all = HEAT_RATIO * pressure[:, row, :]
        half = 0.5 if row == 0 else -0.5
        pieces, means = [], {}
        for arr, sign in ((0, 1.0), (1, -1.0)):
            for s in range(slots):
                t = slot_of[s, side]

                def rows_of(block, slot):
                    return block[:, (arr * slots + slot) * rows:(arr * slots + slot + 1) * rows, :]

                plain, turned = rows_of(plain_all, 0), rows_of(turned_all, 0)
                for other in range(1, slots):
                    plain = jnp.where(t == other, rows_of(plain_all, other), plain)
                    turned = jnp.where(t == other, rows_of(turned_all, other), turned)
                g = jnp.where(face_flip[s, side] != 0, turned, plain)
                r = r_all[s]
                ir = 1.0 / r
                u = u_all[s]
                kp = kp_all[s]
                res = []
                for p in range(2):
                    f = [g[:, p * NV + n, :] for n in range(NV)]
                    conv = ghost_term(f, r, ir, u, kp, arr == 1)
                    for n in range(NV):
                        res.append(sign * half * conv[n] + VISCOSITY * f[n])
                piece = rows_of(partial[row], s) + TIME_STEP * jnp.stack(res, axis=1)
                pieces.append(piece)
                means[arr, s] = jnp.sum(piece * piece, axis=1) / 10.0
        fixed[row] = jnp.concatenate(pieces, axis=1)
        sens_rows[row] = jnp.stack([jnp.sum(means[0, s] * means[1, s], axis=0) for s in range(slots)])
    return fixed[0], fixed[height - 1], sens_rows[0], sens_rows[height - 1]


def reverse_lanes(rows):
    width = rows.shape[-1]
    ri = lax.broadcasted_iota(jnp.int32, (width, width), 0)
    ci = lax.broadcasted_iota(jnp.int32, (width, width), 1)
    turn = jnp.where(ri + ci == width - 1, 1.0, 0.0).astype(jnp.float32)
    flat = rows.reshape(-1, width)
    out = jnp.dot(flat, turn, precision=lax.Precision.HIGHEST, preferred_element_type=jnp.float32)
    return out.reshape(rows.shape)


def edge_kernel(x_ref, a_ref, lo_ref, hi_ref):
    modes, parts, nv, slots, height, _ = x_ref.shape
    for arr, src in enumerate((x_ref, a_ref)):
        for m in range(modes):
            for p in range(parts):
                for n in range(nv):
                    k = p * nv + n
                    for s in range(slots):
                        at = (arr * slots + s) * parts * nv + k
                        lo_ref[m, pl.ds(at, 1), :] = src[m, p, n, s, 0:1, :]
                        hi_ref[m, pl.ds(at, 1), :] = src[m, p, n, s, height - 1:height, :]


def edge_rows(x, a):
    modes, parts, nv, slots, height, width = x.shape
    edge_shape = jax.ShapeDtypeStruct((modes, 2 * slots * parts * nv, width), jnp.float32)
    return pl.pallas_call(edge_kernel, out_shape=[edge_shape, edge_shape])(x, a)


def per_device(direct, adjoint, density, velocity, pressure, block_home, face_nbr, face_flip):
    modes, parts, nv, slots, height, width = direct.shape
    modes_total = modes * lax.axis_size("mode")
    live = (face_nbr >= 0).astype(jnp.int32)
    positions = jnp.take(block_home, jnp.maximum(face_nbr, 0), axis=0)
    slot_of = positions % slots
    table = jnp.stack(
        [
            slot_of[:, 0], face_flip[:, 0], slot_of[:, 1], face_flip[:, 1],
            slot_of[:, 2], live[:, 2], slot_of[:, 3], live[:, 3],
        ],
        axis=1,
    ).reshape(-1)
    mode_base = (lax.axis_index("mode") * modes).astype(jnp.int32)
    table = jnp.concatenate([table.astype(jnp.int32), mode_base[None]])

    with jax.named_scope("edge_exchange_0"):
        down, up = edge_rows(direct, adjoint)
        rlo = shifted(up, "blk", 1)
        rhi = shifted(down, "blk", -1)
    with jax.named_scope("flow_step_0"):
        q1, a1, sens, elo, ehi = run_step(
            table, direct, adjoint, None, None, None, density, velocity, pressure, None, modes_total, True
        )
    with jax.named_scope("edge_fix_0"):
        c0, c7, s0, s7 = fix_rows(elo, ehi, rlo, rhi, slot_of, face_flip, density, velocity, pressure)
        sens = sens.at[:, 0, :].add(s0).at[:, height - 1, :].add(s7)
    with jax.named_scope("edge_exchange_1"):
        rlo = shifted(c7, "blk", 1)
        rhi = shifted(c0, "blk", -1)
    with jax.named_scope("flow_step_1"):
        q2, a2, sens = run_step(
            table, q1, a1, rlo, rhi, (c0, c7), density, velocity, pressure, sens, modes_total, False
        )
    with jax.named_scope("mode_reduce"):
        count = lax.axis_size("mode")
        me = lax.axis_index("mode")
        stacked = jnp.stack([sens] + [shifted(sens, "mode", k) for k in range(1, count)])
        total = None
        for j in range(count):
            part = lax.dynamic_index_in_dim(stacked, (me - j) % count, axis=0, keepdims=False)
            total = part if total is None else total + part
        sensitivity = total / (STEPS * modes_total)
    return (q2, a2, sensitivity)


def solution(mesh):
    placed = (
        P("mode", None, None, "blk", None, None),
        P("mode", None, None, "blk", None, None),
        P("blk", None, None),
        P(None, "blk", None, None),
        P("blk", None, None),
        P(),
        P("blk", None),
        P("blk", None),
    )
    return jax.shard_map(
        per_device,
        mesh=mesh,
        in_specs=placed,
        out_specs=(
            P("mode", None, None, "blk", None, None),
            P("mode", None, None, "blk", None, None),
            P("blk", None, None),
        ),
        check_vma=False,
    )
```

```python
import functools

import jax
import jax.numpy as jnp
from jax import lax
from jax.experimental import pallas as pl
from jax.experimental.pallas import tpu as pltpu
from jax.sharding import PartitionSpec as P

STEPS = 2

HEAT_RATIO = 1.4
VISCOSITY = 0.25
TIME_STEP = 0.05
SPAN_WAVE = 0.5
BASE_FREQ = 0.2

NV = 5
ENTRIES = 8


def shifted(block, axis, distance):
    n = lax.axis_size(axis)
    route = [((i - distance) % n, i) for i in range(n)]
    return lax.ppermute(block, axis, route)


def direct_rates(bf, X, Y, dsX, dcX, lapX, dsY, dcY, lapY, w):
    r, ir, u, v, kp = bf
    b = SPAN_WAVE
    damp = SPAN_WAVE * SPAN_WAVE

    def conv(ds, dc):
        return [
            u * ds[0] + r * ds[1] + (v * dc[0] + r * dc[2]),
            u * ds[1] + ds[4] * ir + v * dc[1],
            u * ds[2] + (v * dc[2] + dc[4] * ir),
            u * ds[3] + v * dc[3],
            kp * ds[1] + u * ds[4] + (kp * dc[2] + v * dc[4]),
        ]

    def span(f):
        return [r * f[3], None, None, f[4] * ir, kp * f[3]]

    cX = conv(dsX, dcX)
    cY = conv(dsY, dcY)
    sX = span(X)
    sY = span(Y)
    re, im = [], []
    for n in range(NV):
        a = -cX[n] + VISCOSITY * (lapX[n] - damp * X[n])
        if sY[n] is not None:
            a = a + b * sY[n]
        a = a + w * Y[n]
        c = -cY[n] + VISCOSITY * (lapY[n] - damp * Y[n])
        if sX[n] is not None:
            c = c - b * sX[n]
        c = c - w * X[n]
        re.append(a)
        im.append(c)
    return re, im


def adjoint_rates(bf, X, Y, dsX, dcX, lapX, dsY, dcY, lapY, w):
    r, ir, u, v, kp = bf
    b = SPAN_WAVE
    damp = SPAN_WAVE * SPAN_WAVE

    def conv(ds, dc):
        return [
            u * ds[0] + v * dc[0],
            r * ds[0] + u * ds[1] + kp * ds[4] + v * dc[1],
            u * ds[2] + (r * dc[0] + v * dc[2] + kp * dc[4]),
            u * ds[3] + v * dc[3],
            ds[1] * ir + u * ds[4] + (dc[2] * ir + v * dc[4]),
        ]

    def span(f):
        return [None, None, None, r * f[0] + kp * f[4], f[3] * ir]

    cX = conv(dsX, dcX)
    cY = conv(dsY, dcY)
    sX = span(X)
    sY = span(Y)
    re, im = [], []
    for n in range(NV):
        a = cX[n] + VISCOSITY * (lapX[n] - damp * X[n])
        if sY[n] is not None:
            a = a - b * sY[n]
        a = a - w * Y[n]
        c = cY[n] + VISCOSITY * (lapY[n] - damp * Y[n])
        if sX[n] is not None:
            c = c + b * sX[n]
        c = c + w * X[n]
        re.append(a)
        im.append(c)
    return re, im


LANES = 128


def pick_rows(ref, arr, slot, slots):
    rows = NV * 2
    out = ref[0, pl.ds(arr * slots * rows, rows), :]
    for other in range(1, slots):
        cand = ref[0, pl.ds((arr * slots + other) * rows, rows), :]
        out = jnp.where((jnp.zeros(out.shape, jnp.int32) + slot) == other, cand, out)
    return out


def step_kernel(tbl, *refs, modes_total, first, ghosts, patched):
    refs = list(refs)
    x_ref, a_ref = refs[0], refs[1]
    refs = refs[2:]
    if ghosts:
        rlo_ref, rhi_ref, tlo_ref, thi_ref = refs[:4]
        refs = refs[4:]
    if patched:
        c0_ref, c7_ref = refs[:2]
        refs = refs[2:]
    rho_ref, vel_ref, prs_ref = refs[:3]
    refs = refs[3:]
    if not first:
        sin_ref = refs.pop(0)
    if first:
        xo_ref, ao_ref, sens_ref, elo_ref, ehi_ref, gh_ref = refs
    else:
        xo_ref, ao_ref, sens_ref, gh_ref = refs
    m = pl.program_id(0)
    slots = x_ref.shape[3]
    height = x_ref.shape[4]
    width = x_ref.shape[5]
    chunks = width // LANES
    shape = (height, LANES)

    @pl.when(m == 0)
    def _init():
        if first:
            sens_ref[...] = jnp.zeros(sens_ref.shape, jnp.float32)
        else:
            sens_ref[...] = sin_ref[...]

    for s in range(slots):
        for side, (tcol, fcol) in enumerate(((0, 1), (2, 3))):
            t = tbl[s * ENTRIES + tcol]
            f = tbl[s * ENTRIES + fcol]
            for arr in range(2):
                if ghosts:
                    recv_ref, turn_ref = ((rlo_ref, tlo_ref), (rhi_ref, thi_ref))[side]
                    plain = pick_rows(recv_ref, arr, t, slots)
                    turned = pick_rows(turn_ref, arr, t, slots)
                    flag = (jnp.zeros(plain.shape, jnp.int32) + f) != 0
                    gh_ref[arr, side, s] = jnp.where(flag, turned, plain)
                else:
                    gh_ref[arr, side, s] = jnp.zeros(gh_ref.shape[3:], jnp.float32)

    kf = (tbl[slots * ENTRIES] + m).astype(jnp.float32)
    w = BASE_FREQ * (jnp.zeros(shape, jnp.float32) + (kf - modes_total / 2 + 0.5))
    row = lax.broadcasted_iota(jnp.int32, shape, 0)
    lane = lax.broadcasted_iota(jnp.int32, shape, 1)
    zero_i = jnp.zeros(shape, jnp.int32)
    first_row = row == 0
    last_row = row == height - 1
    first_lane = lane == 0
    last_lane = lane == LANES - 1
    def edge_row(ref, arr, slot, k, cols):
        if isinstance(slot, int):
            return ref[0, pl.ds((arr * slots + slot) * 2 * NV + k, 1), cols]
        out = ref[0, pl.ds(arr * slots * 2 * NV + k, 1), cols]
        for other in range(1, slots):
            cand = ref[0, pl.ds((arr * slots + other) * 2 * NV + k, 1), cols]
            out = jnp.where((jnp.zeros(out.shape, jnp.int32) + slot) == other, cand, out)
        return out

    def load(src, arr, p, n, slot, k, cols):
        g = src[0, p, n, slot, :, cols]
        if patched:
            top = jnp.broadcast_to(edge_row(c0_ref, arr, slot, k, cols), shape)
            bottom = jnp.broadcast_to(edge_row(c7_ref, arr, slot, k, cols), shape)
            g = jnp.where(first_row, top, jnp.where(last_row, bottom, g))
        return g

    inner = (row > 0) & (row < height - 1)

    for s in range(slots):
        base = s * ENTRIES
        jl_s, jl_live = tbl[base + 4], tbl[base + 5]
        jh_s, jh_live = tbl[base + 6], tbl[base + 7]
        jl_mask = (zero_i + jl_live) != 0
        jh_mask = (zero_i + jh_live) != 0
        for b in range(chunks):
            cs = slice(b * LANES, (b + 1) * LANES)
            r = rho_ref[s, :, cs]
            ir = 1.0 / r
            u = vel_ref[0, s, :, cs]
            v = vel_ref[1, s, :, cs]
            kp = HEAT_RATIO * prs_ref[s, :, cs]
            bf = (r, ir, u, v, kp)
            means = []
            for arr, (src, dst, rates) in enumerate(((x_ref, xo_ref, direct_rates), (a_ref, ao_ref, adjoint_rates))):
                vals, dss, dcs, laps = [], [], [], []
                for p in range(2):
                    for n in range(NV):
                        k = p * NV + n
                        g = load(src, arr, p, n, s, k, cs)
                        lo_b = jnp.broadcast_to(gh_ref[arr, 0, s, k:k + 1, cs], shape)
                        hi_b = jnp.broadcast_to(gh_ref[arr, 1, s, k:k + 1, cs], shape)
                        im1 = jnp.where(first_row, lo_b, pltpu.roll(g, 1, 0))
                        ip1 = jnp.where(last_row, hi_b, pltpu.roll(g, height - 1, 0))
                        if b > 0:
                            left = load(src, arr, p, n, s, k, slice((b - 1) * LANES, b * LANES))
                        else:
                            left = jnp.where(jl_mask, load(src, arr, p, n, jl_s, k, slice(width - LANES, width)), 0.0)
                        if b < chunks - 1:
                            right = load(src, arr, p, n, s, k, slice((b + 1) * LANES, (b + 2) * LANES))
                        else:
                            right = jnp.where(jh_mask, load(src, arr, p, n, jh_s, k, slice(0, LANES)), 0.0)
                        jm1 = jnp.where(first_lane, pltpu.roll(left, 1, 1), pltpu.roll(g, 1, 1))
                        jp1 = jnp.where(last_lane, pltpu.roll(right, LANES - 1, 1), pltpu.roll(g, LANES - 1, 1))
                        vals.append(g)
                        dss.append((ip1 - im1) * 0.5)
                        dcs.append((jp1 - jm1) * 0.5)
                        laps.append(ip1 + im1 + jp1 + jm1 - 4.0 * g)
                X, Y = vals[:NV], vals[NV:]
                re, im = rates(bf, X, Y, dss[:NV], dcs[:NV], laps[:NV], dss[NV:], dcs[NV:], laps[NV:], w)
                total = None
                for p, rate in enumerate((re, im)):
                    for n in range(NV):
                        k = p * NV + n
                        nv = vals[k] + TIME_STEP * rate[n]
                        dst[0, p, n, s, :, cs] = nv
                        if first:
                            elo_ref[arr, 0, s, pl.ds(k, 1), cs] = nv[0:1, :]
                            ehi_ref[arr, 0, s, pl.ds(k, 1), cs] = nv[height - 1:height, :]
                        sq = nv * nv
                        total = sq if total is None else total + sq
                means.append(total / 10.0)
            term = means[0] * means[1]
            if not ghosts:
                term = jnp.where(inner, term, 0.0)
            sens_ref[s, :, cs] = sens_ref[s, :, cs] + term


def run_step(tbl, x, a, rlo, rhi, patch, density, velocity, pressure, sens_in, modes_total, first):
    modes, parts, nv, slots, height, width = x.shape
    state_block = (1, parts, nv, slots, height, width)
    edge_block = (1, 2 * slots * parts * nv, width)
    state_spec = pl.BlockSpec(state_block, lambda m, t: (m, 0, 0, 0, 0, 0))
    edge_spec = pl.BlockSpec(edge_block, lambda m, t: (m, 0, 0))
    flow_spec = pl.BlockSpec((slots, height, width), lambda m, t: (0, 0, 0))
    vel_spec = pl.BlockSpec((2, slots, height, width), lambda m, t: (0, 0, 0, 0))
    ghosts = rlo is not None
    patched = patch is not None
    in_specs = [state_spec, state_spec]
    args = [x, a]
    if ghosts:
        in_specs += [edge_spec] * 4
        args += [rlo, rhi, reverse_lanes(rlo), reverse_lanes(rhi)]
    if patched:
        in_specs += [edge_spec] * 2
        args += list(patch)
    in_specs += [flow_spec, vel_spec, flow_spec]
    args += [density, velocity, pressure]
    if not first:
        in_specs.append(flow_spec)
        args.append(sens_in)
    out_shape = [
        jax.ShapeDtypeStruct(x.shape, jnp.float32),
        jax.ShapeDtypeStruct(a.shape, jnp.float32),
        jax.ShapeDtypeStruct((slots, height, width), jnp.float32),
    ]
    out_specs = [state_spec, state_spec, flow_spec]
    if first:
        part_shape = jax.ShapeDtypeStruct((2, modes, slots, parts * nv, width), jnp.float32)
        part_spec = pl.BlockSpec((2, 1, slots, parts * nv, width), lambda m, t: (0, m, 0, 0, 0))
        out_shape += [part_shape, part_shape]
        out_specs += [part_spec, part_spec]
    grid_spec = pltpu.PrefetchScalarGridSpec(
        num_scalar_prefetch=1,
        grid=(modes,),
        in_specs=in_specs,
        out_specs=out_specs,
        scratch_shapes=[
            pltpu.VMEM((2, 2, slots, parts * nv, width), jnp.float32),
        ],
    )
    kernel = functools.partial(step_kernel, modes_total=modes_total, first=first, ghosts=ghosts, patched=patched)
    return pl.pallas_call(
        kernel,
        grid_spec=grid_spec,
        out_shape=out_shape,
        compiler_params=pltpu.CompilerParams(dimension_semantics=("arbitrary",)),
    )(tbl, *args)


def ghost_term(f, r, ir, u, kp, transpose):
    if transpose:
        return [u * f[0], r * f[0] + u * f[1] + kp * f[4], u * f[2], u * f[3], f[1] * ir + u * f[4]]
    return [u * f[0] + r * f[1], u * f[1] + f[4] * ir, u * f[2], u * f[3], kp * f[1] + u * f[4]]


def unflat(e, slots):
    modes, _, width = e.shape
    return jnp.transpose(e.reshape(modes, 2, slots, 2 * NV, width), (1, 0, 2, 3, 4))


def flat(e):
    _, modes, slots, rows, width = e.shape
    return jnp.transpose(e, (1, 0, 2, 3, 4)).reshape(modes, 2 * slots * rows, width)


def fix_rows(partial0, partial7, rlo, rhi, slot_of, face_flip, density, velocity, pressure):
    slots = density.shape[0]
    rlo, rhi = (unflat(e, slots) for e in (rlo, rhi))
    _, modes, slots, rows, width = partial0.shape
    height = density.shape[1]

    def picked(recv, side):
        plain = jnp.take(recv, slot_of[:, side], axis=2)
        turned = reverse_lanes(plain)
        flag = (face_flip[:, side] != 0)[None, None, :, None, None]
        return jnp.where(flag, turned, plain)

    ghost = {0: picked(rlo, 0), height - 1: picked(rhi, 1)}
    partial = {0: partial0, height - 1: partial7}
    fixed = {}
    sens_rows = {}
    for row in (0, height - 1):
        r = density[:, row, :]
        ir = 1.0 / r
        u = velocity[0][:, row, :]
        kp = HEAT_RATIO * pressure[:, row, :]
        half = 0.5 if row == 0 else -0.5
        out = []
        for arr, sign in ((0, 1.0), (1, -1.0)):
            g = ghost[row][arr].reshape(modes, slots, 2, NV, width)
            res = []
            for p in range(2):
                f = [g[:, :, p, n, :] for n in range(NV)]
                conv = ghost_term(f, r, ir, u, kp, arr == 1)
                for n in range(NV):
                    res.append(sign * half * conv[n] + VISCOSITY * f[n])
            delta = jnp.stack(res, axis=2)
            out.append(partial[row][arr] + TIME_STEP * delta)
        fixed[row] = jnp.stack(out)
        means = jnp.sum(fixed[row] * fixed[row], axis=3) / 10.0
        sens_rows[row] = jnp.sum(means[0] * means[1], axis=0)
    return flat(fixed[0]), flat(fixed[height - 1]), sens_rows[0], sens_rows[height - 1]


def reverse_lanes(rows):
    width = rows.shape[-1]
    ri = lax.broadcasted_iota(jnp.int32, (width, width), 0)
    ci = lax.broadcasted_iota(jnp.int32, (width, width), 1)
    turn = jnp.where(ri + ci == width - 1, 1.0, 0.0).astype(jnp.float32)
    flat = rows.reshape(-1, width)
    out = jnp.dot(flat, turn, precision=lax.Precision.HIGHEST, preferred_element_type=jnp.float32)
    return out.reshape(rows.shape)


def edge_kernel(x_ref, a_ref, lo_ref, hi_ref):
    modes, parts, nv, slots, height, _ = x_ref.shape
    for arr, src in enumerate((x_ref, a_ref)):
        for m in range(modes):
            for p in range(parts):
                for n in range(nv):
                    k = p * nv + n
                    for s in range(slots):
                        at = (arr * slots + s) * parts * nv + k
                        lo_ref[m, pl.ds(at, 1), :] = src[m, p, n, s, 0:1, :]
                        hi_ref[m, pl.ds(at, 1), :] = src[m, p, n, s, height - 1:height, :]


def edge_rows(x, a):
    modes, parts, nv, slots, height, width = x.shape
    edge_shape = jax.ShapeDtypeStruct((modes, 2 * slots * parts * nv, width), jnp.float32)
    return pl.pallas_call(edge_kernel, out_shape=[edge_shape, edge_shape])(x, a)


def per_device(direct, adjoint, density, velocity, pressure, block_home, face_nbr, face_flip):
    modes, parts, nv, slots, height, width = direct.shape
    modes_total = modes * lax.axis_size("mode")
    live = (face_nbr >= 0).astype(jnp.int32)
    positions = jnp.take(block_home, jnp.maximum(face_nbr, 0), axis=0)
    slot_of = positions % slots
    table = jnp.stack(
        [
            slot_of[:, 0], face_flip[:, 0], slot_of[:, 1], face_flip[:, 1],
            slot_of[:, 2], live[:, 2], slot_of[:, 3], live[:, 3],
        ],
        axis=1,
    ).reshape(-1)
    mode_base = (lax.axis_index("mode") * modes).astype(jnp.int32)
    table = jnp.concatenate([table.astype(jnp.int32), mode_base[None]])

    with jax.named_scope("edge_exchange_0"):
        down, up = edge_rows(direct, adjoint)
        rlo = shifted(up, "blk", 1)
        rhi = shifted(down, "blk", -1)
    with jax.named_scope("flow_step_0"):
        q1, a1, sens, elo, ehi = run_step(
            table, direct, adjoint, None, None, None, density, velocity, pressure, None, modes_total, True
        )
    with jax.named_scope("edge_fix_0"):
        c0, c7, s0, s7 = fix_rows(elo, ehi, rlo, rhi, slot_of, face_flip, density, velocity, pressure)
        sens = sens.at[:, 0, :].add(s0).at[:, height - 1, :].add(s7)
    with jax.named_scope("edge_exchange_1"):
        rlo = shifted(c7, "blk", 1)
        rhi = shifted(c0, "blk", -1)
    with jax.named_scope("flow_step_1"):
        q2, a2, sens = run_step(
            table, q1, a1, rlo, rhi, (c0, c7), density, velocity, pressure, sens, modes_total, False
        )
    with jax.named_scope("mode_reduce"):
        count = lax.axis_size("mode")
        me = lax.axis_index("mode")
        stacked = jnp.stack([sens] + [shifted(sens, "mode", k) for k in range(1, count)])
        total = None
        for j in range(count):
            part = lax.dynamic_index_in_dim(stacked, (me - j) % count, axis=0, keepdims=False)
            total = part if total is None else total + part
        sensitivity = total / (STEPS * modes_total)
    return (q2, a2, sensitivity)


def solution(mesh):
    placed = (
        P("mode", None, None, "blk", None, None),
        P("mode", None, None, "blk", None, None),
        P("blk", None, None),
        P(None, "blk", None, None),
        P("blk", None, None),
        P(),
        P("blk", None),
        P("blk", None),
    )
    return jax.shard_map(
        per_device,
        mesh=mesh,
        in_specs=placed,
        out_specs=(
            P("mode", None, None, "blk", None, None),
            P("mode", None, None, "blk", None, None),
            P("blk", None, None),
        ),
        check_vma=False,
    )
```

```python
import functools

import jax
import jax.numpy as jnp
from jax import lax
from jax.experimental import pallas as pl
from jax.experimental.pallas import tpu as pltpu
from jax.sharding import PartitionSpec as P

STEPS = 2

HEAT_RATIO = 1.4
VISCOSITY = 0.25
TIME_STEP = 0.05
SPAN_WAVE = 0.5
BASE_FREQ = 0.2

NV = 5
ENTRIES = 8


def shifted(block, axis, distance):
    n = lax.axis_size(axis)
    route = [((i - distance) % n, i) for i in range(n)]
    return lax.ppermute(block, axis, route)


def direct_rates(bf, X, Y, dsX, dcX, lapX, dsY, dcY, lapY, w):
    r, ir, u, v, kp = bf
    b = SPAN_WAVE
    damp = SPAN_WAVE * SPAN_WAVE

    def conv(ds, dc):
        return [
            u * ds[0] + r * ds[1] + (v * dc[0] + r * dc[2]),
            u * ds[1] + ds[4] * ir + v * dc[1],
            u * ds[2] + (v * dc[2] + dc[4] * ir),
            u * ds[3] + v * dc[3],
            kp * ds[1] + u * ds[4] + (kp * dc[2] + v * dc[4]),
        ]

    def span(f):
        return [r * f[3], None, None, f[4] * ir, kp * f[3]]

    cX = conv(dsX, dcX)
    cY = conv(dsY, dcY)
    sX = span(X)
    sY = span(Y)
    re, im = [], []
    for n in range(NV):
        a = -cX[n] + VISCOSITY * (lapX[n] - damp * X[n])
        if sY[n] is not None:
            a = a + b * sY[n]
        a = a + w * Y[n]
        c = -cY[n] + VISCOSITY * (lapY[n] - damp * Y[n])
        if sX[n] is not None:
            c = c - b * sX[n]
        c = c - w * X[n]
        re.append(a)
        im.append(c)
    return re, im


def adjoint_rates(bf, X, Y, dsX, dcX, lapX, dsY, dcY, lapY, w):
    r, ir, u, v, kp = bf
    b = SPAN_WAVE
    damp = SPAN_WAVE * SPAN_WAVE

    def conv(ds, dc):
        return [
            u * ds[0] + v * dc[0],
            r * ds[0] + u * ds[1] + kp * ds[4] + v * dc[1],
            u * ds[2] + (r * dc[0] + v * dc[2] + kp * dc[4]),
            u * ds[3] + v * dc[3],
            ds[1] * ir + u * ds[4] + (dc[2] * ir + v * dc[4]),
        ]

    def span(f):
        return [None, None, None, r * f[0] + kp * f[4], f[3] * ir]

    cX = conv(dsX, dcX)
    cY = conv(dsY, dcY)
    sX = span(X)
    sY = span(Y)
    re, im = [], []
    for n in range(NV):
        a = cX[n] + VISCOSITY * (lapX[n] - damp * X[n])
        if sY[n] is not None:
            a = a - b * sY[n]
        a = a - w * Y[n]
        c = cY[n] + VISCOSITY * (lapY[n] - damp * Y[n])
        if sX[n] is not None:
            c = c + b * sX[n]
        c = c + w * X[n]
        re.append(a)
        im.append(c)
    return re, im


LANES = 128


def pick_rows(ref, arr, slot, slots):
    rows = NV * 2
    out = ref[0, pl.ds(arr * slots * rows, rows), :]
    for other in range(1, slots):
        cand = ref[0, pl.ds((arr * slots + other) * rows, rows), :]
        out = jnp.where((jnp.zeros(out.shape, jnp.int32) + slot) == other, cand, out)
    return out


def step_kernel(tbl, *refs, modes_total, first, ghosts, patched):
    refs = list(refs)
    x_ref, a_ref = refs[0], refs[1]
    refs = refs[2:]
    if ghosts:
        rlo_ref, rhi_ref, tlo_ref, thi_ref = refs[:4]
        refs = refs[4:]
    if patched:
        c0_ref, c7_ref = refs[:2]
        refs = refs[2:]
    rho_ref, vel_ref, prs_ref = refs[:3]
    refs = refs[3:]
    if not first:
        sin_ref = refs.pop(0)
    if first:
        xo_ref, ao_ref, sens_ref, elo_ref, ehi_ref, gh_ref = refs
    else:
        xo_ref, ao_ref, sens_ref, gh_ref = refs
    m = pl.program_id(0)
    slots = x_ref.shape[3]
    height = x_ref.shape[4]
    width = x_ref.shape[5]
    chunks = width // LANES
    shape = (height, LANES)

    @pl.when(m == 0)
    def _init():
        if first:
            sens_ref[...] = jnp.zeros(sens_ref.shape, jnp.float32)
        else:
            sens_ref[...] = sin_ref[...]

    for s in range(slots):
        for side, (tcol, fcol) in enumerate(((0, 1), (2, 3))):
            t = tbl[s * ENTRIES + tcol]
            f = tbl[s * ENTRIES + fcol]
            for arr in range(2):
                if ghosts:
                    recv_ref, turn_ref = ((rlo_ref, tlo_ref), (rhi_ref, thi_ref))[side]
                    plain = pick_rows(recv_ref, arr, t, slots)
                    turned = pick_rows(turn_ref, arr, t, slots)
                    flag = (jnp.zeros(plain.shape, jnp.int32) + f) != 0
                    gh_ref[arr, side, s] = jnp.where(flag, turned, plain)
                else:
                    gh_ref[arr, side, s] = jnp.zeros(gh_ref.shape[3:], jnp.float32)

    kf = (tbl[slots * ENTRIES] + m).astype(jnp.float32)
    w = BASE_FREQ * (jnp.zeros(shape, jnp.float32) + (kf - modes_total / 2 + 0.5))
    row = lax.broadcasted_iota(jnp.int32, shape, 0)
    lane = lax.broadcasted_iota(jnp.int32, shape, 1)
    zero_i = jnp.zeros(shape, jnp.int32)
    first_row = row == 0
    last_row = row == height - 1
    first_lane = lane == 0
    last_lane = lane == LANES - 1
    def edge_row(ref, arr, slot, k, cols):
        if isinstance(slot, int):
            return ref[0, pl.ds((arr * slots + slot) * 2 * NV + k, 1), cols]
        out = ref[0, pl.ds(arr * slots * 2 * NV + k, 1), cols]
        for other in range(1, slots):
            cand = ref[0, pl.ds((arr * slots + other) * 2 * NV + k, 1), cols]
            out = jnp.where((jnp.zeros(out.shape, jnp.int32) + slot) == other, cand, out)
        return out

    def load(src, arr, p, n, slot, k, cols):
        g = src[0, p, n, slot, :, cols]
        if patched:
            top = jnp.broadcast_to(edge_row(c0_ref, arr, slot, k, cols), shape)
            bottom = jnp.broadcast_to(edge_row(c7_ref, arr, slot, k, cols), shape)
            g = jnp.where(first_row, top, jnp.where(last_row, bottom, g))
        return g

    inner = (row > 0) & (row < height - 1)

    for s in range(slots):
        base = s * ENTRIES
        jl_s, jl_live = tbl[base + 4], tbl[base + 5]
        jh_s, jh_live = tbl[base + 6], tbl[base + 7]
        jl_mask = (zero_i + jl_live) != 0
        jh_mask = (zero_i + jh_live) != 0
        for b in range(chunks):
            cs = slice(b * LANES, (b + 1) * LANES)
            r = rho_ref[s, :, cs]
            ir = 1.0 / r
            u = vel_ref[0, s, :, cs]
            v = vel_ref[1, s, :, cs]
            kp = HEAT_RATIO * prs_ref[s, :, cs]
            bf = (r, ir, u, v, kp)
            means = []
            for arr, (src, dst, rates) in enumerate(((x_ref, xo_ref, direct_rates), (a_ref, ao_ref, adjoint_rates))):
                vals, dss, dcs, laps = [], [], [], []
                for p in range(2):
                    for n in range(NV):
                        k = p * NV + n
                        g = load(src, arr, p, n, s, k, cs)
                        lo_b = jnp.broadcast_to(gh_ref[arr, 0, s, k:k + 1, cs], shape)
                        hi_b = jnp.broadcast_to(gh_ref[arr, 1, s, k:k + 1, cs], shape)
                        im1 = jnp.where(first_row, lo_b, pltpu.roll(g, 1, 0))
                        ip1 = jnp.where(last_row, hi_b, pltpu.roll(g, height - 1, 0))
                        if b > 0:
                            left = load(src, arr, p, n, s, k, slice((b - 1) * LANES, b * LANES))
                        else:
                            left = jnp.where(jl_mask, load(src, arr, p, n, jl_s, k, slice(width - LANES, width)), 0.0)
                        if b < chunks - 1:
                            right = load(src, arr, p, n, s, k, slice((b + 1) * LANES, (b + 2) * LANES))
                        else:
                            right = jnp.where(jh_mask, load(src, arr, p, n, jh_s, k, slice(0, LANES)), 0.0)
                        jm1 = jnp.where(first_lane, pltpu.roll(left, 1, 1), pltpu.roll(g, 1, 1))
                        jp1 = jnp.where(last_lane, pltpu.roll(right, LANES - 1, 1), pltpu.roll(g, LANES - 1, 1))
                        vals.append(g)
                        dss.append((ip1 - im1) * 0.5)
                        dcs.append((jp1 - jm1) * 0.5)
                        laps.append(ip1 + im1 + jp1 + jm1 - 4.0 * g)
                X, Y = vals[:NV], vals[NV:]
                re, im = rates(bf, X, Y, dss[:NV], dcs[:NV], laps[:NV], dss[NV:], dcs[NV:], laps[NV:], w)
                total = None
                for p, rate in enumerate((re, im)):
                    for n in range(NV):
                        k = p * NV + n
                        nv = vals[k] + TIME_STEP * rate[n]
                        dst[0, p, n, s, :, cs] = nv
                        if first:
                            at = (arr * slots + s) * 2 * NV + k
                            elo_ref[0, pl.ds(at, 1), cs] = nv[0:1, :]
                            ehi_ref[0, pl.ds(at, 1), cs] = nv[height - 1:height, :]
                        sq = nv * nv
                        total = sq if total is None else total + sq
                means.append(total / 10.0)
            term = means[0] * means[1]
            if not ghosts:
                term = jnp.where(inner, term, 0.0)
            sens_ref[s, :, cs] = sens_ref[s, :, cs] + term


def run_step(tbl, x, a, rlo, rhi, patch, density, velocity, pressure, sens_in, modes_total, first):
    modes, parts, nv, slots, height, width = x.shape
    state_block = (1, parts, nv, slots, height, width)
    edge_block = (1, 2 * slots * parts * nv, width)
    state_spec = pl.BlockSpec(state_block, lambda m, t: (m, 0, 0, 0, 0, 0))
    edge_spec = pl.BlockSpec(edge_block, lambda m, t: (m, 0, 0))
    flow_spec = pl.BlockSpec((slots, height, width), lambda m, t: (0, 0, 0))
    vel_spec = pl.BlockSpec((2, slots, height, width), lambda m, t: (0, 0, 0, 0))
    ghosts = rlo is not None
    patched = patch is not None
    in_specs = [state_spec, state_spec]
    args = [x, a]
    if ghosts:
        in_specs += [edge_spec] * 4
        args += [rlo, rhi, reverse_lanes(rlo), reverse_lanes(rhi)]
    if patched:
        in_specs += [edge_spec] * 2
        args += list(patch)
    in_specs += [flow_spec, vel_spec, flow_spec]
    args += [density, velocity, pressure]
    if not first:
        in_specs.append(flow_spec)
        args.append(sens_in)
    out_shape = [
        jax.ShapeDtypeStruct(x.shape, jnp.float32),
        jax.ShapeDtypeStruct(a.shape, jnp.float32),
        jax.ShapeDtypeStruct((slots, height, width), jnp.float32),
    ]
    out_specs = [state_spec, state_spec, flow_spec]
    if first:
        edge_shape = jax.ShapeDtypeStruct((modes, 2 * slots * parts * nv, width), jnp.float32)
        out_shape += [edge_shape, edge_shape]
        out_specs += [edge_spec, edge_spec]
    grid_spec = pltpu.PrefetchScalarGridSpec(
        num_scalar_prefetch=1,
        grid=(modes,),
        in_specs=in_specs,
        out_specs=out_specs,
        scratch_shapes=[
            pltpu.VMEM((2, 2, slots, parts * nv, width), jnp.float32),
        ],
    )
    kernel = functools.partial(step_kernel, modes_total=modes_total, first=first, ghosts=ghosts, patched=patched)
    return pl.pallas_call(
        kernel,
        grid_spec=grid_spec,
        out_shape=out_shape,
        compiler_params=pltpu.CompilerParams(dimension_semantics=("arbitrary",)),
    )(tbl, *args)


def ghost_term(f, r, ir, u, kp, transpose):
    if transpose:
        return [u * f[0], r * f[0] + u * f[1] + kp * f[4], u * f[2], u * f[3], f[1] * ir + u * f[4]]
    return [u * f[0] + r * f[1], u * f[1] + f[4] * ir, u * f[2], u * f[3], kp * f[1] + u * f[4]]


def unflat(e, slots):
    modes, _, width = e.shape
    return jnp.transpose(e.reshape(modes, 2, slots, 2 * NV, width), (1, 0, 2, 3, 4))


def flat(e):
    _, modes, slots, rows, width = e.shape
    return jnp.transpose(e, (1, 0, 2, 3, 4)).reshape(modes, 2 * slots * rows, width)


def fix_rows(partial0, partial7, rlo, rhi, slot_of, face_flip, density, velocity, pressure):
    slots = density.shape[0]
    partial0, partial7, rlo, rhi = (unflat(e, slots) for e in (partial0, partial7, rlo, rhi))
    _, modes, slots, rows, width = partial0.shape
    height = density.shape[1]

    def picked(recv, side):
        plain = jnp.take(recv, slot_of[:, side], axis=2)
        turned = reverse_lanes(plain)
        flag = (face_flip[:, side] != 0)[None, None, :, None, None]
        return jnp.where(flag, turned, plain)

    ghost = {0: picked(rlo, 0), height - 1: picked(rhi, 1)}
    partial = {0: partial0, height - 1: partial7}
    fixed = {}
    sens_rows = {}
    for row in (0, height - 1):
        r = density[:, row, :]
        ir = 1.0 / r
        u = velocity[0][:, row, :]
        kp = HEAT_RATIO * pressure[:, row, :]
        half = 0.5 if row == 0 else -0.5
        out = []
        for arr, sign in ((0, 1.0), (1, -1.0)):
            g = ghost[row][arr].reshape(modes, slots, 2, NV, width)
            res = []
            for p in range(2):
                f = [g[:, :, p, n, :] for n in range(NV)]
                conv = ghost_term(f, r, ir, u, kp, arr == 1)
                for n in range(NV):
                    res.append(sign * half * conv[n] + VISCOSITY * f[n])
            delta = jnp.stack(res, axis=2)
            out.append(partial[row][arr] + TIME_STEP * delta)
        fixed[row] = jnp.stack(out)
        means = jnp.sum(fixed[row] * fixed[row], axis=3) / 10.0
        sens_rows[row] = jnp.sum(means[0] * means[1], axis=0)
    return flat(fixed[0]), flat(fixed[height - 1]), sens_rows[0], sens_rows[height - 1]


def reverse_lanes(rows):
    width = rows.shape[-1]
    ri = lax.broadcasted_iota(jnp.int32, (width, width), 0)
    ci = lax.broadcasted_iota(jnp.int32, (width, width), 1)
    turn = jnp.where(ri + ci == width - 1, 1.0, 0.0).astype(jnp.float32)
    flat = rows.reshape(-1, width)
    out = jnp.dot(flat, turn, precision=lax.Precision.HIGHEST, preferred_element_type=jnp.float32)
    return out.reshape(rows.shape)


def edge_kernel(x_ref, a_ref, lo_ref, hi_ref):
    modes, parts, nv, slots, height, _ = x_ref.shape
    for arr, src in enumerate((x_ref, a_ref)):
        for m in range(modes):
            for p in range(parts):
                for n in range(nv):
                    k = p * nv + n
                    for s in range(slots):
                        at = (arr * slots + s) * parts * nv + k
                        lo_ref[m, pl.ds(at, 1), :] = src[m, p, n, s, 0:1, :]
                        hi_ref[m, pl.ds(at, 1), :] = src[m, p, n, s, height - 1:height, :]


def edge_rows(x, a):
    modes, parts, nv, slots, height, width = x.shape
    edge_shape = jax.ShapeDtypeStruct((modes, 2 * slots * parts * nv, width), jnp.float32)
    return pl.pallas_call(edge_kernel, out_shape=[edge_shape, edge_shape])(x, a)


def per_device(direct, adjoint, density, velocity, pressure, block_home, face_nbr, face_flip):
    modes, parts, nv, slots, height, width = direct.shape
    modes_total = modes * lax.axis_size("mode")
    live = (face_nbr >= 0).astype(jnp.int32)
    positions = jnp.take(block_home, jnp.maximum(face_nbr, 0), axis=0)
    slot_of = positions % slots
    table = jnp.stack(
        [
            slot_of[:, 0], face_flip[:, 0], slot_of[:, 1], face_flip[:, 1],
            slot_of[:, 2], live[:, 2], slot_of[:, 3], live[:, 3],
        ],
        axis=1,
    ).reshape(-1)
    mode_base = (lax.axis_index("mode") * modes).astype(jnp.int32)
    table = jnp.concatenate([table.astype(jnp.int32), mode_base[None]])

    with jax.named_scope("edge_exchange_0"):
        down, up = edge_rows(direct, adjoint)
    with jax.named_scope("flow_step_0"):
        q1, a1, sens, elo, ehi = run_step(
            table, direct, adjoint, None, None, None, density, velocity, pressure, None, modes_total, True
        )
    with jax.named_scope("edge_exchange_0"):
        up, down, sens = lax.optimization_barrier((up, down, sens))
        rlo = shifted(up, "blk", 1)
        rhi = shifted(down, "blk", -1)
    with jax.named_scope("edge_fix_0"):
        c0, c7, s0, s7 = fix_rows(elo, ehi, rlo, rhi, slot_of, face_flip, density, velocity, pressure)
        sens = sens.at[:, 0, :].add(s0).at[:, height - 1, :].add(s7)
    with jax.named_scope("edge_exchange_1"):
        rlo = shifted(c7, "blk", 1)
        rhi = shifted(c0, "blk", -1)
    with jax.named_scope("flow_step_1"):
        q2, a2, sens = run_step(
            table, q1, a1, rlo, rhi, (c0, c7), density, velocity, pressure, sens, modes_total, False
        )
    with jax.named_scope("mode_reduce"):
        count = lax.axis_size("mode")
        me = lax.axis_index("mode")
        stacked = jnp.stack([sens] + [shifted(sens, "mode", k) for k in range(1, count)])
        total = None
        for j in range(count):
            part = lax.dynamic_index_in_dim(stacked, (me - j) % count, axis=0, keepdims=False)
            total = part if total is None else total + part
        sensitivity = total / (STEPS * modes_total)
    return (q2, a2, sensitivity)


def solution(mesh):
    placed = (
        P("mode", None, None, "blk", None, None),
        P("mode", None, None, "blk", None, None),
        P("blk", None, None),
        P(None, "blk", None, None),
        P("blk", None, None),
        P(),
        P("blk", None),
        P("blk", None),
    )
    return jax.shard_map(
        per_device,
        mesh=mesh,
        in_specs=placed,
        out_specs=(
            P("mode", None, None, "blk", None, None),
            P("mode", None, None, "blk", None, None),
            P("blk", None, None),
        ),
        check_vma=False,
    )
```

```python
import functools

import jax
import jax.numpy as jnp
from jax import lax
from jax.experimental import pallas as pl
from jax.experimental.pallas import tpu as pltpu
from jax.sharding import PartitionSpec as P

STEPS = 2

HEAT_RATIO = 1.4
VISCOSITY = 0.25
TIME_STEP = 0.05
SPAN_WAVE = 0.5
BASE_FREQ = 0.2

NV = 5
ENTRIES = 8


def shifted(block, axis, distance):
    n = lax.axis_size(axis)
    route = [((i - distance) % n, i) for i in range(n)]
    return lax.ppermute(block, axis, route)


def direct_rates(bf, X, Y, dsX, dcX, lapX, dsY, dcY, lapY, w):
    r, ir, u, v, kp = bf
    b = SPAN_WAVE
    damp = SPAN_WAVE * SPAN_WAVE

    def conv(ds, dc):
        return [
            u * ds[0] + r * ds[1] + (v * dc[0] + r * dc[2]),
            u * ds[1] + ds[4] * ir + v * dc[1],
            u * ds[2] + (v * dc[2] + dc[4] * ir),
            u * ds[3] + v * dc[3],
            kp * ds[1] + u * ds[4] + (kp * dc[2] + v * dc[4]),
        ]

    def span(f):
        return [r * f[3], None, None, f[4] * ir, kp * f[3]]

    cX = conv(dsX, dcX)
    cY = conv(dsY, dcY)
    sX = span(X)
    sY = span(Y)
    re, im = [], []
    for n in range(NV):
        a = -cX[n] + VISCOSITY * (lapX[n] - damp * X[n])
        if sY[n] is not None:
            a = a + b * sY[n]
        a = a + w * Y[n]
        c = -cY[n] + VISCOSITY * (lapY[n] - damp * Y[n])
        if sX[n] is not None:
            c = c - b * sX[n]
        c = c - w * X[n]
        re.append(a)
        im.append(c)
    return re, im


def adjoint_rates(bf, X, Y, dsX, dcX, lapX, dsY, dcY, lapY, w):
    r, ir, u, v, kp = bf
    b = SPAN_WAVE
    damp = SPAN_WAVE * SPAN_WAVE

    def conv(ds, dc):
        return [
            u * ds[0] + v * dc[0],
            r * ds[0] + u * ds[1] + kp * ds[4] + v * dc[1],
            u * ds[2] + (r * dc[0] + v * dc[2] + kp * dc[4]),
            u * ds[3] + v * dc[3],
            ds[1] * ir + u * ds[4] + (dc[2] * ir + v * dc[4]),
        ]

    def span(f):
        return [None, None, None, r * f[0] + kp * f[4], f[3] * ir]

    cX = conv(dsX, dcX)
    cY = conv(dsY, dcY)
    sX = span(X)
    sY = span(Y)
    re, im = [], []
    for n in range(NV):
        a = cX[n] + VISCOSITY * (lapX[n] - damp * X[n])
        if sY[n] is not None:
            a = a - b * sY[n]
        a = a - w * Y[n]
        c = cY[n] + VISCOSITY * (lapY[n] - damp * Y[n])
        if sX[n] is not None:
            c = c + b * sX[n]
        c = c + w * X[n]
        re.append(a)
        im.append(c)
    return re, im


LANES = 128


def pick_rows(ref, arr, slot, slots):
    rows = NV * 2
    out = ref[0, pl.ds(arr * slots * rows, rows), :]
    for other in range(1, slots):
        cand = ref[0, pl.ds((arr * slots + other) * rows, rows), :]
        out = jnp.where((jnp.zeros(out.shape, jnp.int32) + slot) == other, cand, out)
    return out


def step_kernel(tbl, *refs, modes_total, first, ghosts, patched):
    refs = list(refs)
    x_ref, a_ref = refs[0], refs[1]
    refs = refs[2:]
    if ghosts:
        rlo_ref, rhi_ref, tlo_ref, thi_ref = refs[:4]
        refs = refs[4:]
    if patched:
        c0_ref, c7_ref = refs[:2]
        refs = refs[2:]
    rho_ref, vel_ref, prs_ref = refs[:3]
    refs = refs[3:]
    if not first:
        sin_ref = refs.pop(0)
    if first:
        xo_ref, ao_ref, sens_ref, elo_ref, ehi_ref, gh_ref = refs
    else:
        xo_ref, ao_ref, sens_ref, gh_ref = refs
    m = pl.program_id(0)
    slots = x_ref.shape[3]
    height = x_ref.shape[4]
    width = x_ref.shape[5]
    chunks = width // LANES
    shape = (height, LANES)

    @pl.when(m == 0)
    def _init():
        if first:
            sens_ref[...] = jnp.zeros(sens_ref.shape, jnp.float32)
        else:
            sens_ref[...] = sin_ref[...]

    for s in range(slots):
        for side, (tcol, fcol) in enumerate(((0, 1), (2, 3))):
            t = tbl[s * ENTRIES + tcol]
            f = tbl[s * ENTRIES + fcol]
            for arr in range(2):
                if ghosts:
                    recv_ref, turn_ref = ((rlo_ref, tlo_ref), (rhi_ref, thi_ref))[side]
                    plain = pick_rows(recv_ref, arr, t, slots)
                    turned = pick_rows(turn_ref, arr, t, slots)
                    flag = (jnp.zeros(plain.shape, jnp.int32) + f) != 0
                    gh_ref[arr, side, s] = jnp.where(flag, turned, plain)
                else:
                    gh_ref[arr, side, s] = jnp.zeros(gh_ref.shape[3:], jnp.float32)

    kf = (tbl[slots * ENTRIES] + m).astype(jnp.float32)
    w = BASE_FREQ * (jnp.zeros(shape, jnp.float32) + (kf - modes_total / 2 + 0.5))
    row = lax.broadcasted_iota(jnp.int32, shape, 0)
    lane = lax.broadcasted_iota(jnp.int32, shape, 1)
    zero_i = jnp.zeros(shape, jnp.int32)
    first_row = row == 0
    last_row = row == height - 1
    first_lane = lane == 0
    last_lane = lane == LANES - 1
    def edge_row(ref, arr, slot, k, cols):
        if isinstance(slot, int):
            return ref[0, pl.ds((arr * slots + slot) * 2 * NV + k, 1), cols]
        out = ref[0, pl.ds(arr * slots * 2 * NV + k, 1), cols]
        for other in range(1, slots):
            cand = ref[0, pl.ds((arr * slots + other) * 2 * NV + k, 1), cols]
            out = jnp.where((jnp.zeros(out.shape, jnp.int32) + slot) == other, cand, out)
        return out

    def load(src, arr, p, n, slot, k, cols):
        g = src[0, p, n, slot, :, cols]
        if patched:
            top = jnp.broadcast_to(edge_row(c0_ref, arr, slot, k, cols), shape)
            bottom = jnp.broadcast_to(edge_row(c7_ref, arr, slot, k, cols), shape)
            g = jnp.where(first_row, top, jnp.where(last_row, bottom, g))
        return g

    inner = (row > 0) & (row < height - 1)

    for s in range(slots):
        base = s * ENTRIES
        jl_s, jl_live = tbl[base + 4], tbl[base + 5]
        jh_s, jh_live = tbl[base + 6], tbl[base + 7]
        jl_mask = (zero_i + jl_live) != 0
        jh_mask = (zero_i + jh_live) != 0
        for b in range(chunks):
            cs = slice(b * LANES, (b + 1) * LANES)
            r = rho_ref[s, :, cs]
            ir = 1.0 / r
            u = vel_ref[0, s, :, cs]
            v = vel_ref[1, s, :, cs]
            kp = HEAT_RATIO * prs_ref[s, :, cs]
            bf = (r, ir, u, v, kp)
            means = []
            for arr, (src, dst, rates) in enumerate(((x_ref, xo_ref, direct_rates), (a_ref, ao_ref, adjoint_rates))):
                vals, dss, dcs, laps = [], [], [], []
                for p in range(2):
                    for n in range(NV):
                        k = p * NV + n
                        g = load(src, arr, p, n, s, k, cs)
                        lo_b = jnp.broadcast_to(gh_ref[arr, 0, s, k:k + 1, cs], shape)
                        hi_b = jnp.broadcast_to(gh_ref[arr, 1, s, k:k + 1, cs], shape)
                        im1 = jnp.where(first_row, lo_b, pltpu.roll(g, 1, 0))
                        ip1 = jnp.where(last_row, hi_b, pltpu.roll(g, height - 1, 0))
                        if b > 0:
                            left = load(src, arr, p, n, s, k, slice((b - 1) * LANES, b * LANES))
                        else:
                            left = jnp.where(jl_mask, load(src, arr, p, n, jl_s, k, slice(width - LANES, width)), 0.0)
                        if b < chunks - 1:
                            right = load(src, arr, p, n, s, k, slice((b + 1) * LANES, (b + 2) * LANES))
                        else:
                            right = jnp.where(jh_mask, load(src, arr, p, n, jh_s, k, slice(0, LANES)), 0.0)
                        jm1 = jnp.where(first_lane, pltpu.roll(left, 1, 1), pltpu.roll(g, 1, 1))
                        jp1 = jnp.where(last_lane, pltpu.roll(right, LANES - 1, 1), pltpu.roll(g, LANES - 1, 1))
                        vals.append(g)
                        dss.append((ip1 - im1) * 0.5)
                        dcs.append((jp1 - jm1) * 0.5)
                        laps.append(ip1 + im1 + jp1 + jm1 - 4.0 * g)
                X, Y = vals[:NV], vals[NV:]
                re, im = rates(bf, X, Y, dss[:NV], dcs[:NV], laps[:NV], dss[NV:], dcs[NV:], laps[NV:], w)
                total = None
                for p, rate in enumerate((re, im)):
                    for n in range(NV):
                        k = p * NV + n
                        nv = vals[k] + TIME_STEP * rate[n]
                        dst[0, p, n, s, :, cs] = nv
                        if first:
                            at = (arr * slots + s) * 2 * NV + k
                            elo_ref[0, pl.ds(at, 1), cs] = nv[0:1, :]
                            ehi_ref[0, pl.ds(at, 1), cs] = nv[height - 1:height, :]
                        sq = nv * nv
                        total = sq if total is None else total + sq
                means.append(total / 10.0)
            term = means[0] * means[1]
            if not ghosts:
                term = jnp.where(inner, term, 0.0)
            sens_ref[s, :, cs] = sens_ref[s, :, cs] + term


def run_step(tbl, x, a, rlo, rhi, patch, density, velocity, pressure, sens_in, modes_total, first):
    modes, parts, nv, slots, height, width = x.shape
    state_block = (1, parts, nv, slots, height, width)
    edge_block = (1, 2 * slots * parts * nv, width)
    state_spec = pl.BlockSpec(state_block, lambda m, t: (m, 0, 0, 0, 0, 0))
    edge_spec = pl.BlockSpec(edge_block, lambda m, t: (m, 0, 0))
    flow_spec = pl.BlockSpec((slots, height, width), lambda m, t: (0, 0, 0))
    vel_spec = pl.BlockSpec((2, slots, height, width), lambda m, t: (0, 0, 0, 0))
    ghosts = rlo is not None
    patched = patch is not None
    in_specs = [state_spec, state_spec]
    args = [x, a]
    if ghosts:
        in_specs += [edge_spec] * 4
        args += [rlo, rhi, reverse_lanes(rlo), reverse_lanes(rhi)]
    if patched:
        in_specs += [edge_spec] * 2
        args += list(patch)
    in_specs += [flow_spec, vel_spec, flow_spec]
    args += [density, velocity, pressure]
    if not first:
        in_specs.append(flow_spec)
        args.append(sens_in)
    out_shape = [
        jax.ShapeDtypeStruct(x.shape, jnp.float32),
        jax.ShapeDtypeStruct(a.shape, jnp.float32),
        jax.ShapeDtypeStruct((slots, height, width), jnp.float32),
    ]
    out_specs = [state_spec, state_spec, flow_spec]
    if first:
        edge_shape = jax.ShapeDtypeStruct((modes, 2 * slots * parts * nv, width), jnp.float32)
        out_shape += [edge_shape, edge_shape]
        out_specs += [edge_spec, edge_spec]
    grid_spec = pltpu.PrefetchScalarGridSpec(
        num_scalar_prefetch=1,
        grid=(modes,),
        in_specs=in_specs,
        out_specs=out_specs,
        scratch_shapes=[
            pltpu.VMEM((2, 2, slots, parts * nv, width), jnp.float32),
        ],
    )
    kernel = functools.partial(step_kernel, modes_total=modes_total, first=first, ghosts=ghosts, patched=patched)
    return pl.pallas_call(
        kernel,
        grid_spec=grid_spec,
        out_shape=out_shape,
        compiler_params=pltpu.CompilerParams(dimension_semantics=("arbitrary",)),
    )(tbl, *args)


def ghost_term(f, r, ir, u, kp, transpose):
    if transpose:
        return [u * f[0], r * f[0] + u * f[1] + kp * f[4], u * f[2], u * f[3], f[1] * ir + u * f[4]]
    return [u * f[0] + r * f[1], u * f[1] + f[4] * ir, u * f[2], u * f[3], kp * f[1] + u * f[4]]


def unflat(e, slots):
    modes, _, width = e.shape
    return jnp.transpose(e.reshape(modes, 2, slots, 2 * NV, width), (1, 0, 2, 3, 4))


def flat(e):
    _, modes, slots, rows, width = e.shape
    return jnp.transpose(e, (1, 0, 2, 3, 4)).reshape(modes, 2 * slots * rows, width)


def fix_rows(partial0, partial7, rlo, rhi, slot_of, face_flip, density, velocity, pressure):
    slots = density.shape[0]
    partial0, partial7, rlo, rhi = (unflat(e, slots) for e in (partial0, partial7, rlo, rhi))
    _, modes, slots, rows, width = partial0.shape
    height = density.shape[1]

    def picked(recv, side):
        plain = jnp.take(recv, slot_of[:, side], axis=2)
        turned = reverse_lanes(plain)
        flag = (face_flip[:, side] != 0)[None, None, :, None, None]
        return jnp.where(flag, turned, plain)

    ghost = {0: picked(rlo, 0), height - 1: picked(rhi, 1)}
    partial = {0: partial0, height - 1: partial7}
    fixed = {}
    sens_rows = {}
    for row in (0, height - 1):
        r = density[:, row, :]
        ir = 1.0 / r
        u = velocity[0][:, row, :]
        kp = HEAT_RATIO * pressure[:, row, :]
        half = 0.5 if row == 0 else -0.5
        out = []
        for arr, sign in ((0, 1.0), (1, -1.0)):
            g = ghost[row][arr].reshape(modes, slots, 2, NV, width)
            res = []
            for p in range(2):
                f = [g[:, :, p, n, :] for n in range(NV)]
                conv = ghost_term(f, r, ir, u, kp, arr == 1)
                for n in range(NV):
                    res.append(sign * half * conv[n] + VISCOSITY * f[n])
            delta = jnp.stack(res, axis=2)
            out.append(partial[row][arr] + TIME_STEP * delta)
        fixed[row] = jnp.stack(out)
        means = jnp.sum(fixed[row] * fixed[row], axis=3) / 10.0
        sens_rows[row] = jnp.sum(means[0] * means[1], axis=0)
    return flat(fixed[0]), flat(fixed[height - 1]), sens_rows[0], sens_rows[height - 1]


def reverse_lanes(rows):
    width = rows.shape[-1]
    ri = lax.broadcasted_iota(jnp.int32, (width, width), 0)
    ci = lax.broadcasted_iota(jnp.int32, (width, width), 1)
    turn = jnp.where(ri + ci == width - 1, 1.0, 0.0).astype(jnp.float32)
    flat = rows.reshape(-1, width)
    out = jnp.dot(flat, turn, precision=lax.Precision.HIGHEST, preferred_element_type=jnp.float32)
    return out.reshape(rows.shape)


def edge_kernel(x_ref, a_ref, lo_ref, hi_ref):
    modes, parts, nv, slots, height, _ = x_ref.shape
    for arr, src in enumerate((x_ref, a_ref)):
        for m in range(modes):
            for p in range(parts):
                for n in range(nv):
                    k = p * nv + n
                    for s in range(slots):
                        at = (arr * slots + s) * parts * nv + k
                        lo_ref[m, pl.ds(at, 1), :] = src[m, p, n, s, 0:1, :]
                        hi_ref[m, pl.ds(at, 1), :] = src[m, p, n, s, height - 1:height, :]


def edge_rows(x, a):
    modes, parts, nv, slots, height, width = x.shape
    edge_shape = jax.ShapeDtypeStruct((modes, 2 * slots * parts * nv, width), jnp.float32)
    return pl.pallas_call(edge_kernel, out_shape=[edge_shape, edge_shape])(x, a)


def per_device(direct, adjoint, density, velocity, pressure, block_home, face_nbr, face_flip):
    modes, parts, nv, slots, height, width = direct.shape
    modes_total = modes * lax.axis_size("mode")
    live = (face_nbr >= 0).astype(jnp.int32)
    hits = face_nbr[:, :, None] == lax.broadcasted_iota(jnp.int32, (1, 1, block_home.shape[0]), 2)
    positions = jnp.sum(jnp.where(hits, block_home[None, None, :], 0), axis=2)
    slot_of = positions % slots
    table = jnp.stack(
        [
            slot_of[:, 0], face_flip[:, 0], slot_of[:, 1], face_flip[:, 1],
            slot_of[:, 2], live[:, 2], slot_of[:, 3], live[:, 3],
        ],
        axis=1,
    ).reshape(-1)
    mode_base = (lax.axis_index("mode") * modes).astype(jnp.int32)
    table = jnp.concatenate([table.astype(jnp.int32), mode_base[None]])

    with jax.named_scope("edge_exchange_0"):
        down, up = edge_rows(direct, adjoint)
        rlo = shifted(up, "blk", 1)
        rhi = shifted(down, "blk", -1)
    with jax.named_scope("flow_step_0"):
        q1, a1, sens, elo, ehi = run_step(
            table, direct, adjoint, None, None, None, density, velocity, pressure, None, modes_total, True
        )
    with jax.named_scope("edge_fix_0"):
        c0, c7, s0, s7 = fix_rows(elo, ehi, rlo, rhi, slot_of, face_flip, density, velocity, pressure)
        sens = sens.at[:, 0, :].add(s0).at[:, height - 1, :].add(s7)
    with jax.named_scope("edge_exchange_1"):
        rlo = shifted(c7, "blk", 1)
        rhi = shifted(c0, "blk", -1)
    with jax.named_scope("flow_step_1"):
        q2, a2, sens = run_step(
            table, q1, a1, rlo, rhi, (c0, c7), density, velocity, pressure, sens, modes_total, False
        )
    with jax.named_scope("mode_reduce"):
        count = lax.axis_size("mode")
        me = lax.axis_index("mode")
        stacked = jnp.stack([sens] + [shifted(sens, "mode", k) for k in range(1, count)])
        total = None
        for j in range(count):
            part = lax.dynamic_index_in_dim(stacked, (me - j) % count, axis=0, keepdims=False)
            total = part if total is None else total + part
        sensitivity = total / (STEPS * modes_total)
    return (q2, a2, sensitivity)


def solution(mesh):
    placed = (
        P("mode", None, None, "blk", None, None),
        P("mode", None, None, "blk", None, None),
        P("blk", None, None),
        P(None, "blk", None, None),
        P("blk", None, None),
        P(),
        P("blk", None),
        P("blk", None),
    )
    return jax.shard_map(
        per_device,
        mesh=mesh,
        in_specs=placed,
        out_specs=(
            P("mode", None, None, "blk", None, None),
            P("mode", None, None, "blk", None, None),
            P("blk", None, None),
        ),
        check_vma=False,
    )
```
